32 devices in a mesh: tm: 8 (over y, x, core), night: 4 (over z).
Axes of the slice: x: 2, y: 2, z: 4, core: 2. Of those that a mesh axis runs over, the one named last changes fastest.
Arguments:
- patches: bfloat16 [4, 2048, 1024], P('night', 'tm'), may hold values from -6 to 6
- weights: bfloat16 [1024, 4, 512], replicated, may hold values from -0.1875 to 0.1875
- cotangent: bfloat16 [4, 2048, 1024], P('night', 'tm'), may hold values from -6 to 6
- loss_mask: int32 [4, 2048], P('night', 'tm'), may hold values from 0 to 1, as said below
Outputs:
- grad_input: bfloat16 [4, 2048, 1024], P('night', 'tm')
- grad_weights: float32 [1024, 4, 512], P(('tm', 'night'))
The draws below stay inside these ranges and needn't reach their ends.
Inputs may be any that keep to these rules, and one draw needn't show every extreme that they name: `loss_mask`: 1 marks a masked patch; the last patch of every night is always 1.
All inputs are finite; a program needn't handle non-finite values.
Results may differ from the reference program's by a relative error of at most 0.0094.
Values may be sent and summed in bfloat16 or wider, within the bound.
No kernel may reach another device: no remote copies, remote signals or barrier semaphores. Data moves between devices by JAX's collectives and lax.ppermute only.
A program may use at most 128 MiB of HBM per device.

```python
import math
import jax
import jax.numpy as jnp
from jax import lax

D = 1024
HEADS = 8
HSIZE = 64
WIN = 1024
HD = 512
NIGHTS = 4
SEQ = 2048
TOKENS_ALL = 8192


def draw_loss_mask(key, part):
    position = jnp.arange(SEQ, dtype=jnp.int32)
    level = 150 + 300 * position // SEQ
    drawn = jax.random.randint(key, (NIGHTS, SEQ), 0, 1000, dtype=jnp.int32)
    chosen = (drawn < level[None, :]).astype(jnp.int32)
    return chosen.at[:, SEQ - 1].set(1)


def raised(values, rng, source, target, blocks, factor):
    owner, partner = [(jnp.arange(values.shape[dim]) // (values.shape[dim] // blocks)).reshape([-1 if axis == dim else 1 for axis in range(values.ndim)]) for dim in (source, target)]
    chosen = jax.random.permutation(rng, blocks)[partner]
    strong = (owner == chosen) | (owner == (partner + blocks // 2) % blocks)
    return jnp.where(strong, factor * values, values)


def block_scale(key, shape, pieces, smallest, largest):
    def one(axis_at, parts):
        steps = jax.random.uniform(jax.random.fold_in(jax.random.fold_in(key, 6), axis_at), (parts,), jnp.float32, smallest / len(pieces), largest / len(pieces))
        return jnp.repeat(jnp.exp(steps), shape[axis_at] // parts).reshape((-1,) + (1,) * (len(shape) - axis_at - 1))

    gain = one(*pieces[0])
    for cut in pieces[1:]:
        gain = gain * one(*cut)
    return gain


def centred(own_key, shape, spread, reach, shards=(), kind=jnp.bfloat16):
    entries = spread * jax.random.normal(own_key, shape, jnp.float32)
    if shards:
        entries = entries * block_scale(own_key, shape, shards, -0.22, 0.18)
    return jnp.clip(entries, -reach, reach).astype(kind)


def gaussian_with(key, shape, width, bound, pieces, heavy, kind=jnp.bfloat16):
    array = width * jax.random.normal(key, shape, jnp.float32)
    if pieces:
        array = array * block_scale(key, shape, pieces, -0.22, 0.18)
    return jnp.clip(raised(array, jax.random.fold_in(key, 3), *heavy), -bound, bound).astype(kind)


def setup_inputs(seed: int = 0) -> dict:
    splits = jax.random.split(jax.random.key(seed), 5)
    return {
        "patches": gaussian_with(splits[0], (NIGHTS, SEQ, D), 1.0, 6.0, ((0, 4), (1, 8)), (1, 2, 8, 2.0)),
        "weights": centred(splits[1], (D, 4, HD), D ** -0.5, 0.1875),
        "cotangent": gaussian_with(splits[2], (NIGHTS, SEQ, D), 1.0, 6.0, ((0, 4), (1, 8)), (1, 2, 8, 2.0)),
        "loss_mask": draw_loss_mask(jax.random.fold_in(splits[4], 71), 0),
    }


def to_float(value):
    return value.astype(jnp.float32)

def rounded(value):
    return lax.optimization_barrier(value.astype(jnp.bfloat16)).astype(jnp.float32)

def band_block(queries, keys_blk, values_blk, grad_attn, valid, inv_scale):
    query_f = to_float(queries)
    key_f = to_float(keys_blk)
    value_f = to_float(values_blk)
    grad_f = to_float(grad_attn)
    scores = jnp.einsum('qgc,kgc->gqk', query_f, key_f) * inv_scale
    exp_terms = jnp.exp(scores) * valid[None]
    probs = exp_terms / lax.optimization_barrier(jnp.sum(exp_terms, axis=-1, keepdims=True))
    probs_low = rounded(probs)
    attended = jnp.einsum('gqk,kgc->qgc', probs_low, value_f).astype(jnp.bfloat16)
    delta = lax.optimization_barrier(jnp.sum(grad_f * to_float(attended), axis=-1))
    grad_probs = jnp.einsum('qgc,kgc->gqk', grad_f, value_f)
    grad_scores = rounded(probs * (grad_probs - jnp.transpose(delta)[:, :, None]) * inv_scale)
    grad_query = jnp.einsum('gqk,kgc->qgc', grad_scores, key_f)
    grad_key = jnp.einsum('gqk,qgc->kgc', grad_scores, query_f)
    grad_value = jnp.einsum('gqk,qgc->kgc', probs_low, grad_f)
    return (attended, grad_query, grad_key, grad_value)

def night_pass(night_in, night_cot, night_mask, weights, loss_scale):
    in_float = to_float(night_in)
    inv_rms = lax.rsqrt(lax.optimization_barrier(jnp.mean(in_float * in_float, axis=-1)) + 1e-06)
    normed_full = in_float * inv_rms[:, None]
    normed = normed_full.astype(jnp.bfloat16)
    proj_weights = to_float(weights[:, :3, :])
    projected = jnp.einsum('sd,dwh->wsh', to_float(normed), proj_weights).astype(jnp.bfloat16)
    queries = projected[0]
    zero_pad = jnp.zeros((WIN, HD), jnp.bfloat16)
    keys_pad = jnp.concatenate([zero_pad, projected[1]], axis=0)
    values_pad = jnp.concatenate([zero_pad, projected[2]], axis=0)
    grad_out = jnp.where(night_mask[:, None] > 0, night_cot, jnp.zeros_like(night_cot))
    grad_attn = jnp.dot(grad_out, weights[:, 3, :], preferred_element_type=jnp.float32).astype(jnp.bfloat16)
    block_rows = min(512, SEQ)
    key_len = block_rows + WIN
    blocks = SEQ // block_rows
    inv_scale = 1.0 / math.sqrt(HSIZE)
    query_idx = jnp.arange(block_rows, dtype=jnp.int32)[:, None]
    key_idx = jnp.arange(key_len, dtype=jnp.int32)[None, :]
    offsets = query_idx - key_idx + WIN
    band = (offsets >= 0) & (offsets < WIN)

    def block_step(accum, index):
        start = (index * block_rows).astype(jnp.int32)
        query_blk = lax.dynamic_slice_in_dim(queries, start, block_rows, 0).reshape(block_rows, HEADS, HSIZE)
        key_blk = lax.dynamic_slice_in_dim(keys_pad, start, key_len, 0).reshape(key_len, HEADS, HSIZE)
        value_blk = lax.dynamic_slice_in_dim(values_pad, start, key_len, 0).reshape(key_len, HEADS, HSIZE)
        grad_blk = lax.dynamic_slice_in_dim(grad_attn, start, block_rows, 0).reshape(block_rows, HEADS, HSIZE)
        valid = (band & (key_idx >= WIN - start)).astype(jnp.float32)
        attended, grad_query, grad_key, grad_value = band_block(query_blk, key_blk, value_blk, grad_blk, valid, inv_scale)
        update = jnp.stack([grad_key, grad_value]).reshape(2, key_len, HD)
        current = lax.dynamic_slice_in_dim(accum, start, key_len, 1)
        accum = lax.dynamic_update_slice_in_dim(accum, current + update, start, 1)
        return (accum, (attended.reshape(block_rows, HD), grad_query.reshape(block_rows, HD).astype(jnp.bfloat16)))
    accum_init = jnp.zeros((2, SEQ + WIN, HD), jnp.float32)
    accum, (attended_blocks, grad_q_blocks) = lax.scan(block_step, accum_init, jnp.arange(blocks, dtype=jnp.int32))
    attended_all = attended_blocks.reshape(SEQ, HD)
    grad_q = grad_q_blocks.reshape(SEQ, HD)
    grad_kv = accum[:, WIN:].astype(jnp.bfloat16)
    grad_proj = jnp.concatenate([grad_q[None], grad_kv], axis=0)
    grad_normed = jnp.einsum('wsh,dwh->sd', to_float(grad_proj), proj_weights)
    along = lax.optimization_barrier(jnp.sum(grad_normed * normed_full, axis=-1)) / D
    grad_input = (loss_scale * inv_rms[:, None] * (grad_normed - normed_full * along[:, None])).astype(jnp.bfloat16)
    proj_terms = jnp.einsum('sd,wsh->dwh', to_float(normed), to_float(grad_proj))
    out_terms = jnp.einsum('sd,sh->dh', to_float(grad_out), to_float(attended_all))
    terms = jnp.concatenate([proj_terms, out_terms[:, None]], axis=1)
    return (grad_input, terms)

def reference(patches, weights, cotangent, loss_mask):
    count = jnp.sum(loss_mask.astype(jnp.float32))
    loss_scale = jnp.float32(TOKENS_ALL) / count
    inputs_grad = []
    total = jnp.zeros((D, 4, HD), jnp.float32)
    for night_index in range(NIGHTS):
        grad_input, terms = night_pass(patches[night_index], cotangent[night_index], loss_mask[night_index], weights, loss_scale)
        inputs_grad.append(grad_input)
        total = total + terms
    grad_weights = total * (jnp.sqrt(jnp.float32(TOKENS_ALL)) / count)
    return (jnp.stack(inputs_grad), grad_weights)
```

```python
import math

import jax
import jax.numpy as jnp
from jax import lax
from jax.sharding import PartitionSpec as P

HEADS = 8
HSIZE = 64
WIN = 1024


def shifted(value, axis, by):
    peers = lax.axis_size(axis)
    pairs = [(i, i + by) for i in range(peers) if 0 <= i + by < peers]
    return lax.ppermute(value, axis, pairs)


def is_power_of_two(n):
    return n > 0 and n & (n - 1) == 0


def butterfly_sum(value, axes):
    for axis in axes:
        peers = lax.axis_size(axis)
        flip = 1
        while flip < peers:
            pairs = [(i, i ^ flip) for i in range(peers)]
            value = value + lax.ppermute(value, axis, pairs)
            flip *= 2
    return value


def halve(value, dim, axis, flip):
    peers = lax.axis_size(axis)
    bit = (lax.axis_index(axis) // flip) % 2
    keep = lax.dynamic_index_in_dim(value, bit, dim, keepdims=False)
    send = lax.dynamic_index_in_dim(value, 1 - bit, dim, keepdims=False)
    pairs = [(i, i ^ flip) for i in range(peers)]
    return keep + lax.ppermute(send, axis, pairs)


def scatter_rows(value, axes):
    sizes = [lax.axis_size(axis) for axis in axes]
    rows = value.shape[0]
    groups = math.prod(sizes)
    if not all(is_power_of_two(n) for n in sizes) or rows % groups:
        return lax.psum_scatter(value, axes, scatter_dimension=0, tiled=True)
    stages = [
        (axis, 1 << (n.bit_length() - 2 - i))
        for axis, n in zip(axes, sizes)
        for i in range(n.bit_length() - 1)
    ]
    rest = value.shape[1:]
    value = value.reshape((2,) * len(stages) + (rows // groups,) + rest)
    names = list(stages)

    def step(part, part_names, stage):
        dim = part_names.index(stage)
        return halve(part, dim, *stage), part_names[:dim] + part_names[dim + 1 :]

    first = ("tm", 1) if ("tm", 1) in stages else stages[-1]
    value, names = step(value, names, first)
    middle = [s for s in stages if s[0] == axes[0] and s != first]
    tail = [s for s in stages if s[0] != axes[0] and s != first]
    if len(middle) > 1 and rest[-1] % 2 == 0:
        cut = rest[-1] // 2
        left, right = value[..., :cut], value[..., cut:]
        left_names, right_names = list(names), list(names)
        for a, b in zip(middle, middle[::-1]):
            left, left_names = step(left, left_names, a)
            right, right_names = step(right, right_names, b)
        value = jnp.concatenate([left, right], axis=-1)
        names = left_names
    else:
        for stage in middle:
            value, names = step(value, names, stage)
    for stage in tail[::-1]:
        value, names = step(value, names, stage)
    return value


def band_block(queries, keys_blk, values_blk, grad_attn, valid, inv_scale):
    scores = (
        jnp.einsum("qgc,kgc->gqk", queries, keys_blk, preferred_element_type=jnp.float32)
        * inv_scale
    )
    exp_terms = jnp.exp(scores) * valid[None]
    probs = exp_terms / jnp.sum(exp_terms, axis=-1, keepdims=True)
    probs_low = probs.astype(jnp.bfloat16)
    attended = jnp.einsum(
        "gqk,kgc->qgc", probs_low, values_blk, preferred_element_type=jnp.float32
    ).astype(jnp.bfloat16)
    delta = jnp.sum(grad_attn.astype(jnp.float32) * attended.astype(jnp.float32), axis=-1)
    grad_probs = jnp.einsum(
        "qgc,kgc->gqk", grad_attn, values_blk, preferred_element_type=jnp.float32
    )
    grad_scores = (probs * (grad_probs - jnp.transpose(delta)[:, :, None]) * inv_scale).astype(
        jnp.bfloat16
    )
    grad_query = jnp.einsum(
        "gqk,kgc->qgc", grad_scores, keys_blk, preferred_element_type=jnp.float32
    )
    grad_key = jnp.einsum("gqk,qgc->kgc", grad_scores, queries, preferred_element_type=jnp.float32)
    grad_value = jnp.einsum(
        "gqk,qgc->kgc", probs_low, grad_attn, preferred_element_type=jnp.float32
    )
    return (attended, grad_query, grad_key, grad_value)


def shards(patches, weights, cotangent, loss_mask):
    rows = patches.shape[1]
    width = patches.shape[2]
    inner = weights.shape[2]
    span = (WIN + rows - 2) // rows
    block_rows = min(512, rows)
    key_len = block_rows + span * rows
    group = max(1, min(HEADS, 128 // HSIZE))
    group_cols = group * HSIZE
    inv_scale = 1.0 / math.sqrt(HSIZE)
    local_in = patches[0].astype(jnp.float32)
    inv_rms = lax.rsqrt(jnp.mean(local_in * local_in, axis=-1) + 1e-06)
    normed_full = local_in * inv_rms[:, None]
    normed = normed_full.astype(jnp.bfloat16)
    proj_weights = weights[:, :3, :]
    projected = jnp.einsum(
        "rd,dwh->wrh", normed, proj_weights, preferred_element_type=jnp.float32
    ).astype(jnp.bfloat16)
    queries = projected[0]
    key_vals = projected[1:]
    earlier = [shifted(key_vals, "tm", offset) for offset in range(span, 0, -1)]
    extended = jnp.concatenate(earlier + [key_vals], axis=1)
    local_count = jnp.sum(loss_mask.astype(jnp.int32))
    if all(is_power_of_two(lax.axis_size(axis)) for axis in ("tm", "night")):
        total_count = butterfly_sum(local_count, ("tm", "night")).astype(jnp.float32)
    else:
        total_count = lax.psum(local_count, ("tm", "night")).astype(jnp.float32)
    tokens_all = rows * lax.axis_size("tm") * lax.axis_size("night")
    loss_scale = jnp.float32(tokens_all) / total_count
    local_cot = cotangent[0]
    grad_out = jnp.where(loss_mask[0][:, None] > 0, local_cot, jnp.zeros_like(local_cot))
    grad_attn = jnp.dot(grad_out, weights[:, 3, :], preferred_element_type=jnp.float32).astype(
        jnp.bfloat16
    )
    base = lax.axis_index("tm") * rows
    query_idx = jnp.arange(block_rows, dtype=jnp.int32)[:, None]
    key_idx = jnp.arange(key_len, dtype=jnp.int32)[None, :]
    offsets = query_idx - key_idx + span * rows
    band = (offsets >= 0) & (offsets < WIN)
    attended_cols = []
    grad_q_cols = []
    grad_kv_cols = []
    for first in range(0, inner, group_cols):
        accum = jnp.zeros((2, (span + 1) * rows, group_cols), jnp.float32)
        valid = (band & (key_idx >= span * rows - base - 0)).astype(jnp.float32)
        query_blk = queries[0:block_rows, first : first + group_cols].reshape(
            block_rows, group, HSIZE
        )
        kv_blk = extended[:, 0:key_len, first : first + group_cols].reshape(
            2, key_len, group, HSIZE
        )
        grad_blk = grad_attn[0:block_rows, first : first + group_cols].reshape(
            block_rows, group, HSIZE
        )
        attended, grad_query, grad_key, grad_value = band_block(
            query_blk, kv_blk[0], kv_blk[1], grad_blk, valid, inv_scale
        )
        attended_rows = attended.reshape(block_rows, group_cols)
        grad_q_rows = grad_query.reshape(block_rows, group_cols).astype(jnp.bfloat16)
        update = jnp.stack([grad_key, grad_value]).reshape(2, key_len, group_cols)
        accum = accum.at[:, 0:key_len].add(update)
        attended_cols.append(attended_rows)
        grad_q_cols.append(grad_q_rows)
        grad_kv_cols.append(accum)
    attended_all = jnp.concatenate(attended_cols, axis=1)
    grad_q = jnp.concatenate(grad_q_cols, axis=1)
    grad_kv_ext = jnp.concatenate(grad_kv_cols, axis=2)
    owned = grad_kv_ext[:, span * rows :]
    for offset in range(1, span + 1):
        lower = (span - offset) * rows
        owned = owned + shifted(
            grad_kv_ext[:, lower : lower + rows].astype(jnp.bfloat16), "tm", -offset
        ).astype(jnp.float32)
    grad_kv = owned.astype(jnp.bfloat16)
    grad_proj = jnp.concatenate([grad_q[None], grad_kv], axis=0)
    grad_normed = jnp.einsum(
        "wrh,dwh->rd", grad_proj, proj_weights, preferred_element_type=jnp.float32
    )
    along = jnp.sum(grad_normed * normed_full, axis=-1) / width
    grad_input = (
        loss_scale * inv_rms[:, None] * (grad_normed - normed_full * along[:, None])
    ).astype(jnp.bfloat16)
    proj_part = jnp.einsum("rd,wrh->dwh", normed, grad_proj, preferred_element_type=jnp.float32)
    out_part = jnp.einsum("rd,rh->dh", grad_out, attended_all, preferred_element_type=jnp.float32)
    summed = scatter_rows(
        jnp.concatenate([proj_part, out_part[:, None]], axis=1), ("tm", "night")
    )
    grad_weights = summed * (jnp.sqrt(jnp.float32(tokens_all)) / total_count)
    return (grad_input[None], grad_weights)


def solution(mesh):
    return jax.shard_map(
        shards,
        mesh=mesh,
        in_specs=(P("night", "tm", None), P(), P("night", "tm", None), P("night", "tm")),
        out_specs=(P("night", "tm", None), P(("tm", "night"), None, None)),
        check_vma=False,
    )
```

```python
import math

import jax
import jax.numpy as jnp
from jax import lax
from jax.sharding import PartitionSpec as P

HEADS = 8
HSIZE = 64
WIN = 1024


def shifted(value, axis, by):
    peers = lax.axis_size(axis)
    pairs = [(i, i + by) for i in range(peers) if 0 <= i + by < peers]
    return lax.ppermute(value, axis, pairs)


def is_power_of_two(n):
    return n > 0 and n & (n - 1) == 0


def butterfly_sum(value, axes):
    for axis in axes:
        peers = lax.axis_size(axis)
        flip = 1
        while flip < peers:
            pairs = [(i, i ^ flip) for i in range(peers)]
            value = value + lax.ppermute(value, axis, pairs)
            flip *= 2
    return value


def halve(value, dim, axis, flip):
    peers = lax.axis_size(axis)
    bit = (lax.axis_index(axis) // flip) % 2
    keep = lax.dynamic_index_in_dim(value, bit, dim, keepdims=False)
    send = lax.dynamic_index_in_dim(value, 1 - bit, dim, keepdims=False)
    pairs = [(i, i ^ flip) for i in range(peers)]
    return keep + lax.ppermute(send, axis, pairs)


def scatter_rows(value, axes):
    sizes = [lax.axis_size(axis) for axis in axes]
    rows = value.shape[0]
    groups = math.prod(sizes)
    if not all(is_power_of_two(n) for n in sizes) or rows % groups:
        return lax.psum_scatter(value, axes, scatter_dimension=0, tiled=True)
    stages = [
        (axis, 1 << (n.bit_length() - 2 - i))
        for axis, n in zip(axes, sizes)
        for i in range(n.bit_length() - 1)
    ]
    rest = value.shape[1:]
    value = value.reshape((2,) * len(stages) + (rows // groups,) + rest)
    names = list(stages)

    def step(part, part_names, stage):
        dim = part_names.index(stage)
        return halve(part, dim, *stage), part_names[:dim] + part_names[dim + 1 :]

    first = ("tm", 1) if ("tm", 1) in stages else stages[-1]
    value, names = step(value, names, first)
    middle = [s for s in stages if s[0] == axes[0] and s != first]
    tail = [s for s in stages if s[0] != axes[0] and s != first]
    if len(middle) > 1 and rest[-1] % 2 == 0:
        cut = rest[-1] // 2
        left, right = value[..., :cut], value[..., cut:]
        left_names, right_names = list(names), list(names)
        for a, b in zip(middle, middle[::-1]):
            left, left_names = step(left, left_names, a)
            right, right_names = step(right, right_names, b)
        value = jnp.concatenate([left, right], axis=-1)
        names = left_names
    else:
        for stage in middle:
            value, names = step(value, names, stage)
    for stage in tail[::-1]:
        value, names = step(value, names, stage)
    return value


def band_block(queries, keys_blk, values_blk, grad_attn, valid, inv_scale):
    scores = (
        jnp.einsum("qgc,kgc->gqk", queries, keys_blk, preferred_element_type=jnp.float32)
        * inv_scale
    )
    exp_terms = jnp.exp(scores) * valid[None]
    probs = exp_terms / jnp.sum(exp_terms, axis=-1, keepdims=True)
    probs_low = probs.astype(jnp.bfloat16)
    attended = jnp.einsum(
        "gqk,kgc->qgc", probs_low, values_blk, preferred_element_type=jnp.float32
    ).astype(jnp.bfloat16)
    delta = jnp.sum(grad_attn.astype(jnp.float32) * attended.astype(jnp.float32), axis=-1)
    grad_probs = jnp.einsum(
        "qgc,kgc->gqk", grad_attn, values_blk, preferred_element_type=jnp.float32
    )
    grad_scores = (probs * (grad_probs - jnp.transpose(delta)[:, :, None]) * inv_scale).astype(
        jnp.bfloat16
    )
    grad_query = jnp.einsum(
        "gqk,kgc->qgc", grad_scores, keys_blk, preferred_element_type=jnp.float32
    )
    grad_key = jnp.einsum("gqk,qgc->kgc", grad_scores, queries, preferred_element_type=jnp.float32)
    grad_value = jnp.einsum(
        "gqk,qgc->kgc", probs_low, grad_attn, preferred_element_type=jnp.float32
    )
    return (attended, grad_query, grad_key, grad_value)


def shards(patches, weights, cotangent, loss_mask):
    rows = patches.shape[1]
    width = patches.shape[2]
    inner = weights.shape[2]
    span = (WIN + rows - 2) // rows
    block_rows = min(512, rows)
    key_len = block_rows + span * rows
    group = max(1, min(HEADS, 128 // HSIZE))
    group_cols = group * HSIZE
    inv_scale = 1.0 / math.sqrt(HSIZE)
    local_in = patches[0].astype(jnp.float32)
    inv_rms = lax.rsqrt(jnp.mean(local_in * local_in, axis=-1) + 1e-06)
    normed_full = local_in * inv_rms[:, None]
    normed = normed_full.astype(jnp.bfloat16)
    proj_weights = weights[:, :3, :]
    projected = jnp.einsum(
        "rd,dwh->wrh", normed, proj_weights, preferred_element_type=jnp.float32
    ).astype(jnp.bfloat16)
    queries = projected[0]
    key_vals = projected[1:]
    earlier = [shifted(key_vals, "tm", offset) for offset in range(span, 0, -1)]
    extended = jnp.concatenate(earlier + [key_vals], axis=1)
    local_count = jnp.sum(loss_mask.astype(jnp.float32))
    tokens_all = rows * lax.axis_size("tm") * lax.axis_size("night")
    local_cot = cotangent[0]
    grad_out = jnp.where(loss_mask[0][:, None] > 0, local_cot, jnp.zeros_like(local_cot))
    grad_attn = jnp.dot(grad_out, weights[:, 3, :], preferred_element_type=jnp.float32).astype(
        jnp.bfloat16
    )
    base = lax.axis_index("tm") * rows
    query_idx = jnp.arange(block_rows, dtype=jnp.int32)[:, None]
    key_idx = jnp.arange(key_len, dtype=jnp.int32)[None, :]
    offsets = query_idx - key_idx + span * rows
    band = (offsets >= 0) & (offsets < WIN)
    attended_cols = []
    grad_q_cols = []
    grad_kv_cols = []
    for first in range(0, inner, group_cols):
        accum = jnp.zeros((2, (span + 1) * rows, group_cols), jnp.float32)
        valid = (band & (key_idx >= span * rows - base - 0)).astype(jnp.float32)
        query_blk = queries[0:block_rows, first : first + group_cols].reshape(
            block_rows, group, HSIZE
        )
        kv_blk = extended[:, 0:key_len, first : first + group_cols].reshape(
            2, key_len, group, HSIZE
        )
        grad_blk = grad_attn[0:block_rows, first : first + group_cols].reshape(
            block_rows, group, HSIZE
        )
        attended, grad_query, grad_key, grad_value = band_block(
            query_blk, kv_blk[0], kv_blk[1], grad_blk, valid, inv_scale
        )
        attended_rows = attended.reshape(block_rows, group_cols)
        grad_q_rows = grad_query.reshape(block_rows, group_cols).astype(jnp.bfloat16)
        update = jnp.stack([grad_key, grad_value]).reshape(2, key_len, group_cols)
        accum = accum.at[:, 0:key_len].add(update)
        attended_cols.append(attended_rows)
        grad_q_cols.append(grad_q_rows)
        grad_kv_cols.append(accum)
    attended_all = jnp.concatenate(attended_cols, axis=1)
    grad_q = jnp.concatenate(grad_q_cols, axis=1)
    grad_kv_ext = jnp.concatenate(grad_kv_cols, axis=2)
    owned = grad_kv_ext[:, span * rows :]
    for offset in range(1, span + 1):
        lower = (span - offset) * rows
        owned = owned + shifted(
            grad_kv_ext[:, lower : lower + rows].astype(jnp.bfloat16), "tm", -offset
        ).astype(jnp.float32)
    grad_kv = owned.astype(jnp.bfloat16)
    grad_proj = jnp.concatenate([grad_q[None], grad_kv], axis=0)
    grad_normed = jnp.einsum(
        "wrh,dwh->rd", grad_proj, proj_weights, preferred_element_type=jnp.float32
    )
    along = jnp.sum(grad_normed * normed_full, axis=-1) / width
    unscaled_input = inv_rms[:, None] * (grad_normed - normed_full * along[:, None])
    proj_part = jnp.einsum("rd,wrh->dwh", normed, grad_proj, preferred_element_type=jnp.float32)
    out_part = jnp.einsum("rd,rh->dh", grad_out, attended_all, preferred_element_type=jnp.float32)
    blocks = lax.axis_size("tm") * lax.axis_size("night")
    payload = jnp.concatenate([proj_part, out_part[:, None]], axis=1)
    payload = payload.reshape((blocks, width // blocks) + payload.shape[1:])
    count_row = jnp.zeros((blocks, 1) + payload.shape[2:], jnp.float32)
    count_row = count_row.at[:, 0, 0, 0].set(local_count)
    payload = jnp.concatenate([payload, count_row], axis=1)
    payload = payload.reshape((-1,) + payload.shape[2:])
    summed = scatter_rows(payload, ("tm", "night"))
    total_count = summed[-1, 0, 0]
    loss_scale = jnp.float32(tokens_all) / total_count
    grad_input = (loss_scale * unscaled_input).astype(jnp.bfloat16)
    grad_weights = summed[:-1] * (jnp.sqrt(jnp.float32(tokens_all)) / total_count)
    return (grad_input[None], grad_weights)


def solution(mesh):
    return jax.shard_map(
        shards,
        mesh=mesh,
        in_specs=(P("night", "tm", None), P(), P("night", "tm", None), P("night", "tm")),
        out_specs=(P("night", "tm", None), P(("tm", "night"), None, None)),
        check_vma=False,
    )
```

```python
import math

import jax
import jax.numpy as jnp
from jax import lax
from jax.sharding import PartitionSpec as P

HEADS = 8
HSIZE = 64
WIN = 1024


def shifted(value, axis, by):
    peers = lax.axis_size(axis)
    pairs = [(i, i + by) for i in range(peers) if 0 <= i + by < peers]
    return lax.ppermute(value, axis, pairs)


def is_power_of_two(n):
    return n > 0 and n & (n - 1) == 0


def halve(value, dim, axis, flip, send_type):
    peers = lax.axis_size(axis)
    bit = (lax.axis_index(axis) // flip) % 2
    keep = lax.dynamic_index_in_dim(value, bit, dim, keepdims=False)
    send = lax.dynamic_index_in_dim(value, 1 - bit, dim, keepdims=False)
    pairs = [(i, i ^ flip) for i in range(peers)]
    return keep + lax.ppermute(send.astype(send_type), axis, pairs).astype(keep.dtype)


def swap_add(value, axis, flip):
    peers = lax.axis_size(axis)
    pairs = [(i, i ^ flip) for i in range(peers)]
    return value + lax.ppermute(value, axis, pairs)


def scatter_rows(value, tally, axes, first_axis, wire_type):
    sizes = [lax.axis_size(axis) for axis in axes]
    rows = value.shape[0]
    groups = math.prod(sizes)
    if not all(is_power_of_two(n) for n in sizes) or rows % groups:
        return (
            lax.psum_scatter(value, axes, scatter_dimension=0, tiled=True),
            lax.psum(tally, axes),
        )
    stages = [
        (axis, 1 << (n.bit_length() - 2 - i))
        for axis, n in zip(axes, sizes)
        for i in range(n.bit_length() - 1)
    ]
    if not stages:
        return value, tally
    rest = value.shape[1:]
    value = value.reshape((2,) * len(stages) + (rows // groups,) + rest)
    names = list(stages)

    def step(part, part_names, stage, send_type):
        dim = part_names.index(stage)
        return halve(part, dim, *stage, send_type), part_names[:dim] + part_names[dim + 1 :]

    first = (first_axis, 1) if (first_axis, 1) in stages else stages[-1]
    value, names = step(value, names, first, value.dtype)
    tally = swap_add(tally, *first)
    middle = [s for s in stages if s[0] == first[0] and s != first]
    tail = [s for s in stages if s[0] != first[0]][::-1]
    if len(middle) > 1 and rest[-1] % 2 == 0:
        cut = rest[-1] // 2
        left, right = value[..., :cut], value[..., cut:]
        left_names, right_names = list(names), list(names)
        for a, b in zip(middle, middle[::-1]):
            left, left_names = step(left, left_names, a, wire_type)
            tally = swap_add(tally, *a)
            right, right_names = step(right, right_names, b, wire_type)
        value = jnp.concatenate([left, right], axis=-1)
        names = left_names
    else:
        for stage in middle:
            value, names = step(value, names, stage, wire_type)
            tally = swap_add(tally, *stage)
    for stage in tail:
        value, names = step(value, names, stage, wire_type)
        tally = swap_add(tally, *stage)
    return value, tally


def band_block(queries, keys_blk, values_blk, grad_attn, valid, inv_scale):
    scores = (
        jnp.einsum("qgc,kgc->gqk", queries, keys_blk, preferred_element_type=jnp.float32)
        * inv_scale
    )
    exp_terms = jnp.exp(scores) * valid[None]
    probs = exp_terms / jnp.sum(exp_terms, axis=-1, keepdims=True)
    probs_low = probs.astype(jnp.bfloat16)
    attended = jnp.einsum(
        "gqk,kgc->qgc", probs_low, values_blk, preferred_element_type=jnp.float32
    ).astype(jnp.bfloat16)
    delta = jnp.sum(grad_attn.astype(jnp.float32) * attended.astype(jnp.float32), axis=-1)
    grad_probs = jnp.einsum(
        "qgc,kgc->gqk", grad_attn, values_blk, preferred_element_type=jnp.float32
    )
    grad_scores = (probs * (grad_probs - jnp.transpose(delta)[:, :, None]) * inv_scale).astype(
        jnp.bfloat16
    )
    grad_query = jnp.einsum(
        "gqk,kgc->qgc", grad_scores, keys_blk, preferred_element_type=jnp.float32
    )
    grad_key = jnp.einsum("gqk,qgc->kgc", grad_scores, queries, preferred_element_type=jnp.float32)
    grad_value = jnp.einsum(
        "gqk,qgc->kgc", probs_low, grad_attn, preferred_element_type=jnp.float32
    )
    return (attended, grad_query, grad_key, grad_value)


def shards(patches, weights, cotangent, loss_mask):
    rows = patches.shape[1]
    width = patches.shape[2]
    inner = weights.shape[2]
    span = (WIN + rows - 2) // rows
    block_rows = min(512, rows)
    key_len = block_rows + span * rows
    group = max(1, min(HEADS, 128 // HSIZE))
    group_cols = group * HSIZE
    inv_scale = 1.0 / math.sqrt(HSIZE)
    local_in = patches[0].astype(jnp.float32)
    inv_rms = lax.rsqrt(jnp.mean(local_in * local_in, axis=-1) + 1e-06)
    normed_full = local_in * inv_rms[:, None]
    normed = normed_full.astype(jnp.bfloat16)
    proj_weights = weights[:, :3, :]
    projected = jnp.einsum(
        "rd,dwh->wrh", normed, proj_weights, preferred_element_type=jnp.float32
    ).astype(jnp.bfloat16)
    queries = projected[0]
    key_vals = projected[1:]
    earlier = [shifted(key_vals, "tm", offset) for offset in range(span, 0, -1)]
    extended = jnp.concatenate(earlier + [key_vals], axis=1)
    local_count = jnp.sum(loss_mask.astype(jnp.int32))
    tokens_all = rows * lax.axis_size("tm") * lax.axis_size("night")
    local_cot = cotangent[0]
    grad_out = jnp.where(loss_mask[0][:, None] > 0, local_cot, jnp.zeros_like(local_cot))
    grad_attn = jnp.dot(grad_out, weights[:, 3, :], preferred_element_type=jnp.float32).astype(
        jnp.bfloat16
    )
    base = lax.axis_index("tm") * rows
    query_idx = jnp.arange(block_rows, dtype=jnp.int32)[:, None]
    key_idx = jnp.arange(key_len, dtype=jnp.int32)[None, :]
    offsets = query_idx - key_idx + span * rows
    band = (offsets >= 0) & (offsets < WIN)
    attended_cols = []
    grad_q_cols = []
    grad_kv_cols = []
    for first in range(0, inner, group_cols):
        accum = jnp.zeros((2, (span + 1) * rows, group_cols), jnp.float32)
        valid = (band & (key_idx >= span * rows - base - 0)).astype(jnp.float32)
        query_blk = queries[0:block_rows, first : first + group_cols].reshape(
            block_rows, group, HSIZE
        )
        kv_blk = extended[:, 0:key_len, first : first + group_cols].reshape(
            2, key_len, group, HSIZE
        )
        grad_blk = grad_attn[0:block_rows, first : first + group_cols].reshape(
            block_rows, group, HSIZE
        )
        attended, grad_query, grad_key, grad_value = band_block(
            query_blk, kv_blk[0], kv_blk[1], grad_blk, valid, inv_scale
        )
        attended_rows = attended.reshape(block_rows, group_cols)
        grad_q_rows = grad_query.reshape(block_rows, group_cols).astype(jnp.bfloat16)
        update = jnp.stack([grad_key, grad_value]).reshape(2, key_len, group_cols)
        accum = accum.at[:, 0:key_len].add(update)
        attended_cols.append(attended_rows)
        grad_q_cols.append(grad_q_rows)
        grad_kv_cols.append(accum)
    attended_all = jnp.concatenate(attended_cols, axis=1)
    grad_q = jnp.concatenate(grad_q_cols, axis=1)
    grad_kv_ext = jnp.concatenate(grad_kv_cols, axis=2)
    owned = grad_kv_ext[:, span * rows :]
    for offset in range(1, span + 1):
        lower = (span - offset) * rows
        owned = owned + shifted(
            grad_kv_ext[:, lower : lower + rows].astype(jnp.bfloat16), "tm", -offset
        ).astype(jnp.float32)
    grad_kv = owned.astype(jnp.bfloat16)
    grad_proj = jnp.concatenate([grad_q[None], grad_kv], axis=0)
    grad_normed = jnp.einsum(
        "wrh,dwh->rd", grad_proj, proj_weights, preferred_element_type=jnp.float32
    )
    along = jnp.sum(grad_normed * normed_full, axis=-1) / width
    unscaled_input = inv_rms[:, None] * (grad_normed - normed_full * along[:, None])
    proj_part = jnp.einsum("rd,wrh->dwh", normed, grad_proj, preferred_element_type=jnp.float32)
    out_part = jnp.einsum("rd,rh->dh", grad_out, attended_all, preferred_element_type=jnp.float32)
    summed, count = scatter_rows(
        jnp.concatenate([proj_part, out_part[:, None]], axis=1),
        local_count,
        ("tm", "night"),
        "tm",
        jnp.float32,
    )
    total_count = count.astype(jnp.float32)
    loss_scale = jnp.float32(tokens_all) / total_count
    grad_input = (loss_scale * unscaled_input).astype(jnp.bfloat16)
    grad_weights = summed * (jnp.sqrt(jnp.float32(tokens_all)) / total_count)
    return (grad_input[None], grad_weights)


def solution(mesh):
    return jax.shard_map(
        shards,
        mesh=mesh,
        in_specs=(P("night", "tm", None), P(), P("night", "tm", None), P("night", "tm")),
        out_specs=(P("night", "tm", None), P(("tm", "night"), None, None)),
        check_vma=False,
    )
```

```python
import math

import jax
import jax.numpy as jnp
from jax import lax
from jax.sharding import PartitionSpec as P

HEADS = 8
HSIZE = 64
WIN = 1024


def shifted(value, axis, by):
    peers = lax.axis_size(axis)
    pairs = [(i, i + by) for i in range(peers) if 0 <= i + by < peers]
    return lax.ppermute(value, axis, pairs)


def is_power_of_two(n):
    return n > 0 and n & (n - 1) == 0


def halve(value, dim, axis, flip, send_type):
    peers = lax.axis_size(axis)
    bit = (lax.axis_index(axis) // flip) % 2
    keep = lax.dynamic_index_in_dim(value, bit, dim, keepdims=False)
    send = lax.dynamic_index_in_dim(value, 1 - bit, dim, keepdims=False)
    pairs = [(i, i ^ flip) for i in range(peers)]
    return keep + lax.ppermute(send.astype(send_type), axis, pairs).astype(keep.dtype)


def swap_add(value, anchor, axis, flip):
    value, anchor = lax.optimization_barrier((value, anchor))
    peers = lax.axis_size(axis)
    pairs = [(i, i ^ flip) for i in range(peers)]
    return value + lax.ppermute(value, axis, pairs), anchor


def scatter_rows(value, tally, axes, first_axis, wire_type):
    sizes = [lax.axis_size(axis) for axis in axes]
    rows = value.shape[0]
    groups = math.prod(sizes)
    if not all(is_power_of_two(n) for n in sizes) or rows % groups:
        return (
            lax.psum_scatter(value, axes, scatter_dimension=0, tiled=True),
            lax.psum(tally, axes),
        )
    stages = [
        (axis, 1 << (n.bit_length() - 2 - i))
        for axis, n in zip(axes, sizes)
        for i in range(n.bit_length() - 1)
    ]
    if not stages:
        return value, tally
    rest = value.shape[1:]
    value = value.reshape((2,) * len(stages) + (rows // groups,) + rest)
    names = list(stages)

    def step(part, part_names, stage, send_type):
        dim = part_names.index(stage)
        return halve(part, dim, *stage, send_type), part_names[:dim] + part_names[dim + 1 :]

    first = (first_axis, 1) if (first_axis, 1) in stages else stages[-1]
    value, names = step(value, names, first, value.dtype)
    tally, value = swap_add(tally, value, *first)
    middle = [s for s in stages if s[0] == first[0] and s != first]
    tail = [s for s in stages if s[0] != first[0]][::-1]
    if len(middle) > 1 and rest[-1] % 2 == 0:
        cut = rest[-1] // 2
        left, right = value[..., :cut], value[..., cut:]
        left_names, right_names = list(names), list(names)
        for a, b in zip(middle, middle[::-1]):
            left, left_names = step(left, left_names, a, wire_type)
            tally, left = swap_add(tally, left, *a)
            right, right_names = step(right, right_names, b, wire_type)
        value = jnp.concatenate([left, right], axis=-1)
        names = left_names
    else:
        for stage in middle:
            value, names = step(value, names, stage, wire_type)
            tally, value = swap_add(tally, value, *stage)
    for stage in tail:
        value, names = step(value, names, stage, wire_type)
        tally, value = swap_add(tally, value, *stage)
    return value, tally


def band_block(queries, keys_blk, values_blk, grad_attn, valid, inv_scale):
    scores = (
        jnp.einsum("qgc,kgc->gqk", queries, keys_blk, preferred_element_type=jnp.float32)
        * inv_scale
    )
    exp_terms = jnp.exp(scores) * valid[None]
    probs = exp_terms / jnp.sum(exp_terms, axis=-1, keepdims=True)
    probs_low = probs.astype(jnp.bfloat16)
    attended = jnp.einsum(
        "gqk,kgc->qgc", probs_low, values_blk, preferred_element_type=jnp.float32
    ).astype(jnp.bfloat16)
    delta = jnp.sum(grad_attn.astype(jnp.float32) * attended.astype(jnp.float32), axis=-1)
    grad_probs = jnp.einsum(
        "qgc,kgc->gqk", grad_attn, values_blk, preferred_element_type=jnp.float32
    )
    grad_scores = (probs * (grad_probs - jnp.transpose(delta)[:, :, None]) * inv_scale).astype(
        jnp.bfloat16
    )
    grad_query = jnp.einsum(
        "gqk,kgc->qgc", grad_scores, keys_blk, preferred_element_type=jnp.float32
    )
    grad_key = jnp.einsum("gqk,qgc->kgc", grad_scores, queries, preferred_element_type=jnp.float32)
    grad_value = jnp.einsum(
        "gqk,qgc->kgc", probs_low, grad_attn, preferred_element_type=jnp.float32
    )
    return (attended, grad_query, grad_key, grad_value)


def shards(patches, weights, cotangent, loss_mask):
    rows = patches.shape[1]
    width = patches.shape[2]
    inner = weights.shape[2]
    span = (WIN + rows - 2) // rows
    block_rows = min(512, rows)
    key_len = block_rows + span * rows
    group = max(1, min(HEADS, 128 // HSIZE))
    group_cols = group * HSIZE
    inv_scale = 1.0 / math.sqrt(HSIZE)
    local_in = patches[0].astype(jnp.float32)
    inv_rms = lax.rsqrt(jnp.mean(local_in * local_in, axis=-1) + 1e-06)
    normed_full = local_in * inv_rms[:, None]
    normed = normed_full.astype(jnp.bfloat16)
    proj_weights = weights[:, :3, :]
    projected = jnp.einsum(
        "rd,dwh->wrh", normed, proj_weights, preferred_element_type=jnp.float32
    ).astype(jnp.bfloat16)
    queries = projected[0]
    key_vals = projected[1:]
    earlier = [shifted(key_vals, "tm", offset) for offset in range(span, 0, -1)]
    extended = jnp.concatenate(earlier + [key_vals], axis=1)
    local_count = jnp.sum(loss_mask.astype(jnp.int32))
    tokens_all = rows * lax.axis_size("tm") * lax.axis_size("night")
    local_cot = cotangent[0]
    grad_out = jnp.where(loss_mask[0][:, None] > 0, local_cot, jnp.zeros_like(local_cot))
    grad_attn = jnp.dot(grad_out, weights[:, 3, :], preferred_element_type=jnp.float32).astype(
        jnp.bfloat16
    )
    base = lax.axis_index("tm") * rows
    query_idx = jnp.arange(block_rows, dtype=jnp.int32)[:, None]
    key_idx = jnp.arange(key_len, dtype=jnp.int32)[None, :]
    offsets = query_idx - key_idx + span * rows
    band = (offsets >= 0) & (offsets < WIN)
    attended_cols = []
    grad_q_cols = []
    grad_kv_cols = []
    for first in range(0, inner, group_cols):
        accum = jnp.zeros((2, (span + 1) * rows, group_cols), jnp.float32)
        valid = (band & (key_idx >= span * rows - base - 0)).astype(jnp.float32)
        query_blk = queries[0:block_rows, first : first + group_cols].reshape(
            block_rows, group, HSIZE
        )
        kv_blk = extended[:, 0:key_len, first : first + group_cols].reshape(
            2, key_len, group, HSIZE
        )
        grad_blk = grad_attn[0:block_rows, first : first + group_cols].reshape(
            block_rows, group, HSIZE
        )
        attended, grad_query, grad_key, grad_value = band_block(
            query_blk, kv_blk[0], kv_blk[1], grad_blk, valid, inv_scale
        )
        attended_rows = attended.reshape(block_rows, group_cols)
        grad_q_rows = grad_query.reshape(block_rows, group_cols).astype(jnp.bfloat16)
        update = jnp.stack([grad_key, grad_value]).reshape(2, key_len, group_cols)
        accum = accum.at[:, 0:key_len].add(update)
        attended_cols.append(attended_rows)
        grad_q_cols.append(grad_q_rows)
        grad_kv_cols.append(accum)
    attended_all = jnp.concatenate(attended_cols, axis=1)
    grad_q = jnp.concatenate(grad_q_cols, axis=1)
    grad_kv_ext = jnp.concatenate(grad_kv_cols, axis=2)
    owned = grad_kv_ext[:, span * rows :]
    for offset in range(1, span + 1):
        lower = (span - offset) * rows
        owned = owned + shifted(
            grad_kv_ext[:, lower : lower + rows].astype(jnp.bfloat16), "tm", -offset
        ).astype(jnp.float32)
    grad_kv = owned.astype(jnp.bfloat16)
    grad_proj = jnp.concatenate([grad_q[None], grad_kv], axis=0)
    grad_normed = jnp.einsum(
        "wrh,dwh->rd", grad_proj, proj_weights, preferred_element_type=jnp.float32
    )
    along = jnp.sum(grad_normed * normed_full, axis=-1) / width
    unscaled_input = inv_rms[:, None] * (grad_normed - normed_full * along[:, None])
    proj_part = jnp.einsum("rd,wrh->dwh", normed, grad_proj, preferred_element_type=jnp.float32)
    out_part = jnp.einsum("rd,rh->dh", grad_out, attended_all, preferred_element_type=jnp.float32)
    summed, count = scatter_rows(
        jnp.concatenate([proj_part, out_part[:, None]], axis=1),
        local_count,
        ("tm", "night"),
        "tm",
        jnp.float32,
    )
    total_count = count.astype(jnp.float32)
    loss_scale = jnp.float32(tokens_all) / total_count
    grad_input = (loss_scale * unscaled_input).astype(jnp.bfloat16)
    grad_weights = summed * (jnp.sqrt(jnp.float32(tokens_all)) / total_count)
    return (grad_input[None], grad_weights)


def solution(mesh):
    return jax.shard_map(
        shards,
        mesh=mesh,
        in_specs=(P("night", "tm", None), P(), P("night", "tm", None), P("night", "tm")),
        out_specs=(P("night", "tm", None), P(("tm", "night"), None, None)),
        check_vma=False,
    )
```

```python
import math

import jax
import jax.numpy as jnp
from jax import lax
from jax.sharding import PartitionSpec as P

HEADS = 8
HSIZE = 64
WIN = 1024


def shifted(value, axis, by):
    peers = lax.axis_size(axis)
    pairs = [(i, i + by) for i in range(peers) if 0 <= i + by < peers]
    return lax.ppermute(value, axis, pairs)


def is_power_of_two(n):
    return n > 0 and n & (n - 1) == 0


def halve(value, dim, axis, flip, send_type):
    peers = lax.axis_size(axis)
    bit = (lax.axis_index(axis) // flip) % 2
    keep = lax.dynamic_index_in_dim(value, bit, dim, keepdims=False)
    send = lax.dynamic_index_in_dim(value, 1 - bit, dim, keepdims=False)
    pairs = [(i, i ^ flip) for i in range(peers)]
    return keep + lax.ppermute(send.astype(send_type), axis, pairs).astype(keep.dtype)


def swap_add(value, anchor, axis, flip):
    value, anchor = lax.optimization_barrier((value, anchor))
    peers = lax.axis_size(axis)
    pairs = [(i, i ^ flip) for i in range(peers)]
    return value + lax.ppermute(value, axis, pairs), anchor


def scatter_rows(value, tally, axes, first_axis, wire_type):
    sizes = [lax.axis_size(axis) for axis in axes]
    rows = value.shape[0]
    groups = math.prod(sizes)
    if not all(is_power_of_two(n) for n in sizes) or rows % groups:
        return (
            lax.psum_scatter(value, axes, scatter_dimension=0, tiled=True),
            lax.psum(tally, axes),
        )
    stages = [
        (axis, 1 << (n.bit_length() - 2 - i))
        for axis, n in zip(axes, sizes)
        for i in range(n.bit_length() - 1)
    ]
    if not stages:
        return value, tally
    rest = value.shape[1:]
    value = value.reshape((2,) * len(stages) + (rows // groups,) + rest)
    names = list(stages)

    def step(part, part_names, stage, send_type):
        dim = part_names.index(stage)
        return halve(part, dim, *stage, send_type), part_names[:dim] + part_names[dim + 1 :]

    first = (first_axis, 1) if (first_axis, 1) in stages else stages[-1]
    value, names = step(value, names, first, value.dtype)
    tally, value = swap_add(tally, value, *first)
    middle = [s for s in stages if s[0] == first[0] and s != first]
    tail = [s for s in stages if s[0] != first[0]][::-1]
    if len(middle) > 1 and rest[-1] % 2 == 0:
        cut = rest[-1] // 2
        left, right = value[..., :cut], value[..., cut:]
        left_names, right_names = list(names), list(names)
        for a, b in zip(middle, middle[::-1]):
            left, left_names = step(left, left_names, a, wire_type)
            tally, left = swap_add(tally, left, *a)
            right, right_names = step(right, right_names, b, wire_type)
        value = jnp.concatenate([left, right], axis=-1)
        names = left_names
    else:
        for stage in middle:
            value, names = step(value, names, stage, wire_type)
            tally, value = swap_add(tally, value, *stage)
    for stage in tail:
        value, names = step(value, names, stage, wire_type)
        tally, value = swap_add(tally, value, *stage)
    return value, tally


def band_block(queries, keys_blk, values_blk, grad_attn, valid, inv_scale):
    scores = (
        jnp.einsum("qgc,kgc->gqk", queries, keys_blk, preferred_element_type=jnp.float32)
        * inv_scale
    )
    exp_terms = jnp.exp(scores) * valid[None]
    probs = exp_terms / jnp.sum(exp_terms, axis=-1, keepdims=True)
    probs_low = probs.astype(jnp.bfloat16)
    attended = jnp.einsum(
        "gqk,kgc->qgc", probs_low, values_blk, preferred_element_type=jnp.float32
    ).astype(jnp.bfloat16)
    delta = jnp.sum(grad_attn.astype(jnp.float32) * attended.astype(jnp.float32), axis=-1)
    grad_probs = jnp.einsum(
        "qgc,kgc->gqk", grad_attn, values_blk, preferred_element_type=jnp.float32
    )
    grad_scores = (probs * (grad_probs - jnp.transpose(delta)[:, :, None]) * inv_scale).astype(
        jnp.bfloat16
    )
    grad_query = jnp.einsum(
        "gqk,kgc->qgc", grad_scores, keys_blk, preferred_element_type=jnp.float32
    )
    grad_key = jnp.einsum("gqk,qgc->kgc", grad_scores, queries, preferred_element_type=jnp.float32)
    grad_value = jnp.einsum(
        "gqk,qgc->kgc", probs_low, grad_attn, preferred_element_type=jnp.float32
    )
    return (attended, grad_query, grad_key, grad_value)


def shards(patches, weights, cotangent, loss_mask):
    rows = patches.shape[1]
    width = patches.shape[2]
    inner = weights.shape[2]
    span = (WIN + rows - 2) // rows
    block_rows = min(512, rows)
    key_len = block_rows + span * rows
    group = max(1, min(HEADS, 128 // HSIZE))
    group_cols = group * HSIZE
    inv_scale = 1.0 / math.sqrt(HSIZE)
    local_in = patches[0].astype(jnp.float32)
    inv_rms = lax.rsqrt(jnp.mean(local_in * local_in, axis=-1) + 1e-06)
    normed_full = local_in * inv_rms[:, None]
    normed = normed_full.astype(jnp.bfloat16)
    proj_weights = weights[:, :3, :]
    projected = jnp.einsum(
        "rd,dwh->wrh", normed, proj_weights, preferred_element_type=jnp.float32
    ).astype(jnp.bfloat16)
    queries = projected[0]
    key_vals = projected[1:]
    earlier = [shifted(key_vals, "tm", offset) for offset in range(span, 0, -1)]
    extended = jnp.concatenate(earlier + [key_vals], axis=1)
    local_count = jnp.sum(loss_mask.astype(jnp.int32))
    tokens_all = rows * lax.axis_size("tm") * lax.axis_size("night")
    local_cot = cotangent[0]
    grad_out = jnp.where(loss_mask[0][:, None] > 0, local_cot, jnp.zeros_like(local_cot))
    grad_attn = jnp.dot(grad_out, weights[:, 3, :], preferred_element_type=jnp.float32).astype(
        jnp.bfloat16
    )
    base = lax.axis_index("tm") * rows
    query_idx = jnp.arange(block_rows, dtype=jnp.int32)[:, None]
    key_idx = jnp.arange(key_len, dtype=jnp.int32)[None, :]
    offsets = query_idx - key_idx + span * rows
    band = (offsets >= 0) & (offsets < WIN)
    attended_cols = []
    grad_q_cols = []
    grad_kv_cols = []
    for first in range(0, inner, group_cols):
        accum = jnp.zeros((2, (span + 1) * rows, group_cols), jnp.float32)
        valid = (band & (key_idx >= span * rows - base - 0)).astype(jnp.float32)
        query_blk = queries[0:block_rows, first : first + group_cols].reshape(
            block_rows, group, HSIZE
        )
        kv_blk = extended[:, 0:key_len, first : first + group_cols].reshape(
            2, key_len, group, HSIZE
        )
        grad_blk = grad_attn[0:block_rows, first : first + group_cols].reshape(
            block_rows, group, HSIZE
        )
        attended, grad_query, grad_key, grad_value = band_block(
            query_blk, kv_blk[0], kv_blk[1], grad_blk, valid, inv_scale
        )
        attended_rows = attended.reshape(block_rows, group_cols)
        grad_q_rows = grad_query.reshape(block_rows, group_cols).astype(jnp.bfloat16)
        update = jnp.stack([grad_key, grad_value]).reshape(2, key_len, group_cols)
        accum = accum.at[:, 0:key_len].add(update)
        attended_cols.append(attended_rows)
        grad_q_cols.append(grad_q_rows)
        grad_kv_cols.append(accum)
    attended_all = jnp.concatenate(attended_cols, axis=1)
    grad_q = jnp.concatenate(grad_q_cols, axis=1)
    grad_kv_ext = jnp.concatenate(grad_kv_cols, axis=2)
    owned = grad_kv_ext[:, span * rows :]
    for offset in range(1, span + 1):
        lower = (span - offset) * rows
        owned = owned + shifted(
            grad_kv_ext[:, lower : lower + rows].astype(jnp.bfloat16), "tm", -offset
        ).astype(jnp.float32)
    grad_kv = owned.astype(jnp.bfloat16)
    grad_proj = jnp.concatenate([grad_q[None], grad_kv], axis=0)
    grad_normed = jnp.einsum(
        "wrh,dwh->rd", grad_proj, proj_weights, preferred_element_type=jnp.float32
    )
    along = jnp.sum(grad_normed * normed_full, axis=-1) / width
    unscaled_input = inv_rms[:, None] * (grad_normed - normed_full * along[:, None])
    proj_part = jnp.einsum("rd,wrh->dwh", normed, grad_proj, preferred_element_type=jnp.float32)
    out_part = jnp.einsum("rd,rh->dh", grad_out, attended_all, preferred_element_type=jnp.float32)
    summed, count = scatter_rows(
        jnp.concatenate([proj_part, out_part[:, None]], axis=1),
        local_count,
        ("tm", "night"),
        "tm",
        jnp.bfloat16,
    )
    total_count = count.astype(jnp.float32)
    loss_scale = jnp.float32(tokens_all) / total_count
    grad_input = (loss_scale * unscaled_input).astype(jnp.bfloat16)
    grad_weights = summed * (jnp.sqrt(jnp.float32(tokens_all)) / total_count)
    return (grad_input[None], grad_weights)


def solution(mesh):
    return jax.shard_map(
        shards,
        mesh=mesh,
        in_specs=(P("night", "tm", None), P(), P("night", "tm", None), P("night", "tm")),
        out_specs=(P("night", "tm", None), P(("tm", "night"), None, None)),
        check_vma=False,
    )
```

```python
import math

import jax
import jax.numpy as jnp
from jax import lax
from jax.sharding import PartitionSpec as P

HEADS = 8
HSIZE = 64
WIN = 1024


def shifted(value, axis, by):
    peers = lax.axis_size(axis)
    pairs = [(i, i + by) for i in range(peers) if 0 <= i + by < peers]
    return lax.ppermute(value, axis, pairs)


def is_power_of_two(n):
    return n > 0 and n & (n - 1) == 0


def halve(value, dim, axis, flip, send_type):
    peers = lax.axis_size(axis)
    bit = (lax.axis_index(axis) // flip) % 2
    keep = lax.dynamic_index_in_dim(value, bit, dim, keepdims=False)
    send = lax.dynamic_index_in_dim(value, 1 - bit, dim, keepdims=False)
    pairs = [(i, i ^ flip) for i in range(peers)]
    return keep + lax.ppermute(send.astype(send_type), axis, pairs).astype(keep.dtype)


def swap_add(value, anchor, axis, flip):
    value, anchor = lax.optimization_barrier((value, anchor))
    peers = lax.axis_size(axis)
    pairs = [(i, i ^ flip) for i in range(peers)]
    return value + lax.ppermute(value, axis, pairs), anchor


def scatter_rows(value, tally, axes, first_axis, wire_type):
    sizes = [lax.axis_size(axis) for axis in axes]
    rows = value.shape[0]
    groups = math.prod(sizes)
    if not all(is_power_of_two(n) for n in sizes) or rows % groups:
        return (
            lax.psum_scatter(value, axes, scatter_dimension=0, tiled=True),
            lax.psum(tally, axes),
        )
    stages = [
        (axis, 1 << (n.bit_length() - 2 - i))
        for axis, n in zip(axes, sizes)
        for i in range(n.bit_length() - 1)
    ]
    if not stages:
        return value, tally
    rest = value.shape[1:]
    value = value.reshape((2,) * len(stages) + (rows // groups,) + rest)
    names = list(stages)

    def step(part, part_names, stage, send_type):
        dim = part_names.index(stage)
        return halve(part, dim, *stage, send_type), part_names[:dim] + part_names[dim + 1 :]

    first = (first_axis, 1) if (first_axis, 1) in stages else stages[-1]
    value, names = step(value, names, first, value.dtype)
    tally, value = swap_add(tally, value, *first)
    middle = [s for s in stages if s[0] == first[0] and s != first]
    tail = [s for s in stages if s[0] != first[0]][::-1]
    if len(middle) > 1 and rest[-1] % 2 == 0:
        cut = rest[-1] // 2
        left, right = value[..., :cut], value[..., cut:]
        left_names, right_names = list(names), list(names)
        for a, b in zip(middle, middle[::-1]):
            left, left_names = step(left, left_names, a, wire_type)
            tally, left = swap_add(tally, left, *a)
            right, right_names = step(right, right_names, b, wire_type)
        value = jnp.concatenate([left, right], axis=-1)
        names = left_names
    else:
        for stage in middle:
            value, names = step(value, names, stage, wire_type)
            tally, value = swap_add(tally, value, *stage)
    for stage in tail:
        value, names = step(value, names, stage, wire_type)
        tally, value = swap_add(tally, value, *stage)
    return value, tally


def band_block(queries, keys_blk, values_blk, grad_attn, valid, inv_scale):
    scores = (
        jnp.einsum("qgc,kgc->gqk", queries, keys_blk, preferred_element_type=jnp.float32)
        * inv_scale
    )
    exp_terms = jnp.exp(scores) * valid[None]
    probs = exp_terms / jnp.sum(exp_terms, axis=-1, keepdims=True)
    probs_low = probs.astype(jnp.bfloat16)
    attended = jnp.einsum(
        "gqk,kgc->qgc", probs_low, values_blk, preferred_element_type=jnp.float32
    ).astype(jnp.bfloat16)
    delta = jnp.sum(grad_attn.astype(jnp.float32) * attended.astype(jnp.float32), axis=-1)
    grad_probs = jnp.einsum(
        "qgc,kgc->gqk", grad_attn, values_blk, preferred_element_type=jnp.float32
    )
    grad_scores = (probs * (grad_probs - jnp.transpose(delta)[:, :, None]) * inv_scale).astype(
        jnp.bfloat16
    )
    grad_query = jnp.einsum(
        "gqk,kgc->qgc", grad_scores, keys_blk, preferred_element_type=jnp.float32
    )
    grad_key = jnp.einsum("gqk,qgc->kgc", grad_scores, queries, preferred_element_type=jnp.float32)
    grad_value = jnp.einsum(
        "gqk,qgc->kgc", probs_low, grad_attn, preferred_element_type=jnp.float32
    )
    return (attended, grad_query, grad_key, grad_value)


def shards(patches, weights, cotangent, loss_mask):
    rows = patches.shape[1]
    width = patches.shape[2]
    inner = weights.shape[2]
    span = (WIN + rows - 2) // rows
    block_rows = min(512, rows)
    key_len = block_rows + span * rows
    group = HEADS
    group_cols = group * HSIZE
    inv_scale = 1.0 / math.sqrt(HSIZE)
    local_in = patches[0].astype(jnp.float32)
    inv_rms = lax.rsqrt(jnp.mean(local_in * local_in, axis=-1) + 1e-06)
    normed_full = local_in * inv_rms[:, None]
    normed = normed_full.astype(jnp.bfloat16)
    proj_weights = weights[:, :3, :]
    projected = jnp.einsum(
        "rd,dwh->wrh", normed, proj_weights, preferred_element_type=jnp.float32
    ).astype(jnp.bfloat16)
    queries = projected[0]
    key_vals = projected[1:]
    earlier = [shifted(key_vals, "tm", offset) for offset in range(span, 0, -1)]
    extended = jnp.concatenate(earlier + [key_vals], axis=1)
    local_count = jnp.sum(loss_mask.astype(jnp.int32))
    tokens_all = rows * lax.axis_size("tm") * lax.axis_size("night")
    local_cot = cotangent[0]
    grad_out = jnp.where(loss_mask[0][:, None] > 0, local_cot, jnp.zeros_like(local_cot))
    grad_attn = jnp.dot(grad_out, weights[:, 3, :], preferred_element_type=jnp.float32).astype(
        jnp.bfloat16
    )
    base = lax.axis_index("tm") * rows
    query_idx = jnp.arange(block_rows, dtype=jnp.int32)[:, None]
    key_idx = jnp.arange(key_len, dtype=jnp.int32)[None, :]
    offsets = query_idx - key_idx + span * rows
    band = (offsets >= 0) & (offsets < WIN)
    attended_cols = []
    grad_q_cols = []
    grad_kv_cols = []
    for first in range(0, inner, group_cols):
        accum = jnp.zeros((2, (span + 1) * rows, group_cols), jnp.float32)
        valid = (band & (key_idx >= span * rows - base - 0)).astype(jnp.float32)
        query_blk = queries[0:block_rows, first : first + group_cols].reshape(
            block_rows, group, HSIZE
        )
        kv_blk = extended[:, 0:key_len, first : first + group_cols].reshape(
            2, key_len, group, HSIZE
        )
        grad_blk = grad_attn[0:block_rows, first : first + group_cols].reshape(
            block_rows, group, HSIZE
        )
        attended, grad_query, grad_key, grad_value = band_block(
            query_blk, kv_blk[0], kv_blk[1], grad_blk, valid, inv_scale
        )
        attended_rows = attended.reshape(block_rows, group_cols)
        grad_q_rows = grad_query.reshape(block_rows, group_cols).astype(jnp.bfloat16)
        update = jnp.stack([grad_key, grad_value]).reshape(2, key_len, group_cols)
        accum = accum.at[:, 0:key_len].add(update)
        attended_cols.append(attended_rows)
        grad_q_cols.append(grad_q_rows)
        grad_kv_cols.append(accum)
    attended_all = jnp.concatenate(attended_cols, axis=1)
    grad_q = jnp.concatenate(grad_q_cols, axis=1)
    grad_kv_ext = jnp.concatenate(grad_kv_cols, axis=2)
    owned = grad_kv_ext[:, span * rows :]
    for offset in range(1, span + 1):
        lower = (span - offset) * rows
        owned = owned + shifted(
            grad_kv_ext[:, lower : lower + rows].astype(jnp.bfloat16), "tm", -offset
        ).astype(jnp.float32)
    grad_kv = owned.astype(jnp.bfloat16)
    grad_proj = jnp.concatenate([grad_q[None], grad_kv], axis=0)
    grad_normed = jnp.einsum(
        "wrh,dwh->rd", grad_proj, proj_weights, preferred_element_type=jnp.float32
    )
    along = jnp.sum(grad_normed * normed_full, axis=-1) / width
    unscaled_input = inv_rms[:, None] * (grad_normed - normed_full * along[:, None])
    proj_part = jnp.einsum("rd,wrh->dwh", normed, grad_proj, preferred_element_type=jnp.float32)
    out_part = jnp.einsum("rd,rh->dh", grad_out, attended_all, preferred_element_type=jnp.float32)
    summed, count = scatter_rows(
        jnp.concatenate([proj_part, out_part[:, None]], axis=1),
        local_count,
        ("tm", "night"),
        "tm",
        jnp.bfloat16,
    )
    total_count = count.astype(jnp.float32)
    loss_scale = jnp.float32(tokens_all) / total_count
    grad_input = (loss_scale * unscaled_input).astype(jnp.bfloat16)
    grad_weights = summed * (jnp.sqrt(jnp.float32(tokens_all)) / total_count)
    return (grad_input[None], grad_weights)


def solution(mesh):
    return jax.shard_map(
        shards,
        mesh=mesh,
        in_specs=(P("night", "tm", None), P(), P("night", "tm", None), P("night", "tm")),
        out_specs=(P("night", "tm", None), P(("tm", "night"), None, None)),
        check_vma=False,
    )
```

```python
import math

import jax
import jax.numpy as jnp
from jax import lax
from jax.sharding import PartitionSpec as P

HEADS = 8
HSIZE = 64
WIN = 1024


def shifted(value, axis, by):
    peers = lax.axis_size(axis)
    pairs = [(i, i + by) for i in range(peers) if 0 <= i + by < peers]
    return lax.ppermute(value, axis, pairs)


def is_power_of_two(n):
    return n > 0 and n & (n - 1) == 0


def halve(value, dim, axis, flip, send_type):
    peers = lax.axis_size(axis)
    bit = (lax.axis_index(axis) // flip) % 2
    keep = lax.dynamic_index_in_dim(value, bit, dim, keepdims=False)
    send = lax.dynamic_index_in_dim(value, 1 - bit, dim, keepdims=False)
    pairs = [(i, i ^ flip) for i in range(peers)]
    return keep + lax.ppermute(send.astype(send_type), axis, pairs).astype(keep.dtype)


def swap_add(value, anchor, axis, flip):
    value, anchor = lax.optimization_barrier((value, anchor))
    peers = lax.axis_size(axis)
    pairs = [(i, i ^ flip) for i in range(peers)]
    return value + lax.ppermute(value, axis, pairs), anchor


def scatter_rows(value, tally, axes, first_axis, wire_type, tail_first=False):
    sizes = [lax.axis_size(axis) for axis in axes]
    rows = value.shape[0]
    groups = math.prod(sizes)
    if not all(is_power_of_two(n) for n in sizes) or rows % groups:
        return (
            lax.psum_scatter(value, axes, scatter_dimension=0, tiled=True),
            None if tally is None else lax.psum(tally, axes),
        )
    stages = [
        (axis, 1 << (n.bit_length() - 2 - i))
        for axis, n in zip(axes, sizes)
        for i in range(n.bit_length() - 1)
    ]
    if not stages:
        return value, tally
    rest = value.shape[1:]
    value = value.reshape((2,) * len(stages) + (rows // groups,) + rest)
    names = list(stages)

    def step(part, part_names, stage, send_type):
        dim = part_names.index(stage)
        return halve(part, dim, *stage, send_type), part_names[:dim] + part_names[dim + 1 :]

    first = (first_axis, 1) if (first_axis, 1) in stages else stages[-1]
    def count_along(tally, anchor, stage):
        if tally is None:
            return tally, anchor
        return swap_add(tally, anchor, *stage)

    def run_tail(value, names, tally):
        for stage in tail:
            value, names = step(value, names, stage, wire_type)
            tally, value = count_along(tally, value, stage)
        return value, names, tally

    value, names = step(value, names, first, value.dtype)
    tally, value = count_along(tally, value, first)
    middle = [s for s in stages if s[0] == first[0] and s != first]
    tail = [s for s in stages if s[0] != first[0]][::-1]
    if tail_first:
        value, names, tally = run_tail(value, names, tally)
    if len(middle) > 1 and rest[-1] % 2 == 0:
        cut = rest[-1] // 2
        left, right = value[..., :cut], value[..., cut:]
        left_names, right_names = list(names), list(names)
        for a, b in zip(middle, middle[::-1]):
            left, left_names = step(left, left_names, a, wire_type)
            tally, left = count_along(tally, left, a)
            right, right_names = step(right, right_names, b, wire_type)
        value = jnp.concatenate([left, right], axis=-1)
        names = left_names
    else:
        for stage in middle:
            value, names = step(value, names, stage, wire_type)
            tally, value = count_along(tally, value, stage)
    if not tail_first:
        value, names, tally = run_tail(value, names, tally)
    return value, tally


def band_block(queries, keys_blk, values_blk, grad_attn, valid, inv_scale):
    scores = (
        jnp.einsum("qgc,kgc->gqk", queries, keys_blk, preferred_element_type=jnp.float32)
        * inv_scale
    )
    exp_terms = jnp.exp(scores) * valid[None]
    probs = exp_terms / jnp.sum(exp_terms, axis=-1, keepdims=True)
    probs_low = probs.astype(jnp.bfloat16)
    attended = jnp.einsum(
        "gqk,kgc->qgc", probs_low, values_blk, preferred_element_type=jnp.float32
    ).astype(jnp.bfloat16)
    delta = jnp.sum(grad_attn.astype(jnp.float32) * attended.astype(jnp.float32), axis=-1)
    grad_probs = jnp.einsum(
        "qgc,kgc->gqk", grad_attn, values_blk, preferred_element_type=jnp.float32
    )
    grad_scores = (probs * (grad_probs - jnp.transpose(delta)[:, :, None]) * inv_scale).astype(
        jnp.bfloat16
    )
    grad_query = jnp.einsum(
        "gqk,kgc->qgc", grad_scores, keys_blk, preferred_element_type=jnp.float32
    )
    grad_key = jnp.einsum("gqk,qgc->kgc", grad_scores, queries, preferred_element_type=jnp.float32)
    grad_value = jnp.einsum(
        "gqk,qgc->kgc", probs_low, grad_attn, preferred_element_type=jnp.float32
    )
    return (attended, grad_query, grad_key, grad_value)


def shards(patches, weights, cotangent, loss_mask):
    rows = patches.shape[1]
    width = patches.shape[2]
    inner = weights.shape[2]
    span = (WIN + rows - 2) // rows
    block_rows = min(512, rows)
    key_len = block_rows + span * rows
    group = HEADS
    group_cols = group * HSIZE
    inv_scale = 1.0 / math.sqrt(HSIZE)
    local_in = patches[0].astype(jnp.float32)
    inv_rms = lax.rsqrt(jnp.mean(local_in * local_in, axis=-1) + 1e-06)
    normed_full = local_in * inv_rms[:, None]
    normed = normed_full.astype(jnp.bfloat16)
    proj_weights = weights[:, :3, :]
    projected = jnp.einsum(
        "rd,dwh->wrh", normed, proj_weights, preferred_element_type=jnp.float32
    ).astype(jnp.bfloat16)
    queries = projected[0]
    key_vals = projected[1:]
    earlier = [shifted(key_vals, "tm", offset) for offset in range(span, 0, -1)]
    extended = jnp.concatenate(earlier + [key_vals], axis=1)
    local_count = jnp.sum(loss_mask.astype(jnp.int32))
    tokens_all = rows * lax.axis_size("tm") * lax.axis_size("night")
    local_cot = cotangent[0]
    grad_out = jnp.where(loss_mask[0][:, None] > 0, local_cot, jnp.zeros_like(local_cot))
    grad_attn = jnp.dot(grad_out, weights[:, 3, :], preferred_element_type=jnp.float32).astype(
        jnp.bfloat16
    )
    base = lax.axis_index("tm") * rows
    query_idx = jnp.arange(block_rows, dtype=jnp.int32)[:, None]
    key_idx = jnp.arange(key_len, dtype=jnp.int32)[None, :]
    offsets = query_idx - key_idx + span * rows
    band = (offsets >= 0) & (offsets < WIN)
    attended_cols = []
    grad_q_cols = []
    grad_kv_cols = []
    for first in range(0, inner, group_cols):
        accum = jnp.zeros((2, (span + 1) * rows, group_cols), jnp.float32)
        valid = (band & (key_idx >= span * rows - base - 0)).astype(jnp.float32)
        query_blk = queries[0:block_rows, first : first + group_cols].reshape(
            block_rows, group, HSIZE
        )
        kv_blk = extended[:, 0:key_len, first : first + group_cols].reshape(
            2, key_len, group, HSIZE
        )
        grad_blk = grad_attn[0:block_rows, first : first + group_cols].reshape(
            block_rows, group, HSIZE
        )
        attended, grad_query, grad_key, grad_value = band_block(
            query_blk, kv_blk[0], kv_blk[1], grad_blk, valid, inv_scale
        )
        attended_rows = attended.reshape(block_rows, group_cols)
        grad_q_rows = grad_query.reshape(block_rows, group_cols).astype(jnp.bfloat16)
        update = jnp.stack([grad_key, grad_value]).reshape(2, key_len, group_cols)
        accum = accum.at[:, 0:key_len].add(update)
        attended_cols.append(attended_rows)
        grad_q_cols.append(grad_q_rows)
        grad_kv_cols.append(accum)
    attended_all = jnp.concatenate(attended_cols, axis=1)
    grad_q = jnp.concatenate(grad_q_cols, axis=1)
    query_part = jnp.einsum("rd,rh->dh", normed, grad_q, preferred_element_type=jnp.float32)
    out_part = jnp.einsum("rd,rh->dh", grad_out, attended_all, preferred_element_type=jnp.float32)
    early, count = scatter_rows(
        jnp.stack([query_part, out_part], axis=1),
        local_count,
        ("tm", "night"),
        "tm",
        jnp.bfloat16,
        tail_first=True,
    )
    grad_kv_ext = jnp.concatenate(grad_kv_cols, axis=2)
    owned = grad_kv_ext[:, span * rows :]
    for offset in range(1, span + 1):
        lower = (span - offset) * rows
        owned = owned + shifted(
            grad_kv_ext[:, lower : lower + rows].astype(jnp.bfloat16), "tm", -offset
        ).astype(jnp.float32)
    grad_kv = owned.astype(jnp.bfloat16)
    grad_proj = jnp.concatenate([grad_q[None], grad_kv], axis=0)
    grad_normed = jnp.einsum(
        "wrh,dwh->rd", grad_proj, proj_weights, preferred_element_type=jnp.float32
    )
    along = jnp.sum(grad_normed * normed_full, axis=-1) / width
    unscaled_input = inv_rms[:, None] * (grad_normed - normed_full * along[:, None])
    key_value_part = jnp.einsum(
        "rd,wrh->dwh", normed, grad_kv, preferred_element_type=jnp.float32
    )
    late, _ = scatter_rows(key_value_part, None, ("tm", "night"), "tm", jnp.bfloat16)
    summed = jnp.concatenate([early[:, :1], late, early[:, 1:]], axis=1)
    total_count = count.astype(jnp.float32)
    loss_scale = jnp.float32(tokens_all) / total_count
    grad_input = (loss_scale * unscaled_input).astype(jnp.bfloat16)
    grad_weights = summed * (jnp.sqrt(jnp.float32(tokens_all)) / total_count)
    return (grad_input[None], grad_weights)


def solution(mesh):
    return jax.shard_map(
        shards,
        mesh=mesh,
        in_specs=(P("night", "tm", None), P(), P("night", "tm", None), P("night", "tm")),
        out_specs=(P("night", "tm", None), P(("tm", "night"), None, None)),
        check_vma=False,
    )
```

```python
import math

import jax
import jax.numpy as jnp
from jax import lax
from jax.sharding import PartitionSpec as P

HEADS = 8
HSIZE = 64
WIN = 1024


def shifted(value, axis, by):
    peers = lax.axis_size(axis)
    pairs = [(i, i + by) for i in range(peers) if 0 <= i + by < peers]
    return lax.ppermute(value, axis, pairs)


def is_power_of_two(n):
    return n > 0 and n & (n - 1) == 0


def halve(value, dim, axis, flip, send_type):
    peers = lax.axis_size(axis)
    bit = (lax.axis_index(axis) // flip) % 2
    keep = lax.dynamic_index_in_dim(value, bit, dim, keepdims=False)
    send = lax.dynamic_index_in_dim(value, 1 - bit, dim, keepdims=False)
    pairs = [(i, i ^ flip) for i in range(peers)]
    return keep + lax.ppermute(send.astype(send_type), axis, pairs).astype(keep.dtype)


def swap_add(value, anchor, axis, flip):
    value, anchor = lax.optimization_barrier((value, anchor))
    peers = lax.axis_size(axis)
    pairs = [(i, i ^ flip) for i in range(peers)]
    return value + lax.ppermute(value, axis, pairs), anchor


def scatter_rows(value, tally, axes, first_axis, wire_type, tail_first=False):
    sizes = [lax.axis_size(axis) for axis in axes]
    rows = value.shape[0]
    groups = math.prod(sizes)
    if not all(is_power_of_two(n) for n in sizes) or rows % groups:
        return (
            lax.psum_scatter(value, axes, scatter_dimension=0, tiled=True),
            None if tally is None else lax.psum(tally, axes),
        )
    stages = [
        (axis, 1 << (n.bit_length() - 2 - i))
        for axis, n in zip(axes, sizes)
        for i in range(n.bit_length() - 1)
    ]
    if not stages:
        return value, tally
    rest = value.shape[1:]
    value = value.reshape((2,) * len(stages) + (rows // groups,) + rest)
    names = list(stages)

    def step(part, part_names, stage, send_type):
        dim = part_names.index(stage)
        return halve(part, dim, *stage, send_type), part_names[:dim] + part_names[dim + 1 :]

    first = (first_axis, 1) if (first_axis, 1) in stages else stages[-1]
    def count_along(tally, anchor, stage):
        if tally is None:
            return tally, anchor
        return swap_add(tally, anchor, *stage)

    def run_tail(value, names, tally):
        for stage in tail:
            value, names = step(value, names, stage, wire_type)
            tally, value = count_along(tally, value, stage)
        return value, names, tally

    value, names = step(value, names, first, value.dtype)
    tally, value = count_along(tally, value, first)
    middle = [s for s in stages if s[0] == first[0] and s != first]
    tail = [s for s in stages if s[0] != first[0]][::-1]
    if tail_first:
        value, names, tally = run_tail(value, names, tally)
    if len(middle) > 1 and rest[-1] % 2 == 0:
        cut = rest[-1] // 2
        left, right = value[..., :cut], value[..., cut:]
        left_names, right_names = list(names), list(names)
        for a, b in zip(middle, middle[::-1]):
            left, left_names = step(left, left_names, a, wire_type)
            tally, left = count_along(tally, left, a)
            right, right_names = step(right, right_names, b, wire_type)
        value = jnp.concatenate([left, right], axis=-1)
        names = left_names
    else:
        for stage in middle:
            value, names = step(value, names, stage, wire_type)
            tally, value = count_along(tally, value, stage)
    if not tail_first:
        value, names, tally = run_tail(value, names, tally)
    return value, tally


def band_block(queries, keys_blk, values_blk, grad_attn, valid, inv_scale):
    scores = (
        jnp.einsum("qgc,kgc->gqk", queries, keys_blk, preferred_element_type=jnp.float32)
        * inv_scale
    )
    exp_terms = jnp.exp(scores) * valid[None]
    probs = exp_terms / jnp.sum(exp_terms, axis=-1, keepdims=True)
    probs_low = probs.astype(jnp.bfloat16)
    attended = jnp.einsum(
        "gqk,kgc->qgc", probs_low, values_blk, preferred_element_type=jnp.float32
    ).astype(jnp.bfloat16)
    delta = jnp.sum(grad_attn.astype(jnp.float32) * attended.astype(jnp.float32), axis=-1)
    grad_probs = jnp.einsum(
        "qgc,kgc->gqk", grad_attn, values_blk, preferred_element_type=jnp.float32
    )
    grad_scores = (probs * (grad_probs - jnp.transpose(delta)[:, :, None]) * inv_scale).astype(
        jnp.bfloat16
    )
    grad_query = jnp.einsum(
        "gqk,kgc->gcq", grad_scores, keys_blk, preferred_element_type=jnp.float32
    )
    grad_key = jnp.einsum("gqk,qgc->gck", grad_scores, queries, preferred_element_type=jnp.float32)
    grad_value = jnp.einsum(
        "gqk,qgc->gck", probs_low, grad_attn, preferred_element_type=jnp.float32
    )
    return (attended, grad_query, grad_key, grad_value)


def shards(patches, weights, cotangent, loss_mask):
    rows = patches.shape[1]
    width = patches.shape[2]
    inner = weights.shape[2]
    span = (WIN + rows - 2) // rows
    block_rows = min(512, rows)
    key_len = block_rows + span * rows
    group = HEADS
    group_cols = group * HSIZE
    inv_scale = 1.0 / math.sqrt(HSIZE)
    local_in = patches[0].astype(jnp.float32)
    inv_rms = lax.rsqrt(jnp.mean(local_in * local_in, axis=-1) + 1e-06)
    normed_full = local_in * inv_rms[:, None]
    normed = normed_full.astype(jnp.bfloat16)
    proj_weights = weights[:, :3, :]
    projected = jnp.einsum(
        "rd,dwh->wrh", normed, proj_weights, preferred_element_type=jnp.float32
    ).astype(jnp.bfloat16)
    queries = projected[0]
    key_vals = projected[1:]
    earlier = [shifted(key_vals, "tm", offset) for offset in range(span, 0, -1)]
    extended = jnp.concatenate(earlier + [key_vals], axis=1)
    local_count = jnp.sum(loss_mask.astype(jnp.int32))
    tokens_all = rows * lax.axis_size("tm") * lax.axis_size("night")
    local_cot = cotangent[0]
    grad_out = jnp.where(loss_mask[0][:, None] > 0, local_cot, jnp.zeros_like(local_cot))
    grad_attn = jnp.dot(grad_out, weights[:, 3, :], preferred_element_type=jnp.float32).astype(
        jnp.bfloat16
    )
    base = lax.axis_index("tm") * rows
    query_idx = jnp.arange(block_rows, dtype=jnp.int32)[:, None]
    key_idx = jnp.arange(key_len, dtype=jnp.int32)[None, :]
    offsets = query_idx - key_idx + span * rows
    band = (offsets >= 0) & (offsets < WIN)
    valid = (band & (key_idx >= span * rows - base)).astype(jnp.float32)
    attended, grad_query, grad_key, grad_value = band_block(
        queries.reshape(rows, HEADS, HSIZE),
        extended[0].reshape(key_len, HEADS, HSIZE),
        extended[1].reshape(key_len, HEADS, HSIZE),
        grad_attn.reshape(rows, HEADS, HSIZE),
        valid,
        inv_scale,
    )
    attended_all = attended.reshape(rows, inner)
    grad_q = grad_query.astype(jnp.bfloat16)
    query_part = jnp.einsum(
        "rd,gcr->dgc", normed, grad_q, preferred_element_type=jnp.float32
    ).reshape(width, inner)
    out_part = jnp.einsum("rd,rh->dh", grad_out, attended_all, preferred_element_type=jnp.float32)
    early, count = scatter_rows(
        jnp.stack([query_part, out_part], axis=1),
        local_count,
        ("tm", "night"),
        "tm",
        jnp.bfloat16,
        tail_first=True,
    )
    owned = jnp.stack([grad_key[..., span * rows :], grad_value[..., span * rows :]])
    for offset in range(1, span + 1):
        lower = (span - offset) * rows
        piece = jnp.stack(
            [grad_key[..., lower : lower + rows], grad_value[..., lower : lower + rows]]
        )
        owned = owned + shifted(piece.astype(jnp.bfloat16), "tm", -offset).astype(jnp.float32)
    grad_kv = owned.astype(jnp.bfloat16)
    grad_proj = jnp.concatenate([grad_q[None], grad_kv], axis=0)
    split_weights = proj_weights.reshape(width, 3, HEADS, HSIZE)
    grad_normed = jnp.einsum(
        "wgcr,dwgc->rd", grad_proj, split_weights, preferred_element_type=jnp.float32
    )
    along = jnp.sum(grad_normed * normed_full, axis=-1) / width
    unscaled_input = inv_rms[:, None] * (grad_normed - normed_full * along[:, None])
    key_value_part = jnp.einsum(
        "rd,wgcr->dwgc", normed, grad_kv, preferred_element_type=jnp.float32
    ).reshape(width, 2, inner)
    late, _ = scatter_rows(key_value_part, None, ("tm", "night"), "tm", jnp.bfloat16)
    summed = jnp.concatenate([early[:, :1], late, early[:, 1:]], axis=1)
    total_count = count.astype(jnp.float32)
    loss_scale = jnp.float32(tokens_all) / total_count
    grad_input = (loss_scale * unscaled_input).astype(jnp.bfloat16)
    grad_weights = summed * (jnp.sqrt(jnp.float32(tokens_all)) / total_count)
    return (grad_input[None], grad_weights)


def solution(mesh):
    return jax.shard_map(
        shards,
        mesh=mesh,
        in_specs=(P("night", "tm", None), P(), P("night", "tm", None), P("night", "tm")),
        out_specs=(P("night", "tm", None), P(("tm", "night"), None, None)),
        check_vma=False,
    )
```

```python
import math

import jax
import jax.numpy as jnp
from jax import lax
from jax.sharding import PartitionSpec as P

HEADS = 8
HSIZE = 64
WIN = 1024


def shifted(value, axis, by):
    peers = lax.axis_size(axis)
    pairs = [(i, i + by) for i in range(peers) if 0 <= i + by < peers]
    return lax.ppermute(value, axis, pairs)


def is_power_of_two(n):
    return n > 0 and n & (n - 1) == 0


def halve(value, dim, axis, flip, send_type):
    peers = lax.axis_size(axis)
    bit = (lax.axis_index(axis) // flip) % 2
    keep = lax.dynamic_index_in_dim(value, bit, dim, keepdims=False)
    send = lax.dynamic_index_in_dim(value, 1 - bit, dim, keepdims=False)
    pairs = [(i, i ^ flip) for i in range(peers)]
    return keep + lax.ppermute(send.astype(send_type), axis, pairs).astype(keep.dtype)


def swap_add(value, anchor, axis, flip):
    value, anchor = lax.optimization_barrier((value, anchor))
    peers = lax.axis_size(axis)
    pairs = [(i, i ^ flip) for i in range(peers)]
    return value + lax.ppermute(value, axis, pairs), anchor


def scatter_rows(value, tally, axes, first_axis, wire_type, tail_first=False):
    sizes = [lax.axis_size(axis) for axis in axes]
    rows = value.shape[0]
    groups = math.prod(sizes)
    if not all(is_power_of_two(n) for n in sizes) or rows % groups:
        return (
            lax.psum_scatter(value, axes, scatter_dimension=0, tiled=True),
            None if tally is None else lax.psum(tally, axes),
        )
    stages = [
        (axis, 1 << (n.bit_length() - 2 - i))
        for axis, n in zip(axes, sizes)
        for i in range(n.bit_length() - 1)
    ]
    if not stages:
        return value, tally
    rest = value.shape[1:]
    value = value.reshape((2,) * len(stages) + (rows // groups,) + rest)
    names = list(stages)

    def step(part, part_names, stage, send_type):
        dim = part_names.index(stage)
        return halve(part, dim, *stage, send_type), part_names[:dim] + part_names[dim + 1 :]

    first = (first_axis, 1) if (first_axis, 1) in stages else stages[-1]
    def count_along(tally, anchor, stage):
        if tally is None:
            return tally, anchor
        return swap_add(tally, anchor, *stage)

    def run_tail(value, names, tally):
        for stage in tail:
            value, names = step(value, names, stage, wire_type)
            tally, value = count_along(tally, value, stage)
        return value, names, tally

    value, names = step(value, names, first, value.dtype)
    tally, value = count_along(tally, value, first)
    middle = [s for s in stages if s[0] == first[0] and s != first]
    tail = [s for s in stages if s[0] != first[0]][::-1]
    if tail_first:
        value, names, tally = run_tail(value, names, tally)
    if len(middle) > 1 and rest[-1] % 2 == 0:
        cut = rest[-1] // 2
        left, right = value[..., :cut], value[..., cut:]
        left_names, right_names = list(names), list(names)
        for a, b in zip(middle, middle[::-1]):
            left, left_names = step(left, left_names, a, wire_type)
            tally, left = count_along(tally, left, a)
            right, right_names = step(right, right_names, b, wire_type)
        value = jnp.concatenate([left, right], axis=-1)
        names = left_names
    else:
        for stage in middle:
            value, names = step(value, names, stage, wire_type)
            tally, value = count_along(tally, value, stage)
    if not tail_first:
        value, names, tally = run_tail(value, names, tally)
    return value, tally


def band_block(queries, keys_blk, values_blk, grad_attn, valid, inv_scale):
    scores = (
        jnp.einsum("qgc,kgc->gqk", queries, keys_blk, preferred_element_type=jnp.float32)
        * inv_scale
    )
    exp_terms = jnp.exp(scores) * valid[None]
    probs = exp_terms / jnp.sum(exp_terms, axis=-1, keepdims=True)
    probs_low = probs.astype(jnp.bfloat16)
    attended = jnp.einsum(
        "gqk,kgc->qgc", probs_low, values_blk, preferred_element_type=jnp.float32
    ).astype(jnp.bfloat16)
    delta = jnp.sum(grad_attn.astype(jnp.float32) * attended.astype(jnp.float32), axis=-1)
    grad_probs = jnp.einsum(
        "qgc,kgc->gqk", grad_attn, values_blk, preferred_element_type=jnp.float32
    )
    grad_scores = (probs * (grad_probs - jnp.transpose(delta)[:, :, None]) * inv_scale).astype(
        jnp.bfloat16
    )
    grad_query = jnp.einsum(
        "gqk,kgc->gcq", grad_scores, keys_blk, preferred_element_type=jnp.float32
    )
    grad_key = jnp.einsum("gqk,qgc->gck", grad_scores, queries, preferred_element_type=jnp.float32)
    grad_value = jnp.einsum(
        "gqk,qgc->gck", probs_low, grad_attn, preferred_element_type=jnp.float32
    )
    return (attended, grad_query, grad_key, grad_value)


def shards(patches, weights, cotangent, loss_mask):
    rows = patches.shape[1]
    width = patches.shape[2]
    inner = weights.shape[2]
    span = (WIN + rows - 2) // rows
    block_rows = min(512, rows)
    key_len = block_rows + span * rows
    group = HEADS
    group_cols = group * HSIZE
    inv_scale = 1.0 / math.sqrt(HSIZE)
    local_in = patches[0].astype(jnp.float32)
    inv_rms = lax.rsqrt(jnp.mean(local_in * local_in, axis=-1) + 1e-06)
    normed_full = local_in * inv_rms[:, None]
    normed = normed_full.astype(jnp.bfloat16)
    projected = jnp.einsum(
        "rd,dwh->wrh", normed, weights, preferred_element_type=jnp.float32
    ).astype(jnp.bfloat16)
    queries = projected[0]
    key_vals = projected[1:3]
    earlier = [shifted(key_vals, "tm", offset) for offset in range(span, 0, -1)]
    extended = jnp.concatenate(earlier + [key_vals], axis=1)
    local_count = jnp.sum(loss_mask.astype(jnp.int32))
    tokens_all = rows * lax.axis_size("tm") * lax.axis_size("night")
    local_cot = cotangent[0]
    grad_out = jnp.where(loss_mask[0][:, None] > 0, local_cot, jnp.zeros_like(local_cot))
    grad_attn = jnp.einsum(
        "rd,dwh->wrh", grad_out, weights, preferred_element_type=jnp.float32
    )[3].astype(jnp.bfloat16)
    base = lax.axis_index("tm") * rows
    query_idx = jnp.arange(block_rows, dtype=jnp.int32)[:, None]
    key_idx = jnp.arange(key_len, dtype=jnp.int32)[None, :]
    offsets = query_idx - key_idx + span * rows
    band = (offsets >= 0) & (offsets < WIN)
    valid = (band & (key_idx >= span * rows - base)).astype(jnp.float32)
    attended, grad_query, grad_key, grad_value = band_block(
        queries.reshape(rows, HEADS, HSIZE),
        extended[0].reshape(key_len, HEADS, HSIZE),
        extended[1].reshape(key_len, HEADS, HSIZE),
        grad_attn.reshape(rows, HEADS, HSIZE),
        valid,
        inv_scale,
    )
    attended_all = attended.reshape(rows, inner)
    grad_q = grad_query.astype(jnp.bfloat16)
    query_part = jnp.einsum(
        "rd,gcr->dgc", normed, grad_q, preferred_element_type=jnp.float32
    ).reshape(width, inner)
    out_part = jnp.einsum("rd,rh->dh", grad_out, attended_all, preferred_element_type=jnp.float32)
    early, count = scatter_rows(
        jnp.stack([query_part, out_part], axis=1),
        local_count,
        ("tm", "night"),
        "tm",
        jnp.bfloat16,
        tail_first=True,
    )
    owned = jnp.stack([grad_key[..., span * rows :], grad_value[..., span * rows :]])
    for offset in range(1, span + 1):
        lower = (span - offset) * rows
        piece = jnp.stack(
            [grad_key[..., lower : lower + rows], grad_value[..., lower : lower + rows]]
        )
        owned = owned + shifted(piece.astype(jnp.bfloat16), "tm", -offset).astype(jnp.float32)
    grad_kv = owned.astype(jnp.bfloat16)
    grad_proj = jnp.concatenate([grad_q[None], grad_kv, jnp.zeros_like(grad_q)[None]], axis=0)
    split_weights = weights.reshape(width, weights.shape[1], HEADS, HSIZE)
    grad_normed = jnp.einsum(
        "wgcr,dwgc->rd", grad_proj, split_weights, preferred_element_type=jnp.float32
    )
    along = jnp.sum(grad_normed * normed_full, axis=-1) / width
    unscaled_input = inv_rms[:, None] * (grad_normed - normed_full * along[:, None])
    key_value_part = jnp.einsum(
        "rd,wgcr->dwgc", normed, grad_proj[1:3], preferred_element_type=jnp.float32
    ).reshape(width, 2, inner)
    late, _ = scatter_rows(key_value_part, None, ("tm", "night"), "tm", jnp.bfloat16)
    summed = jnp.concatenate([early[:, :1], late, early[:, 1:]], axis=1)
    total_count = count.astype(jnp.float32)
    loss_scale = jnp.float32(tokens_all) / total_count
    grad_input = (loss_scale * unscaled_input).astype(jnp.bfloat16)
    grad_weights = summed * (jnp.sqrt(jnp.float32(tokens_all)) / total_count)
    return (grad_input[None], grad_weights)


def solution(mesh):
    return jax.shard_map(
        shards,
        mesh=mesh,
        in_specs=(P("night", "tm", None), P(), P("night", "tm", None), P("night", "tm")),
        out_specs=(P("night", "tm", None), P(("tm", "night"), None, None)),
        check_vma=False,
    )
```

```python
import math

import jax
import jax.numpy as jnp
from jax import lax
from jax.sharding import PartitionSpec as P

HEADS = 8
HSIZE = 64
WIN = 1024


def shifted(value, axis, by):
    peers = lax.axis_size(axis)
    pairs = [(i, i + by) for i in range(peers) if 0 <= i + by < peers]
    return lax.ppermute(value, axis, pairs)


def is_power_of_two(n):
    return n > 0 and n & (n - 1) == 0


def halve(value, dim, axis, flip, send_type):
    peers = lax.axis_size(axis)
    bit = (lax.axis_index(axis) // flip) % 2
    keep = lax.dynamic_index_in_dim(value, bit, dim, keepdims=False)
    send = lax.dynamic_index_in_dim(value, 1 - bit, dim, keepdims=False)
    pairs = [(i, i ^ flip) for i in range(peers)]
    return keep + lax.ppermute(send.astype(send_type), axis, pairs).astype(keep.dtype)


def swap_add(value, anchor, axis, flip):
    value, anchor = lax.optimization_barrier((value, anchor))
    peers = lax.axis_size(axis)
    pairs = [(i, i ^ flip) for i in range(peers)]
    return value + lax.ppermute(value, axis, pairs), anchor


def scatter_rows(value, tally, axes, first_axis, wire_type, tail_first=False):
    sizes = [lax.axis_size(axis) for axis in axes]
    rows = value.shape[0]
    groups = math.prod(sizes)
    if not all(is_power_of_two(n) for n in sizes) or rows % groups:
        return (
            lax.psum_scatter(value, axes, scatter_dimension=0, tiled=True),
            None if tally is None else lax.psum(tally, axes),
        )
    stages = [
        (axis, 1 << (n.bit_length() - 2 - i))
        for axis, n in zip(axes, sizes)
        for i in range(n.bit_length() - 1)
    ]
    if not stages:
        return value, tally
    rest = value.shape[1:]
    value = value.reshape((2,) * len(stages) + (rows // groups,) + rest)
    names = list(stages)

    def step(part, part_names, stage, send_type):
        dim = part_names.index(stage)
        return halve(part, dim, *stage, send_type), part_names[:dim] + part_names[dim + 1 :]

    first = (first_axis, 1) if (first_axis, 1) in stages else stages[-1]
    def count_along(tally, anchor, stage):
        if tally is None:
            return tally, anchor
        return swap_add(tally, anchor, *stage)

    def run_tail(value, names, tally):
        for stage in tail:
            value, names = step(value, names, stage, wire_type)
            tally, value = count_along(tally, value, stage)
        return value, names, tally

    value, names = step(value, names, first, value.dtype)
    tally, value = count_along(tally, value, first)
    middle = [s for s in stages if s[0] == first[0] and s != first]
    tail = [s for s in stages if s[0] != first[0]][::-1]
    if tail_first:
        value, names, tally = run_tail(value, names, tally)
    if len(middle) > 1 and rest[-1] % 2 == 0:
        cut = rest[-1] // 2
        left, right = value[..., :cut], value[..., cut:]
        left_names, right_names = list(names), list(names)
        for a, b in zip(middle, middle[::-1]):
            left, left_names = step(left, left_names, a, wire_type)
            tally, left = count_along(tally, left, a)
            right, right_names = step(right, right_names, b, wire_type)
        value = jnp.concatenate([left, right], axis=-1)
        names = left_names
    else:
        for stage in middle:
            value, names = step(value, names, stage, wire_type)
            tally, value = count_along(tally, value, stage)
    if not tail_first:
        value, names, tally = run_tail(value, names, tally)
    return value, tally


def band_block(queries, keys_blk, values_blk, grad_attn, valid, inv_scale):
    scores = (
        jnp.einsum("qgc,kgc->gqk", queries, keys_blk, preferred_element_type=jnp.float32)
        * inv_scale
    )
    exp_terms = jnp.exp(scores) * valid[None]
    probs = exp_terms / jnp.sum(exp_terms, axis=-1, keepdims=True)
    probs_low = probs.astype(jnp.bfloat16)
    attended = jnp.einsum(
        "gqk,kgc->qgc", probs_low, values_blk, preferred_element_type=jnp.float32
    ).astype(jnp.bfloat16)
    delta = jnp.sum(grad_attn.astype(jnp.float32) * attended.astype(jnp.float32), axis=-1)
    grad_probs = jnp.einsum(
        "qgc,kgc->gqk", grad_attn, values_blk, preferred_element_type=jnp.float32
    )
    grad_scores = (probs * (grad_probs - jnp.transpose(delta)[:, :, None]) * inv_scale).astype(
        jnp.bfloat16
    )
    grad_query = jnp.einsum(
        "gqk,kgc->gcq", grad_scores, keys_blk, preferred_element_type=jnp.float32
    )
    grad_key = jnp.einsum("gqk,qgc->gck", grad_scores, queries, preferred_element_type=jnp.float32)
    grad_value = jnp.einsum(
        "gqk,qgc->gck", probs_low, grad_attn, preferred_element_type=jnp.float32
    )
    return (attended, grad_query, grad_key, grad_value)


def shards(patches, weights, cotangent, loss_mask):
    rows = patches.shape[1]
    width = patches.shape[2]
    inner = weights.shape[2]
    span = (WIN + rows - 2) // rows
    block_rows = min(512, rows)
    key_len = block_rows + span * rows
    group = HEADS
    group_cols = group * HSIZE
    inv_scale = 1.0 / math.sqrt(HSIZE)
    local_in = patches[0].astype(jnp.float32)
    inv_rms = lax.rsqrt(jnp.mean(local_in * local_in, axis=-1) + 1e-06)
    normed_full = local_in * inv_rms[:, None]
    normed = normed_full.astype(jnp.bfloat16)
    projected = jnp.einsum(
        "rd,dwh->wrh", normed, weights, preferred_element_type=jnp.float32
    ).astype(jnp.bfloat16)
    queries = projected[0]
    key_vals = projected[1:3]
    earlier = [shifted(key_vals, "tm", offset) for offset in range(span, 0, -1)]
    extended = jnp.concatenate(earlier + [key_vals], axis=1)
    local_count = jnp.sum(loss_mask.astype(jnp.int32))
    tokens_all = rows * lax.axis_size("tm") * lax.axis_size("night")
    local_cot = cotangent[0]
    grad_out = jnp.where(loss_mask[0][:, None] > 0, local_cot, jnp.zeros_like(local_cot))
    grad_attn = jnp.einsum(
        "rd,dwh->wrh", grad_out, weights, preferred_element_type=jnp.float32
    )[3].astype(jnp.bfloat16)
    base = lax.axis_index("tm") * rows
    query_idx = jnp.arange(block_rows, dtype=jnp.int32)[:, None]
    key_idx = jnp.arange(key_len, dtype=jnp.int32)[None, :]
    offsets = query_idx - key_idx + span * rows
    band = (offsets >= 0) & (offsets < WIN)
    valid = (band & (key_idx >= span * rows - base)).astype(jnp.float32)
    attended, grad_query, grad_key, grad_value = band_block(
        queries.reshape(rows, HEADS, HSIZE),
        extended[0].reshape(key_len, HEADS, HSIZE),
        extended[1].reshape(key_len, HEADS, HSIZE),
        grad_attn.reshape(rows, HEADS, HSIZE),
        valid,
        inv_scale,
    )
    attended_all = attended.reshape(rows, inner)
    grad_q = grad_query.astype(jnp.bfloat16)
    query_part = jnp.einsum(
        "rd,gcr->dgc", normed, grad_q, preferred_element_type=jnp.float32
    ).reshape(width, inner)
    out_part = jnp.einsum("rd,rh->dh", grad_out, attended_all, preferred_element_type=jnp.float32)
    early, count = scatter_rows(
        jnp.stack([query_part, out_part], axis=1),
        local_count,
        ("tm", "night"),
        "tm",
        jnp.bfloat16,
        tail_first=True,
    )
    owned = jnp.stack([grad_key[..., span * rows :], grad_value[..., span * rows :]])
    for offset in range(1, span + 1):
        lower = (span - offset) * rows
        piece = jnp.stack(
            [grad_key[..., lower : lower + rows], grad_value[..., lower : lower + rows]]
        )
        owned = owned + shifted(piece.astype(jnp.bfloat16), "tm", -offset).astype(jnp.float32)
    grad_kv = owned.astype(jnp.bfloat16)
    grad_proj = jnp.concatenate([grad_q[None], grad_kv, jnp.zeros_like(grad_q)[None]], axis=0)
    grad_rows = grad_proj.transpose(0, 3, 1, 2).reshape(grad_proj.shape[0], rows, inner)
    grad_normed = jnp.einsum(
        "wrh,dwh->rd", grad_rows, weights, preferred_element_type=jnp.float32
    )
    along = jnp.sum(grad_normed * normed_full, axis=-1) / width
    unscaled_input = inv_rms[:, None] * (grad_normed - normed_full * along[:, None])
    key_value_part = jnp.einsum(
        "rd,wgcr->dwgc", normed, grad_proj[1:3], preferred_element_type=jnp.float32
    ).reshape(width, 2, inner)
    late, _ = scatter_rows(key_value_part, None, ("tm", "night"), "tm", jnp.bfloat16)
    summed = jnp.concatenate([early[:, :1], late, early[:, 1:]], axis=1)
    total_count = count.astype(jnp.float32)
    loss_scale = jnp.float32(tokens_all) / total_count
    grad_input = (loss_scale * unscaled_input).astype(jnp.bfloat16)
    grad_weights = summed * (jnp.sqrt(jnp.float32(tokens_all)) / total_count)
    return (grad_input[None], grad_weights)


def solution(mesh):
    return jax.shard_map(
        shards,
        mesh=mesh,
        in_specs=(P("night", "tm", None), P(), P("night", "tm", None), P("night", "tm")),
        out_specs=(P("night", "tm", None), P(("tm", "night"), None, None)),
        check_vma=False,
    )
```

```python
import math

import jax
import jax.numpy as jnp
from jax import lax
from jax.sharding import PartitionSpec as P

HEADS = 8
HSIZE = 64
WIN = 1024


def shifted(value, axis, by):
    peers = lax.axis_size(axis)
    pairs = [(i, i + by) for i in range(peers) if 0 <= i + by < peers]
    return lax.ppermute(value, axis, pairs)


def is_power_of_two(n):
    return n > 0 and n & (n - 1) == 0


def halve(value, dim, axis, flip, send_type):
    peers = lax.axis_size(axis)
    bit = (lax.axis_index(axis) // flip) % 2
    keep = lax.dynamic_index_in_dim(value, bit, dim, keepdims=False)
    send = lax.dynamic_index_in_dim(value, 1 - bit, dim, keepdims=False)
    pairs = [(i, i ^ flip) for i in range(peers)]
    return keep + lax.ppermute(send.astype(send_type), axis, pairs).astype(keep.dtype)


def swap_add(value, anchor, axis, flip):
    value, anchor = lax.optimization_barrier((value, anchor))
    peers = lax.axis_size(axis)
    pairs = [(i, i ^ flip) for i in range(peers)]
    return value + lax.ppermute(value, axis, pairs), anchor


def scatter_rows(value, tally, axes, first_axis, wire_type, tail_first=False, balance=True):
    sizes = [lax.axis_size(axis) for axis in axes]
    rows = value.shape[0]
    groups = math.prod(sizes)
    if not all(is_power_of_two(n) for n in sizes) or rows % groups:
        return (
            lax.psum_scatter(value, axes, scatter_dimension=0, tiled=True),
            None if tally is None else lax.psum(tally, axes),
        )
    stages = [
        (axis, 1 << (n.bit_length() - 2 - i))
        for axis, n in zip(axes, sizes)
        for i in range(n.bit_length() - 1)
    ]
    if not stages:
        return value, tally
    rest = value.shape[1:]
    value = value.reshape((2,) * len(stages) + (rows // groups,) + rest)
    names = list(stages)

    def step(part, part_names, stage, send_type):
        dim = part_names.index(stage)
        return halve(part, dim, *stage, send_type), part_names[:dim] + part_names[dim + 1 :]

    first = (first_axis, 1) if (first_axis, 1) in stages else stages[-1]
    def count_along(tally, anchor, stage):
        if tally is None:
            return tally, anchor
        return swap_add(tally, anchor, *stage)

    def run_tail(value, names, tally):
        for stage in tail:
            value, names = step(value, names, stage, wire_type)
            tally, value = count_along(tally, value, stage)
        return value, names, tally

    value, names = step(value, names, first, value.dtype)
    tally, value = count_along(tally, value, first)
    middle = [s for s in stages if s[0] == first[0] and s != first]
    tail = [s for s in stages if s[0] != first[0]][::-1]
    if tail_first:
        value, names, tally = run_tail(value, names, tally)
    if balance and len(middle) > 1 and rest[-1] % 2 == 0:
        cut = rest[-1] // 2
        left, right = value[..., :cut], value[..., cut:]
        left_names, right_names = list(names), list(names)
        for a, b in zip(middle, middle[::-1]):
            left, left_names = step(left, left_names, a, wire_type)
            tally, left = count_along(tally, left, a)
            right, right_names = step(right, right_names, b, wire_type)
        value = jnp.concatenate([left, right], axis=-1)
        names = left_names
    else:
        for stage in middle:
            value, names = step(value, names, stage, wire_type)
            tally, value = count_along(tally, value, stage)
    if not tail_first:
        value, names, tally = run_tail(value, names, tally)
    return value, tally


def band_block(queries, keys_blk, values_blk, grad_attn, valid, inv_scale):
    scores = (
        jnp.einsum("qgc,kgc->gqk", queries, keys_blk, preferred_element_type=jnp.float32)
        * inv_scale
    )
    exp_terms = jnp.exp(scores) * valid[None]
    probs = exp_terms / jnp.sum(exp_terms, axis=-1, keepdims=True)
    probs_low = probs.astype(jnp.bfloat16)
    attended = jnp.einsum(
        "gqk,kgc->qgc", probs_low, values_blk, preferred_element_type=jnp.float32
    ).astype(jnp.bfloat16)
    delta = jnp.sum(grad_attn.astype(jnp.float32) * attended.astype(jnp.float32), axis=-1)
    grad_probs = jnp.einsum(
        "qgc,kgc->gqk", grad_attn, values_blk, preferred_element_type=jnp.float32
    )
    grad_scores = (probs * (grad_probs - jnp.transpose(delta)[:, :, None]) * inv_scale).astype(
        jnp.bfloat16
    )
    grad_query = jnp.einsum(
        "gqk,kgc->gcq", grad_scores, keys_blk, preferred_element_type=jnp.float32
    )
    grad_key = jnp.einsum("gqk,qgc->gck", grad_scores, queries, preferred_element_type=jnp.float32)
    grad_value = jnp.einsum(
        "gqk,qgc->gck", probs_low, grad_attn, preferred_element_type=jnp.float32
    )
    return (attended, grad_query, grad_key, grad_value)


def shards(patches, weights, cotangent, loss_mask):
    rows = patches.shape[1]
    width = patches.shape[2]
    inner = weights.shape[2]
    span = (WIN + rows - 2) // rows
    block_rows = min(512, rows)
    key_len = block_rows + span * rows
    group = HEADS
    group_cols = group * HSIZE
    inv_scale = 1.0 / math.sqrt(HSIZE)
    local_in = patches[0].astype(jnp.float32)
    inv_rms = lax.rsqrt(jnp.mean(local_in * local_in, axis=-1) + 1e-06)
    normed_full = local_in * inv_rms[:, None]
    normed = normed_full.astype(jnp.bfloat16)
    projected = jnp.einsum(
        "rd,dwh->wrh", normed, weights, preferred_element_type=jnp.float32
    ).astype(jnp.bfloat16)
    queries = projected[0]
    key_vals = projected[1:3]
    earlier = [shifted(key_vals, "tm", offset) for offset in range(span, 0, -1)]
    extended = jnp.concatenate(earlier + [key_vals], axis=1)
    local_count = jnp.sum(loss_mask.astype(jnp.int32))
    tokens_all = rows * lax.axis_size("tm") * lax.axis_size("night")
    local_cot = cotangent[0]
    grad_out = jnp.where(loss_mask[0][:, None] > 0, local_cot, jnp.zeros_like(local_cot))
    grad_attn = jnp.einsum(
        "rd,dwh->wrh", grad_out, weights, preferred_element_type=jnp.float32
    )[3].astype(jnp.bfloat16)
    base = lax.axis_index("tm") * rows
    query_idx = jnp.arange(block_rows, dtype=jnp.int32)[:, None]
    key_idx = jnp.arange(key_len, dtype=jnp.int32)[None, :]
    offsets = query_idx - key_idx + span * rows
    band = (offsets >= 0) & (offsets < WIN)
    valid = (band & (key_idx >= span * rows - base)).astype(jnp.float32)
    attended, grad_query, grad_key, grad_value = band_block(
        queries.reshape(rows, HEADS, HSIZE),
        extended[0].reshape(key_len, HEADS, HSIZE),
        extended[1].reshape(key_len, HEADS, HSIZE),
        grad_attn.reshape(rows, HEADS, HSIZE),
        valid,
        inv_scale,
    )
    attended_all = attended.reshape(rows, inner)
    grad_q = grad_query.astype(jnp.bfloat16)
    query_part = jnp.einsum(
        "rd,gcr->dgc", normed, grad_q, preferred_element_type=jnp.float32
    ).reshape(width, inner)
    out_part = jnp.einsum("rd,rh->dh", grad_out, attended_all, preferred_element_type=jnp.float32)
    early, count = scatter_rows(
        jnp.stack([query_part, out_part], axis=1),
        local_count,
        ("tm", "night"),
        "tm",
        jnp.bfloat16,
        tail_first=True,
        balance=False,
    )
    owned = jnp.stack([grad_key[..., span * rows :], grad_value[..., span * rows :]])
    for offset in range(1, span + 1):
        lower = (span - offset) * rows
        piece = jnp.stack(
            [grad_key[..., lower : lower + rows], grad_value[..., lower : lower + rows]]
        )
        owned = owned + shifted(piece.astype(jnp.bfloat16), "tm", -offset).astype(jnp.float32)
    grad_kv = owned.astype(jnp.bfloat16)
    grad_proj = jnp.concatenate([grad_q[None], grad_kv, jnp.zeros_like(grad_q)[None]], axis=0)
    grad_rows = grad_proj.transpose(0, 3, 1, 2).reshape(grad_proj.shape[0], rows, inner)
    grad_normed = jnp.einsum(
        "wrh,dwh->rd", grad_rows, weights, preferred_element_type=jnp.float32
    )
    along = jnp.sum(grad_normed * normed_full, axis=-1) / width
    unscaled_input = inv_rms[:, None] * (grad_normed - normed_full * along[:, None])
    key_value_part = jnp.einsum(
        "rd,wgcr->dwgc", normed, grad_proj[1:3], preferred_element_type=jnp.float32
    ).reshape(width, 2, inner)
    late, _ = scatter_rows(key_value_part, None, ("tm", "night"), "tm", jnp.bfloat16)
    summed = jnp.concatenate([early[:, :1], late, early[:, 1:]], axis=1)
    total_count = count.astype(jnp.float32)
    loss_scale = jnp.float32(tokens_all) / total_count
    grad_input = (loss_scale * unscaled_input).astype(jnp.bfloat16)
    grad_weights = summed * (jnp.sqrt(jnp.float32(tokens_all)) / total_count)
    return (grad_input[None], grad_weights)


def solution(mesh):
    return jax.shard_map(
        shards,
        mesh=mesh,
        in_specs=(P("night", "tm", None), P(), P("night", "tm", None), P("night", "tm")),
        out_specs=(P("night", "tm", None), P(("tm", "night"), None, None)),
        check_vma=False,
    )
```

```python
import math

import jax
import jax.numpy as jnp
from jax import lax
from jax.sharding import PartitionSpec as P

HEADS = 8
HSIZE = 64
WIN = 1024


def shifted(value, axis, by):
    peers = lax.axis_size(axis)
    pairs = [(i, i + by) for i in range(peers) if 0 <= i + by < peers]
    return lax.ppermute(value, axis, pairs)


def is_power_of_two(n):
    return n > 0 and n & (n - 1) == 0


def halve(value, dim, axis, flip, send_type):
    peers = lax.axis_size(axis)
    bit = (lax.axis_index(axis) // flip) % 2
    keep = lax.dynamic_index_in_dim(value, bit, dim, keepdims=False)
    send = lax.dynamic_index_in_dim(value, 1 - bit, dim, keepdims=False)
    pairs = [(i, i ^ flip) for i in range(peers)]
    return keep + lax.ppermute(send.astype(send_type), axis, pairs).astype(keep.dtype)


def exchange_all(value, dims, axis, flips, send_type):
    peers = lax.axis_size(axis)
    me = lax.axis_index(axis)
    count = len(flips)
    code = sum(((me // f) % 2) * (1 << (count - 1 - j)) for j, f in enumerate(flips))
    lead = value.shape[:count]
    merged = value.reshape((math.prod(lead),) + value.shape[count:])
    total = lax.dynamic_index_in_dim(merged, code, 0, keepdims=False)
    for m in range(1, 1 << count):
        mask = sum(f for j, f in enumerate(flips) if (m >> (count - 1 - j)) & 1)
        send = lax.dynamic_index_in_dim(merged, code ^ m, 0, keepdims=False)
        pairs = [(i, i ^ mask) for i in range(peers)]
        total = total + lax.ppermute(send.astype(send_type), axis, pairs).astype(total.dtype)
    return total


def swap_add(value, anchor, axis, flip):
    value, anchor = lax.optimization_barrier((value, anchor))
    peers = lax.axis_size(axis)
    pairs = [(i, i ^ flip) for i in range(peers)]
    return value + lax.ppermute(value, axis, pairs), anchor


def scatter_rows(value, tally, axes, first_axis, wire_type, tail_first=False, direct=True):
    sizes = [lax.axis_size(axis) for axis in axes]
    rows = value.shape[0]
    groups = math.prod(sizes)
    if not all(is_power_of_two(n) for n in sizes) or rows % groups:
        return (
            lax.psum_scatter(value, axes, scatter_dimension=0, tiled=True),
            None if tally is None else lax.psum(tally, axes),
        )
    stages = [
        (axis, 1 << (n.bit_length() - 2 - i))
        for axis, n in zip(axes, sizes)
        for i in range(n.bit_length() - 1)
    ]
    if not stages:
        return value, tally
    rest = value.shape[1:]
    value = value.reshape((2,) * len(stages) + (rows // groups,) + rest)
    names = list(stages)

    def step(part, part_names, stage, send_type):
        dim = part_names.index(stage)
        return halve(part, dim, *stage, send_type), part_names[:dim] + part_names[dim + 1 :]

    first = (first_axis, 1) if (first_axis, 1) in stages else stages[-1]
    def count_along(tally, anchor, stage):
        if tally is None:
            return tally, anchor
        return swap_add(tally, anchor, *stage)

    def run_group(value, names, tally, group):
        dim = names.index(group[0])
        assert names[dim : dim + len(group)] == list(group)
        moved = jnp.moveaxis(value, list(range(dim, dim + len(group))), list(range(len(group))))
        value = exchange_all(moved, None, group[0][0], [s[1] for s in group], wire_type)
        names = names[:dim] + names[dim + len(group) :]
        for stage in group:
            tally, value = count_along(tally, value, stage)
        return value, names, tally

    def run_tail(value, names, tally):
        if direct and len(tail) > 1:
            return run_group(value, names, tally, sorted(tail, key=names.index))
        for stage in tail:
            value, names = step(value, names, stage, wire_type)
            tally, value = count_along(tally, value, stage)
        return value, names, tally

    value, names = step(value, names, first, value.dtype)
    tally, value = count_along(tally, value, first)
    middle = [s for s in stages if s[0] == first[0] and s != first]
    tail = [s for s in stages if s[0] != first[0]][::-1]
    if tail_first:
        value, names, tally = run_tail(value, names, tally)
    if direct and len(middle) > 1:
        value, names, tally = run_group(value, names, tally, sorted(middle, key=names.index))
    elif len(middle) > 1 and rest[-1] % 2 == 0:
        cut = rest[-1] // 2
        left, right = value[..., :cut], value[..., cut:]
        left_names, right_names = list(names), list(names)
        for a, b in zip(middle, middle[::-1]):
            left, left_names = step(left, left_names, a, wire_type)
            tally, left = count_along(tally, left, a)
            right, right_names = step(right, right_names, b, wire_type)
        value = jnp.concatenate([left, right], axis=-1)
        names = left_names
    else:
        for stage in middle:
            value, names = step(value, names, stage, wire_type)
            tally, value = count_along(tally, value, stage)
    if not tail_first:
        value, names, tally = run_tail(value, names, tally)
    return value, tally


def band_block(queries, keys_blk, values_blk, grad_attn, valid, inv_scale):
    scores = (
        jnp.einsum("qgc,kgc->gqk", queries, keys_blk, preferred_element_type=jnp.float32)
        * inv_scale
    )
    exp_terms = jnp.exp(scores) * valid[None]
    probs = exp_terms / jnp.sum(exp_terms, axis=-1, keepdims=True)
    probs_low = probs.astype(jnp.bfloat16)
    attended = jnp.einsum(
        "gqk,kgc->qgc", probs_low, values_blk, preferred_element_type=jnp.float32
    ).astype(jnp.bfloat16)
    delta = jnp.sum(grad_attn.astype(jnp.float32) * attended.astype(jnp.float32), axis=-1)
    grad_probs = jnp.einsum(
        "qgc,kgc->gqk", grad_attn, values_blk, preferred_element_type=jnp.float32
    )
    grad_scores = (probs * (grad_probs - jnp.transpose(delta)[:, :, None]) * inv_scale).astype(
        jnp.bfloat16
    )
    grad_query = jnp.einsum(
        "gqk,kgc->gcq", grad_scores, keys_blk, preferred_element_type=jnp.float32
    )
    grad_key = jnp.einsum("gqk,qgc->gck", grad_scores, queries, preferred_element_type=jnp.float32)
    grad_value = jnp.einsum(
        "gqk,qgc->gck", probs_low, grad_attn, preferred_element_type=jnp.float32
    )
    return (attended, grad_query, grad_key, grad_value)


def shards(patches, weights, cotangent, loss_mask):
    rows = patches.shape[1]
    width = patches.shape[2]
    inner = weights.shape[2]
    span = (WIN + rows - 2) // rows
    block_rows = min(512, rows)
    key_len = block_rows + span * rows
    group = HEADS
    group_cols = group * HSIZE
    inv_scale = 1.0 / math.sqrt(HSIZE)
    local_in = patches[0].astype(jnp.float32)
    inv_rms = lax.rsqrt(jnp.mean(local_in * local_in, axis=-1) + 1e-06)
    normed_full = local_in * inv_rms[:, None]
    normed = normed_full.astype(jnp.bfloat16)
    projected = jnp.einsum(
        "rd,dwh->wrh", normed, weights, preferred_element_type=jnp.float32
    ).astype(jnp.bfloat16)
    queries = projected[0]
    key_vals = projected[1:3]
    earlier = [shifted(key_vals, "tm", offset) for offset in range(span, 0, -1)]
    extended = jnp.concatenate(earlier + [key_vals], axis=1)
    local_count = jnp.sum(loss_mask.astype(jnp.int32))
    tokens_all = rows * lax.axis_size("tm") * lax.axis_size("night")
    local_cot = cotangent[0]
    grad_out = jnp.where(loss_mask[0][:, None] > 0, local_cot, jnp.zeros_like(local_cot))
    grad_attn = jnp.einsum(
        "rd,dwh->wrh", grad_out, weights, preferred_element_type=jnp.float32
    )[3].astype(jnp.bfloat16)
    base = lax.axis_index("tm") * rows
    query_idx = jnp.arange(block_rows, dtype=jnp.int32)[:, None]
    key_idx = jnp.arange(key_len, dtype=jnp.int32)[None, :]
    offsets = query_idx - key_idx + span * rows
    band = (offsets >= 0) & (offsets < WIN)
    valid = (band & (key_idx >= span * rows - base)).astype(jnp.float32)
    attended, grad_query, grad_key, grad_value = band_block(
        queries.reshape(rows, HEADS, HSIZE),
        extended[0].reshape(key_len, HEADS, HSIZE),
        extended[1].reshape(key_len, HEADS, HSIZE),
        grad_attn.reshape(rows, HEADS, HSIZE),
        valid,
        inv_scale,
    )
    attended_all = attended.reshape(rows, inner)
    grad_q = grad_query.astype(jnp.bfloat16)
    query_part = jnp.einsum(
        "rd,gcr->dgc", normed, grad_q, preferred_element_type=jnp.float32
    ).reshape(width, inner)
    out_part = jnp.einsum("rd,rh->dh", grad_out, attended_all, preferred_element_type=jnp.float32)
    early, count = scatter_rows(
        jnp.stack([query_part, out_part], axis=1),
        local_count,
        ("tm", "night"),
        "tm",
        jnp.bfloat16,
        tail_first=True,
    )
    owned = jnp.stack([grad_key[..., span * rows :], grad_value[..., span * rows :]])
    for offset in range(1, span + 1):
        lower = (span - offset) * rows
        piece = jnp.stack(
            [grad_key[..., lower : lower + rows], grad_value[..., lower : lower + rows]]
        )
        owned = owned + shifted(piece.astype(jnp.bfloat16), "tm", -offset).astype(jnp.float32)
    grad_kv = owned.astype(jnp.bfloat16)
    grad_proj = jnp.concatenate([grad_q[None], grad_kv, jnp.zeros_like(grad_q)[None]], axis=0)
    grad_rows = grad_proj.transpose(0, 3, 1, 2).reshape(grad_proj.shape[0], rows, inner)
    grad_normed = jnp.einsum(
        "wrh,dwh->rd", grad_rows, weights, preferred_element_type=jnp.float32
    )
    along = jnp.sum(grad_normed * normed_full, axis=-1) / width
    unscaled_input = inv_rms[:, None] * (grad_normed - normed_full * along[:, None])
    key_value_part = jnp.einsum(
        "rd,wgcr->dwgc", normed, grad_proj[1:3], preferred_element_type=jnp.float32
    ).reshape(width, 2, inner)
    late, _ = scatter_rows(key_value_part, None, ("tm", "night"), "tm", jnp.bfloat16)
    summed = jnp.concatenate([early[:, :1], late, early[:, 1:]], axis=1)
    total_count = count.astype(jnp.float32)
    loss_scale = jnp.float32(tokens_all) / total_count
    grad_input = (loss_scale * unscaled_input).astype(jnp.bfloat16)
    grad_weights = summed * (jnp.sqrt(jnp.float32(tokens_all)) / total_count)
    return (grad_input[None], grad_weights)


def solution(mesh):
    return jax.shard_map(
        shards,
        mesh=mesh,
        in_specs=(P("night", "tm", None), P(), P("night", "tm", None), P("night", "tm")),
        out_specs=(P("night", "tm", None), P(("tm", "night"), None, None)),
        check_vma=False,
    )
```

```python
import math

import jax
import jax.numpy as jnp
from jax import lax
from jax.sharding import PartitionSpec as P

HEADS = 8
HSIZE = 64
WIN = 1024


def shifted(value, axis, by):
    peers = lax.axis_size(axis)
    pairs = [(i, i + by) for i in range(peers) if 0 <= i + by < peers]
    return lax.ppermute(value, axis, pairs)


def is_power_of_two(n):
    return n > 0 and n & (n - 1) == 0


def halve(value, dim, axis, flip, send_type):
    peers = lax.axis_size(axis)
    bit = (lax.axis_index(axis) // flip) % 2
    keep = lax.dynamic_index_in_dim(value, bit, dim, keepdims=False)
    send = lax.dynamic_index_in_dim(value, 1 - bit, dim, keepdims=False)
    pairs = [(i, i ^ flip) for i in range(peers)]
    return keep + lax.ppermute(send.astype(send_type), axis, pairs).astype(keep.dtype)


def swap_add(value, anchor, axis, flip):
    value, anchor = lax.optimization_barrier((value, anchor))
    peers = lax.axis_size(axis)
    pairs = [(i, i ^ flip) for i in range(peers)]
    return value + lax.ppermute(value, axis, pairs), anchor


def scatter_rows(value, tally, axes, first_axis, wire_type, tail_first=False):
    sizes = [lax.axis_size(axis) for axis in axes]
    rows = value.shape[0]
    groups = math.prod(sizes)
    if not all(is_power_of_two(n) for n in sizes) or rows % groups:
        return (
            lax.psum_scatter(value, axes, scatter_dimension=0, tiled=True),
            None if tally is None else lax.psum(tally, axes),
        )
    stages = [
        (axis, 1 << (n.bit_length() - 2 - i))
        for axis, n in zip(axes, sizes)
        for i in range(n.bit_length() - 1)
    ]
    if not stages:
        return value, tally
    rest = value.shape[1:]
    value = value.reshape((2,) * len(stages) + (rows // groups,) + rest)
    names = list(stages)

    def step(part, part_names, stage, send_type):
        dim = part_names.index(stage)
        return halve(part, dim, *stage, send_type), part_names[:dim] + part_names[dim + 1 :]

    first = (first_axis, 1) if (first_axis, 1) in stages else stages[-1]
    def count_along(tally, anchor, stage):
        if tally is None:
            return tally, anchor
        return swap_add(tally, anchor, *stage)

    def run_tail(value, names, tally):
        for stage in tail:
            value, names = step(value, names, stage, wire_type)
            tally, value = count_along(tally, value, stage)
        return value, names, tally

    value, names = step(value, names, first, wire_type)
    tally, value = count_along(tally, value, first)
    middle = [s for s in stages if s[0] == first[0] and s != first]
    tail = [s for s in stages if s[0] != first[0]][::-1]
    if tail_first:
        value, names, tally = run_tail(value, names, tally)
    if len(middle) > 1 and rest[-1] % 2 == 0:
        cut = rest[-1] // 2
        left, right = value[..., :cut], value[..., cut:]
        left_names, right_names = list(names), list(names)
        for a, b in zip(middle, middle[::-1]):
            left, left_names = step(left, left_names, a, wire_type)
            tally, left = count_along(tally, left, a)
            right, right_names = step(right, right_names, b, wire_type)
        value = jnp.concatenate([left, right], axis=-1)
        names = left_names
    else:
        for stage in middle:
            value, names = step(value, names, stage, wire_type)
            tally, value = count_along(tally, value, stage)
    if not tail_first:
        value, names, tally = run_tail(value, names, tally)
    return value, tally


def band_block(queries, keys_blk, values_blk, grad_attn, valid, inv_scale):
    scores = (
        jnp.einsum("qgc,kgc->gqk", queries, keys_blk, preferred_element_type=jnp.float32)
        * inv_scale
    )
    exp_terms = jnp.exp(scores) * valid[None]
    probs = exp_terms / jnp.sum(exp_terms, axis=-1, keepdims=True)
    probs_low = probs.astype(jnp.bfloat16)
    attended = jnp.einsum(
        "gqk,kgc->qgc", probs_low, values_blk, preferred_element_type=jnp.float32
    ).astype(jnp.bfloat16)
    delta = jnp.sum(grad_attn.astype(jnp.float32) * attended.astype(jnp.float32), axis=-1)
    grad_probs = jnp.einsum(
        "qgc,kgc->gqk", grad_attn, values_blk, preferred_element_type=jnp.float32
    )
    grad_scores = (probs * (grad_probs - jnp.transpose(delta)[:, :, None]) * inv_scale).astype(
        jnp.bfloat16
    )
    grad_query = jnp.einsum(
        "gqk,kgc->gcq", grad_scores, keys_blk, preferred_element_type=jnp.float32
    )
    grad_key = jnp.einsum("gqk,qgc->gck", grad_scores, queries, preferred_element_type=jnp.float32)
    grad_value = jnp.einsum(
        "gqk,qgc->gck", probs_low, grad_attn, preferred_element_type=jnp.float32
    )
    return (attended, grad_query, grad_key, grad_value)


def shards(patches, weights, cotangent, loss_mask):
    rows = patches.shape[1]
    width = patches.shape[2]
    inner = weights.shape[2]
    span = (WIN + rows - 2) // rows
    block_rows = min(512, rows)
    key_len = block_rows + span * rows
    group = HEADS
    group_cols = group * HSIZE
    inv_scale = 1.0 / math.sqrt(HSIZE)
    local_in = patches[0].astype(jnp.float32)
    inv_rms = lax.rsqrt(jnp.mean(local_in * local_in, axis=-1) + 1e-06)
    normed_full = local_in * inv_rms[:, None]
    normed = normed_full.astype(jnp.bfloat16)
    projected = jnp.einsum(
        "rd,dwh->wrh", normed, weights, preferred_element_type=jnp.float32
    ).astype(jnp.bfloat16)
    queries = projected[0]
    key_vals = projected[1:3]
    earlier = [shifted(key_vals, "tm", offset) for offset in range(span, 0, -1)]
    extended = jnp.concatenate(earlier + [key_vals], axis=1)
    local_count = jnp.sum(loss_mask.astype(jnp.int32))
    tokens_all = rows * lax.axis_size("tm") * lax.axis_size("night")
    local_cot = cotangent[0]
    grad_out = jnp.where(loss_mask[0][:, None] > 0, local_cot, jnp.zeros_like(local_cot))
    grad_attn = jnp.einsum(
        "rd,dwh->wrh", grad_out, weights, preferred_element_type=jnp.float32
    )[3].astype(jnp.bfloat16)
    base = lax.axis_index("tm") * rows
    query_idx = jnp.arange(block_rows, dtype=jnp.int32)[:, None]
    key_idx = jnp.arange(key_len, dtype=jnp.int32)[None, :]
    offsets = query_idx - key_idx + span * rows
    band = (offsets >= 0) & (offsets < WIN)
    valid = (band & (key_idx >= span * rows - base)).astype(jnp.float32)
    attended, grad_query, grad_key, grad_value = band_block(
        queries.reshape(rows, HEADS, HSIZE),
        extended[0].reshape(key_len, HEADS, HSIZE),
        extended[1].reshape(key_len, HEADS, HSIZE),
        grad_attn.reshape(rows, HEADS, HSIZE),
        valid,
        inv_scale,
    )
    attended_all = attended.reshape(rows, inner)
    grad_q = grad_query.astype(jnp.bfloat16)
    query_part = jnp.einsum(
        "rd,gcr->dgc", normed, grad_q, preferred_element_type=jnp.float32
    ).reshape(width, inner)
    out_part = jnp.einsum("rd,rh->dh", grad_out, attended_all, preferred_element_type=jnp.float32)
    early, count = scatter_rows(
        jnp.stack([query_part, out_part], axis=1),
        local_count,
        ("tm", "night"),
        "tm",
        jnp.bfloat16,
        tail_first=True,
    )
    owned = jnp.stack([grad_key[..., span * rows :], grad_value[..., span * rows :]])
    for offset in range(1, span + 1):
        lower = (span - offset) * rows
        piece = jnp.stack(
            [grad_key[..., lower : lower + rows], grad_value[..., lower : lower + rows]]
        )
        owned = owned + shifted(piece.astype(jnp.bfloat16), "tm", -offset).astype(jnp.float32)
    grad_kv = owned.astype(jnp.bfloat16)
    grad_proj = jnp.concatenate([grad_q[None], grad_kv, jnp.zeros_like(grad_q)[None]], axis=0)
    grad_rows = grad_proj.transpose(0, 3, 1, 2).reshape(grad_proj.shape[0], rows, inner)
    grad_normed = jnp.einsum(
        "wrh,dwh->rd", grad_rows, weights, preferred_element_type=jnp.float32
    )
    along = jnp.sum(grad_normed * normed_full, axis=-1) / width
    unscaled_input = inv_rms[:, None] * (grad_normed - normed_full * along[:, None])
    key_value_part = jnp.einsum(
        "rd,wgcr->dwgc", normed, grad_proj[1:3], preferred_element_type=jnp.float32
    ).reshape(width, 2, inner)
    late, _ = scatter_rows(key_value_part, None, ("tm", "night"), "tm", jnp.bfloat16)
    summed = jnp.concatenate([early[:, :1], late, early[:, 1:]], axis=1)
    total_count = count.astype(jnp.float32)
    loss_scale = jnp.float32(tokens_all) / total_count
    grad_input = (loss_scale * unscaled_input).astype(jnp.bfloat16)
    grad_weights = summed * (jnp.sqrt(jnp.float32(tokens_all)) / total_count)
    return (grad_input[None], grad_weights)


def solution(mesh):
    return jax.shard_map(
        shards,
        mesh=mesh,
        in_specs=(P("night", "tm", None), P(), P("night", "tm", None), P("night", "tm")),
        out_specs=(P("night", "tm", None), P(("tm", "night"), None, None)),
        check_vma=False,
    )
```

```python
import math

import jax
import jax.numpy as jnp
from jax import lax
from jax.sharding import PartitionSpec as P

HEADS = 8
HSIZE = 64
WIN = 1024


def shifted(value, axis, by):
    peers = lax.axis_size(axis)
    pairs = [(i, i + by) for i in range(peers) if 0 <= i + by < peers]
    return lax.ppermute(value, axis, pairs)


def is_power_of_two(n):
    return n > 0 and n & (n - 1) == 0


def halve(value, dim, axis, flip, send_type):
    peers = lax.axis_size(axis)
    bit = (lax.axis_index(axis) // flip) % 2
    keep = lax.dynamic_index_in_dim(value, bit, dim, keepdims=False)
    send = lax.dynamic_index_in_dim(value, 1 - bit, dim, keepdims=False)
    pairs = [(i, i ^ flip) for i in range(peers)]
    return keep + lax.ppermute(send.astype(send_type), axis, pairs).astype(keep.dtype)


def swap_add(value, anchor, axis, flip):
    value, anchor = lax.optimization_barrier((value, anchor))
    peers = lax.axis_size(axis)
    pairs = [(i, i ^ flip) for i in range(peers)]
    return value + lax.ppermute(value, axis, pairs), anchor


def scatter_rows(value, tally, axes, first_axis, wire_type, tail_first=False):
    sizes = [lax.axis_size(axis) for axis in axes]
    rows = value.shape[0]
    groups = math.prod(sizes)
    if not all(is_power_of_two(n) for n in sizes) or rows % groups:
        return (
            lax.psum_scatter(value, axes, scatter_dimension=0, tiled=True),
            None if tally is None else lax.psum(tally, axes),
        )
    stages = [
        (axis, 1 << (n.bit_length() - 2 - i))
        for axis, n in zip(axes, sizes)
        for i in range(n.bit_length() - 1)
    ]
    if not stages:
        return value, tally
    rest = value.shape[1:]
    value = value.reshape((2,) * len(stages) + (rows // groups,) + rest)
    names = list(stages)

    def step(part, part_names, stage, send_type):
        dim = part_names.index(stage)
        return halve(part, dim, *stage, send_type), part_names[:dim] + part_names[dim + 1 :]

    first = (first_axis, 1) if (first_axis, 1) in stages else stages[-1]
    def count_along(tally, anchor, stage):
        if tally is None:
            return tally, anchor
        return swap_add(tally, anchor, *stage)

    def run_tail(value, names, tally):
        for stage in tail:
            value, names = step(value, names, stage, wire_type)
            tally, value = count_along(tally, value, stage)
        return value, names, tally

    value, names = step(value, names, first, wire_type)
    tally, value = count_along(tally, value, first)
    middle = [s for s in stages if s[0] == first[0] and s != first]
    tail = [s for s in stages if s[0] != first[0]][::-1]
    if tail_first:
        value, names, tally = run_tail(value, names, tally)
    if len(middle) > 1 and rest[-1] % 2 == 0:
        cut = rest[-1] // 2
        left, right = value[..., :cut], value[..., cut:]
        left_names, right_names = list(names), list(names)
        for a, b in zip(middle, middle[::-1]):
            left, left_names = step(left, left_names, a, wire_type)
            tally, left = count_along(tally, left, a)
            right, right_names = step(right, right_names, b, wire_type)
        value = jnp.concatenate([left, right], axis=-1)
        names = left_names
    else:
        for stage in middle:
            value, names = step(value, names, stage, wire_type)
            tally, value = count_along(tally, value, stage)
    if not tail_first:
        value, names, tally = run_tail(value, names, tally)
    return value, tally


def band_block(queries, keys_blk, values_blk, grad_attn, valid, inv_scale):
    scores = (
        jnp.einsum("qgc,kgc->gqk", queries, keys_blk, preferred_element_type=jnp.float32)
        * inv_scale
    )
    exp_terms = jnp.exp(scores) * valid[None]
    probs = exp_terms / jnp.sum(exp_terms, axis=-1, keepdims=True)
    probs_low = probs.astype(jnp.bfloat16)
    attended = jnp.einsum(
        "gqk,kgc->qgc", probs_low, values_blk, preferred_element_type=jnp.float32
    ).astype(jnp.bfloat16)
    delta = jnp.sum(grad_attn.astype(jnp.float32) * attended.astype(jnp.float32), axis=-1)
    grad_probs = jnp.einsum(
        "qgc,kgc->gqk", grad_attn, values_blk, preferred_element_type=jnp.float32
    )
    grad_scores = (probs * (grad_probs - jnp.transpose(delta)[:, :, None]) * inv_scale).astype(
        jnp.bfloat16
    )
    grad_query = jnp.einsum(
        "gqk,kgc->gcq", grad_scores, keys_blk, preferred_element_type=jnp.float32
    )
    grad_key = jnp.einsum("gqk,qgc->gck", grad_scores, queries, preferred_element_type=jnp.float32)
    grad_value = jnp.einsum(
        "gqk,qgc->gck", probs_low, grad_attn, preferred_element_type=jnp.float32
    )
    return (attended, grad_query, grad_key, grad_value)


def shards(patches, weights, cotangent, loss_mask):
    rows = patches.shape[1]
    width = patches.shape[2]
    inner = weights.shape[2]
    span = (WIN + rows - 2) // rows
    block_rows = min(512, rows)
    key_len = block_rows + span * rows
    group = HEADS
    group_cols = group * HSIZE
    inv_scale = 1.0 / math.sqrt(HSIZE)
    local_in = patches[0].astype(jnp.float32)
    inv_rms = lax.rsqrt(jnp.mean(local_in * local_in, axis=-1) + 1e-06)
    normed_full = local_in * inv_rms[:, None]
    normed = normed_full.astype(jnp.bfloat16)
    projected = jnp.einsum(
        "rd,dwh->wrh", normed, weights, preferred_element_type=jnp.float32
    ).astype(jnp.bfloat16)
    queries = projected[0]
    key_vals = projected[1:3]
    earlier = [shifted(key_vals, "tm", offset) for offset in range(span, 0, -1)]
    extended = jnp.concatenate(earlier + [key_vals], axis=1)
    local_count = jnp.sum(loss_mask.astype(jnp.int32))
    tokens_all = rows * lax.axis_size("tm") * lax.axis_size("night")
    local_cot = cotangent[0]
    grad_out = jnp.where(loss_mask[0][:, None] > 0, local_cot, jnp.zeros_like(local_cot))
    grad_attn = jnp.einsum(
        "rd,dwh->wrh", grad_out, weights, preferred_element_type=jnp.float32
    )[3].astype(jnp.bfloat16)
    base = lax.axis_index("tm") * rows
    query_idx = jnp.arange(block_rows, dtype=jnp.int32)[:, None]
    key_idx = jnp.arange(key_len, dtype=jnp.int32)[None, :]
    offsets = query_idx - key_idx + span * rows
    band = (offsets >= 0) & (offsets < WIN)
    valid = (band & (key_idx >= span * rows - base)).astype(jnp.float32)
    attended, grad_query, grad_key, grad_value = band_block(
        queries.reshape(rows, HEADS, HSIZE),
        extended[0].reshape(key_len, HEADS, HSIZE),
        extended[1].reshape(key_len, HEADS, HSIZE),
        grad_attn.reshape(rows, HEADS, HSIZE),
        valid,
        inv_scale,
    )
    attended_all = attended.reshape(rows, inner)
    grad_q = grad_query.astype(jnp.bfloat16)
    query_part = jnp.einsum(
        "rd,gcr->dgc", normed, grad_q, preferred_element_type=jnp.float32
    ).reshape(width, inner)
    out_part = jnp.einsum("rd,rh->dh", grad_out, attended_all, preferred_element_type=jnp.float32)
    early_terms = jnp.stack([query_part, out_part], axis=1)
    blocks = lax.axis_size("tm") * lax.axis_size("night")
    block_rows_out = width // blocks
    bits = rows.bit_length()
    if width % blocks == 0 and block_rows_out % 8 == 0 and blocks <= 256 and bits <= inner:
        digits = (local_count // (2 ** jnp.arange(bits, dtype=jnp.int32))) % 2
        count_rows = jnp.zeros((blocks, 8) + early_terms.shape[1:], jnp.float32)
        count_rows = count_rows.at[:, 0, 0, :bits].set(digits.astype(jnp.float32))
        payload = jnp.concatenate(
            [early_terms.reshape((blocks, block_rows_out) + early_terms.shape[1:]), count_rows],
            axis=1,
        ).reshape((-1,) + early_terms.shape[1:])
        early, _ = scatter_rows(
            payload, None, ("tm", "night"), "tm", jnp.bfloat16, tail_first=True
        )
        digit_sums = early[block_rows_out, 0, :bits].astype(jnp.int32)
        count = jnp.sum(digit_sums * (2 ** jnp.arange(bits, dtype=jnp.int32)))
        early = early[:block_rows_out]
    else:
        early, count = scatter_rows(
            early_terms, local_count, ("tm", "night"), "tm", jnp.bfloat16, tail_first=True
        )
    owned = jnp.stack([grad_key[..., span * rows :], grad_value[..., span * rows :]])
    for offset in range(1, span + 1):
        lower = (span - offset) * rows
        piece = jnp.stack(
            [grad_key[..., lower : lower + rows], grad_value[..., lower : lower + rows]]
        )
        owned = owned + shifted(piece.astype(jnp.bfloat16), "tm", -offset).astype(jnp.float32)
    grad_kv = owned.astype(jnp.bfloat16)
    grad_proj = jnp.concatenate([grad_q[None], grad_kv, jnp.zeros_like(grad_q)[None]], axis=0)
    grad_rows = grad_proj.transpose(0, 3, 1, 2).reshape(grad_proj.shape[0], rows, inner)
    grad_normed = jnp.einsum(
        "wrh,dwh->rd", grad_rows, weights, preferred_element_type=jnp.float32
    )
    along = jnp.sum(grad_normed * normed_full, axis=-1) / width
    unscaled_input = inv_rms[:, None] * (grad_normed - normed_full * along[:, None])
    key_value_part = jnp.einsum(
        "rd,wgcr->dwgc", normed, grad_proj[1:3], preferred_element_type=jnp.float32
    ).reshape(width, 2, inner)
    late, _ = scatter_rows(key_value_part, None, ("tm", "night"), "tm", jnp.bfloat16)
    summed = jnp.concatenate([early[:, :1], late, early[:, 1:]], axis=1)
    total_count = count.astype(jnp.float32)
    loss_scale = jnp.float32(tokens_all) / total_count
    grad_input = (loss_scale * unscaled_input).astype(jnp.bfloat16)
    grad_weights = summed * (jnp.sqrt(jnp.float32(tokens_all)) / total_count)
    return (grad_input[None], grad_weights)


def solution(mesh):
    return jax.shard_map(
        shards,
        mesh=mesh,
        in_specs=(P("night", "tm", None), P(), P("night", "tm", None), P("night", "tm")),
        out_specs=(P("night", "tm", None), P(("tm", "night"), None, None)),
        check_vma=False,
    )
```

```python
import math

import jax
import jax.numpy as jnp
from jax import lax
from jax.sharding import PartitionSpec as P

HEADS = 8
HSIZE = 64
WIN = 1024


def shifted(value, axis, by):
    peers = lax.axis_size(axis)
    pairs = [(i, i + by) for i in range(peers) if 0 <= i + by < peers]
    return lax.ppermute(value, axis, pairs)


def is_power_of_two(n):
    return n > 0 and n & (n - 1) == 0


def halve(value, dim, axis, flip, send_type):
    peers = lax.axis_size(axis)
    bit = (lax.axis_index(axis) // flip) % 2
    keep = lax.dynamic_index_in_dim(value, bit, dim, keepdims=False)
    send = lax.dynamic_index_in_dim(value, 1 - bit, dim, keepdims=False)
    pairs = [(i, i ^ flip) for i in range(peers)]
    return keep + lax.ppermute(send.astype(send_type), axis, pairs).astype(keep.dtype)


def swap_add(value, anchor, axis, flip):
    value, anchor = lax.optimization_barrier((value, anchor))
    peers = lax.axis_size(axis)
    pairs = [(i, i ^ flip) for i in range(peers)]
    return value + lax.ppermute(value, axis, pairs), anchor


def scatter_rows(value, tally, axes, first_axis, wire_type, tail_first=False):
    sizes = [lax.axis_size(axis) for axis in axes]
    rows = value.shape[0]
    groups = math.prod(sizes)
    if not all(is_power_of_two(n) for n in sizes) or rows % groups:
        return (
            lax.psum_scatter(value, axes, scatter_dimension=0, tiled=True),
            None if tally is None else lax.psum(tally, axes),
        )
    stages = [
        (axis, 1 << (n.bit_length() - 2 - i))
        for axis, n in zip(axes, sizes)
        for i in range(n.bit_length() - 1)
    ]
    if not stages:
        return value, tally
    rest = value.shape[1:]
    value = value.reshape((2,) * len(stages) + (rows // groups,) + rest)
    names = list(stages)

    def step(part, part_names, stage, send_type):
        dim = part_names.index(stage)
        return halve(part, dim, *stage, send_type), part_names[:dim] + part_names[dim + 1 :]

    first = (first_axis, 1) if (first_axis, 1) in stages else stages[-1]
    def count_along(tally, anchor, stage):
        if tally is None:
            return tally, anchor
        return swap_add(tally, anchor, *stage)

    def run_tail(value, names, tally):
        for stage in tail:
            value, names = step(value, names, stage, wire_type)
            tally, value = count_along(tally, value, stage)
        return value, names, tally

    value, names = step(value, names, first, wire_type)
    tally, value = count_along(tally, value, first)
    middle = [s for s in stages if s[0] == first[0] and s != first]
    tail = [s for s in stages if s[0] != first[0]][::-1]
    if tail_first:
        value, names, tally = run_tail(value, names, tally)
    if len(middle) > 1 and rest[-1] % 2 == 0:
        cut = rest[-1] // 2
        left, right = value[..., :cut], value[..., cut:]
        left_names, right_names = list(names), list(names)
        for a, b in zip(middle, middle[::-1]):
            left, left_names = step(left, left_names, a, wire_type)
            tally, left = count_along(tally, left, a)
            right, right_names = step(right, right_names, b, wire_type)
        value = jnp.concatenate([left, right], axis=-1)
        names = left_names
    else:
        for stage in middle:
            value, names = step(value, names, stage, wire_type)
            tally, value = count_along(tally, value, stage)
    if not tail_first:
        value, names, tally = run_tail(value, names, tally)
    return value, tally


def band_block(queries, keys_blk, values_blk, grad_attn, valid, inv_scale):
    scores = (
        jnp.einsum("qgc,kgc->gqk", queries, keys_blk, preferred_element_type=jnp.float32)
        * inv_scale
    )
    exp_terms = jnp.exp(scores) * valid[None]
    probs = exp_terms / jnp.sum(exp_terms, axis=-1, keepdims=True)
    probs_low = probs.astype(jnp.bfloat16)
    attended = jnp.einsum(
        "gqk,kgc->qgc", probs_low, values_blk, preferred_element_type=jnp.float32
    ).astype(jnp.bfloat16)
    delta = jnp.sum(grad_attn.astype(jnp.float32) * attended.astype(jnp.float32), axis=-1)
    grad_probs = jnp.einsum(
        "qgc,kgc->gqk", grad_attn, values_blk, preferred_element_type=jnp.float32
    )
    grad_scores = (probs * (grad_probs - jnp.transpose(delta)[:, :, None]) * inv_scale).astype(
        jnp.bfloat16
    )
    grad_query = jnp.einsum(
        "gqk,kgc->gcq", grad_scores, keys_blk, preferred_element_type=jnp.float32
    )
    grad_key = jnp.einsum("gqk,qgc->gck", grad_scores, queries, preferred_element_type=jnp.float32)
    grad_value = jnp.einsum(
        "gqk,qgc->gck", probs_low, grad_attn, preferred_element_type=jnp.float32
    )
    return (attended, grad_query, grad_key, grad_value)


def shards(patches, weights, cotangent, loss_mask):
    rows = patches.shape[1]
    width = patches.shape[2]
    inner = weights.shape[2]
    span = (WIN + rows - 2) // rows
    block_rows = min(512, rows)
    key_len = block_rows + span * rows
    group = HEADS
    group_cols = group * HSIZE
    inv_scale = 1.0 / math.sqrt(HSIZE)
    local_in = patches[0].astype(jnp.float32)
    inv_rms = lax.rsqrt(jnp.mean(local_in * local_in, axis=-1) + 1e-06)
    normed_full = local_in * inv_rms[:, None]
    normed = normed_full.astype(jnp.bfloat16)
    projected = jnp.einsum(
        "rd,dwh->wrh", normed, weights, preferred_element_type=jnp.float32
    ).astype(jnp.bfloat16)
    queries = projected[0]
    key_vals = projected[1:3]
    earlier = [shifted(key_vals, "tm", offset) for offset in range(span, 0, -1)]
    extended = jnp.concatenate(earlier + [key_vals], axis=1)
    local_count = jnp.sum(loss_mask.astype(jnp.int32))
    tokens_all = rows * lax.axis_size("tm") * lax.axis_size("night")
    local_cot = cotangent[0]
    grad_out = jnp.where(loss_mask[0][:, None] > 0, local_cot, jnp.zeros_like(local_cot))
    grad_attn = jnp.einsum(
        "rd,dwh->wrh", grad_out, weights, preferred_element_type=jnp.float32
    )[3].astype(jnp.bfloat16)
    base = lax.axis_index("tm") * rows
    query_idx = jnp.arange(block_rows, dtype=jnp.int32)[:, None]
    key_idx = jnp.arange(key_len, dtype=jnp.int32)[None, :]
    offsets = query_idx - key_idx + span * rows
    band = (offsets >= 0) & (offsets < WIN)
    valid = (band & (key_idx >= span * rows - base)).astype(jnp.float32)
    attended, grad_query, grad_key, grad_value = band_block(
        queries.reshape(rows, HEADS, HSIZE),
        extended[0].reshape(key_len, HEADS, HSIZE),
        extended[1].reshape(key_len, HEADS, HSIZE),
        grad_attn.reshape(rows, HEADS, HSIZE),
        valid,
        inv_scale,
    )
    attended_all = attended.reshape(rows, inner)
    grad_q = grad_query.astype(jnp.bfloat16)
    query_part = jnp.einsum(
        "rd,gcr->dgc", normed, grad_q, preferred_element_type=jnp.float32
    ).reshape(width, inner)
    out_part = jnp.einsum("rd,rh->dh", grad_out, attended_all, preferred_element_type=jnp.float32)
    early_terms = jnp.stack([query_part, out_part], axis=1)
    blocks = lax.axis_size("tm") * lax.axis_size("night")
    block_rows_out = width // blocks
    bits = rows.bit_length()
    if width % blocks == 0 and block_rows_out % 8 == 0 and blocks <= 256 and bits <= inner:
        digits = (local_count // (2 ** jnp.arange(bits, dtype=jnp.int32))) % 2
        count_rows = jnp.zeros((blocks, 8) + early_terms.shape[1:], jnp.float32)
        count_rows = count_rows.at[:, 0, 0, :bits].set(digits.astype(jnp.float32))
        payload = jnp.concatenate(
            [early_terms.reshape((blocks, block_rows_out) + early_terms.shape[1:]), count_rows],
            axis=1,
        ).reshape((-1,) + early_terms.shape[1:])
        early, _ = scatter_rows(
            payload, None, ("tm", "night"), "tm", jnp.bfloat16, tail_first=True
        )
        digit_sums = early[block_rows_out, 0, :bits].astype(jnp.int32)
        count = jnp.sum(digit_sums * (2 ** jnp.arange(bits, dtype=jnp.int32)))
        early = early[:block_rows_out]
    else:
        early, count = scatter_rows(
            early_terms, local_count, ("tm", "night"), "tm", jnp.bfloat16, tail_first=True
        )
    owned = jnp.stack([grad_key[..., span * rows :], grad_value[..., span * rows :]])
    for offset in range(span, 0, -1):
        lower = (span - offset) * rows
        piece = jnp.stack(
            [grad_key[..., lower : lower + rows], grad_value[..., lower : lower + rows]]
        )
        owned = owned + shifted(piece.astype(jnp.bfloat16), "tm", -offset).astype(jnp.float32)
    grad_kv = owned.astype(jnp.bfloat16)
    grad_proj = jnp.concatenate([grad_q[None], grad_kv, jnp.zeros_like(grad_q)[None]], axis=0)
    grad_rows = grad_proj.transpose(0, 3, 1, 2).reshape(grad_proj.shape[0], rows, inner)
    grad_normed = jnp.einsum(
        "wrh,dwh->rd", grad_rows, weights, preferred_element_type=jnp.float32
    )
    along = jnp.sum(grad_normed * normed_full, axis=-1) / width
    unscaled_input = inv_rms[:, None] * (grad_normed - normed_full * along[:, None])
    key_value_part = jnp.einsum(
        "rd,wgcr->dwgc", normed, grad_proj[1:3], preferred_element_type=jnp.float32
    ).reshape(width, 2, inner)
    late, _ = scatter_rows(key_value_part, None, ("tm", "night"), "tm", jnp.bfloat16)
    summed = jnp.concatenate([early[:, :1], late, early[:, 1:]], axis=1)
    total_count = count.astype(jnp.float32)
    loss_scale = jnp.float32(tokens_all) / total_count
    grad_input = (loss_scale * unscaled_input).astype(jnp.bfloat16)
    grad_weights = summed * (jnp.sqrt(jnp.float32(tokens_all)) / total_count)
    return (grad_input[None], grad_weights)


def solution(mesh):
    return jax.shard_map(
        shards,
        mesh=mesh,
        in_specs=(P("night", "tm", None), P(), P("night", "tm", None), P("night", "tm")),
        out_specs=(P("night", "tm", None), P(("tm", "night"), None, None)),
        check_vma=False,
    )
```

```python
import math

import jax
import jax.numpy as jnp
from jax import lax
from jax.sharding import PartitionSpec as P

HEADS = 8
HSIZE = 64
WIN = 1024


def shifted(value, axis, by):
    peers = lax.axis_size(axis)
    pairs = [(i, i + by) for i in range(peers) if 0 <= i + by < peers]
    return lax.ppermute(value, axis, pairs)


def is_power_of_two(n):
    return n > 0 and n & (n - 1) == 0


def halve(value, dim, axis, flip, send_type):
    peers = lax.axis_size(axis)
    bit = (lax.axis_index(axis) // flip) % 2
    keep = lax.dynamic_index_in_dim(value, bit, dim, keepdims=False)
    send = lax.dynamic_index_in_dim(value, 1 - bit, dim, keepdims=False)
    pairs = [(i, i ^ flip) for i in range(peers)]
    return keep + lax.ppermute(send.astype(send_type), axis, pairs).astype(keep.dtype)


def swap_add(value, anchor, axis, flip):
    value, anchor = lax.optimization_barrier((value, anchor))
    peers = lax.axis_size(axis)
    pairs = [(i, i ^ flip) for i in range(peers)]
    return value + lax.ppermute(value, axis, pairs), anchor


def scatter_rows(value, tally, axes, first_axis, wire_type, tail_first=False):
    sizes = [lax.axis_size(axis) for axis in axes]
    rows = value.shape[0]
    groups = math.prod(sizes)
    if not all(is_power_of_two(n) for n in sizes) or rows % groups:
        return (
            lax.psum_scatter(value, axes, scatter_dimension=0, tiled=True),
            None if tally is None else lax.psum(tally, axes),
        )
    stages = [
        (axis, 1 << (n.bit_length() - 2 - i))
        for axis, n in zip(axes, sizes)
        for i in range(n.bit_length() - 1)
    ]
    if not stages:
        return value, tally
    rest = value.shape[1:]
    value = value.reshape((2,) * len(stages) + (rows // groups,) + rest)
    names = list(stages)

    def step(part, part_names, stage, send_type):
        dim = part_names.index(stage)
        return halve(part, dim, *stage, send_type), part_names[:dim] + part_names[dim + 1 :]

    first = (first_axis, 1) if (first_axis, 1) in stages else stages[-1]
    def count_along(tally, anchor, stage):
        if tally is None:
            return tally, anchor
        return swap_add(tally, anchor, *stage)

    def run_tail(value, names, tally):
        for stage in tail:
            value, names = step(value, names, stage, wire_type)
            tally, value = count_along(tally, value, stage)
        return value, names, tally

    value, names = step(value, names, first, wire_type)
    tally, value = count_along(tally, value, first)
    middle = [s for s in stages if s[0] == first[0] and s != first]
    tail = [s for s in stages if s[0] != first[0]][::-1]
    if tail_first:
        value, names, tally = run_tail(value, names, tally)
    if len(middle) > 1 and rest[-1] % 2 == 0:
        cut = rest[-1] // 2
        left, right = value[..., :cut], value[..., cut:]
        left_names, right_names = list(names), list(names)
        for a, b in zip(middle, middle[::-1]):
            left, left_names = step(left, left_names, a, wire_type)
            tally, left = count_along(tally, left, a)
            right, right_names = step(right, right_names, b, wire_type)
        value = jnp.concatenate([left, right], axis=-1)
        names = left_names
    else:
        for stage in middle:
            value, names = step(value, names, stage, wire_type)
            tally, value = count_along(tally, value, stage)
    if not tail_first:
        value, names, tally = run_tail(value, names, tally)
    return value, tally


def band_block(queries, keys_blk, values_blk, grad_attn, valid, inv_scale):
    scores = (
        jnp.einsum("qgc,kgc->gqk", queries, keys_blk, preferred_element_type=jnp.float32)
        * inv_scale
    )
    exp_terms = jnp.exp(scores) * valid[None]
    probs = exp_terms / jnp.sum(exp_terms, axis=-1, keepdims=True)
    probs_low = probs.astype(jnp.bfloat16)
    attended = jnp.einsum(
        "gqk,kgc->qgc", probs_low, values_blk, preferred_element_type=jnp.float32
    ).astype(jnp.bfloat16)
    delta = jnp.sum(grad_attn.astype(jnp.float32) * attended.astype(jnp.float32), axis=-1)
    grad_probs = jnp.einsum(
        "qgc,kgc->gqk", grad_attn, values_blk, preferred_element_type=jnp.float32
    )
    grad_scores = (probs * (grad_probs - jnp.transpose(delta)[:, :, None]) * inv_scale).astype(
        jnp.bfloat16
    )
    grad_query = jnp.einsum(
        "gqk,kgc->gcq", grad_scores, keys_blk, preferred_element_type=jnp.float32
    )
    grad_key = jnp.einsum("gqk,qgc->gck", grad_scores, queries, preferred_element_type=jnp.float32)
    grad_value = jnp.einsum(
        "gqk,qgc->gck", probs_low, grad_attn, preferred_element_type=jnp.float32
    )
    return (attended, grad_query, grad_key, grad_value)


def shards(patches, weights, cotangent, loss_mask):
    rows = patches.shape[1]
    width = patches.shape[2]
    inner = weights.shape[2]
    span = (WIN + rows - 2) // rows
    block_rows = min(512, rows)
    key_len = block_rows + span * rows
    group = HEADS
    group_cols = group * HSIZE
    inv_scale = 1.0 / math.sqrt(HSIZE)
    local_in = patches[0].astype(jnp.float32)
    inv_rms = lax.rsqrt(jnp.mean(local_in * local_in, axis=-1) + 1e-06)
    normed_full = local_in * inv_rms[:, None]
    normed = normed_full.astype(jnp.bfloat16)
    projected = jnp.einsum(
        "rd,dwh->wrh", normed, weights, preferred_element_type=jnp.float32
    ).astype(jnp.bfloat16)
    queries = projected[0]
    key_vals = projected[1:3]
    arrived = {offset: shifted(key_vals, "tm", offset) for offset in range(1, span + 1)}
    earlier = [arrived[offset] for offset in range(span, 0, -1)]
    extended = jnp.concatenate(earlier + [key_vals], axis=1)
    local_count = jnp.sum(loss_mask.astype(jnp.int32))
    tokens_all = rows * lax.axis_size("tm") * lax.axis_size("night")
    local_cot = cotangent[0]
    grad_out = jnp.where(loss_mask[0][:, None] > 0, local_cot, jnp.zeros_like(local_cot))
    grad_attn = jnp.einsum(
        "rd,dwh->wrh", grad_out, weights, preferred_element_type=jnp.float32
    )[3].astype(jnp.bfloat16)
    base = lax.axis_index("tm") * rows
    query_idx = jnp.arange(block_rows, dtype=jnp.int32)[:, None]
    key_idx = jnp.arange(key_len, dtype=jnp.int32)[None, :]
    offsets = query_idx - key_idx + span * rows
    band = (offsets >= 0) & (offsets < WIN)
    valid = (band & (key_idx >= span * rows - base)).astype(jnp.float32)
    attended, grad_query, grad_key, grad_value = band_block(
        queries.reshape(rows, HEADS, HSIZE),
        extended[0].reshape(key_len, HEADS, HSIZE),
        extended[1].reshape(key_len, HEADS, HSIZE),
        grad_attn.reshape(rows, HEADS, HSIZE),
        valid,
        inv_scale,
    )
    attended_all = attended.reshape(rows, inner)
    grad_q = grad_query.astype(jnp.bfloat16)
    query_part = jnp.einsum(
        "rd,gcr->dgc", normed, grad_q, preferred_element_type=jnp.float32
    ).reshape(width, inner)
    out_part = jnp.einsum("rd,rh->dh", grad_out, attended_all, preferred_element_type=jnp.float32)
    early_terms = jnp.stack([query_part, out_part], axis=1)
    blocks = lax.axis_size("tm") * lax.axis_size("night")
    block_rows_out = width // blocks
    bits = rows.bit_length()
    if width % blocks == 0 and block_rows_out % 8 == 0 and blocks <= 256 and bits <= inner:
        digits = (local_count // (2 ** jnp.arange(bits, dtype=jnp.int32))) % 2
        count_rows = jnp.zeros((blocks, 8) + early_terms.shape[1:], jnp.float32)
        count_rows = count_rows.at[:, 0, 0, :bits].set(digits.astype(jnp.float32))
        payload = jnp.concatenate(
            [early_terms.reshape((blocks, block_rows_out) + early_terms.shape[1:]), count_rows],
            axis=1,
        ).reshape((-1,) + early_terms.shape[1:])
        early, _ = scatter_rows(
            payload, None, ("tm", "night"), "tm", jnp.bfloat16, tail_first=True
        )
        digit_sums = early[block_rows_out, 0, :bits].astype(jnp.int32)
        count = jnp.sum(digit_sums * (2 ** jnp.arange(bits, dtype=jnp.int32)))
        early = early[:block_rows_out]
    else:
        early, count = scatter_rows(
            early_terms, local_count, ("tm", "night"), "tm", jnp.bfloat16, tail_first=True
        )
    owned = jnp.stack([grad_key[..., span * rows :], grad_value[..., span * rows :]])
    for offset in range(1, span + 1):
        lower = (span - offset) * rows
        piece = jnp.stack(
            [grad_key[..., lower : lower + rows], grad_value[..., lower : lower + rows]]
        )
        owned = owned + shifted(piece.astype(jnp.bfloat16), "tm", -offset).astype(jnp.float32)
    grad_kv = owned.astype(jnp.bfloat16)
    grad_proj = jnp.concatenate([grad_q[None], grad_kv, jnp.zeros_like(grad_q)[None]], axis=0)
    grad_rows = grad_proj.transpose(0, 3, 1, 2).reshape(grad_proj.shape[0], rows, inner)
    grad_normed = jnp.einsum(
        "wrh,dwh->rd", grad_rows, weights, preferred_element_type=jnp.float32
    )
    along = jnp.sum(grad_normed * normed_full, axis=-1) / width
    unscaled_input = inv_rms[:, None] * (grad_normed - normed_full * along[:, None])
    key_value_part = jnp.einsum(
        "rd,wgcr->dwgc", normed, grad_proj[1:3], preferred_element_type=jnp.float32
    ).reshape(width, 2, inner)
    late, _ = scatter_rows(key_value_part, None, ("tm", "night"), "tm", jnp.bfloat16)
    summed = jnp.concatenate([early[:, :1], late, early[:, 1:]], axis=1)
    total_count = count.astype(jnp.float32)
    loss_scale = jnp.float32(tokens_all) / total_count
    grad_input = (loss_scale * unscaled_input).astype(jnp.bfloat16)
    grad_weights = summed * (jnp.sqrt(jnp.float32(tokens_all)) / total_count)
    return (grad_input[None], grad_weights)


def solution(mesh):
    return jax.shard_map(
        shards,
        mesh=mesh,
        in_specs=(P("night", "tm", None), P(), P("night", "tm", None), P("night", "tm")),
        out_specs=(P("night", "tm", None), P(("tm", "night"), None, None)),
        check_vma=False,
    )
```

```python
import math

import jax
import jax.numpy as jnp
from jax import lax
from jax.sharding import PartitionSpec as P

HEADS = 8
HSIZE = 64
WIN = 1024


def shifted(value, axis, by):
    peers = lax.axis_size(axis)
    pairs = [(i, i + by) for i in range(peers) if 0 <= i + by < peers]
    return lax.ppermute(value, axis, pairs)


def is_power_of_two(n):
    return n > 0 and n & (n - 1) == 0


def halve(value, dim, axis, flip, send_type):
    peers = lax.axis_size(axis)
    bit = (lax.axis_index(axis) // flip) % 2
    keep = lax.dynamic_index_in_dim(value, bit, dim, keepdims=False)
    send = lax.dynamic_index_in_dim(value, 1 - bit, dim, keepdims=False)
    pairs = [(i, i ^ flip) for i in range(peers)]
    return keep + lax.ppermute(send.astype(send_type), axis, pairs).astype(keep.dtype)


def swap_add(value, anchor, axis, flip):
    value, anchor = lax.optimization_barrier((value, anchor))
    peers = lax.axis_size(axis)
    pairs = [(i, i ^ flip) for i in range(peers)]
    return value + lax.ppermute(value, axis, pairs), anchor


def scatter_rows(value, tally, axes, first_axis, wire_type, tail_first=False, balance=True):
    sizes = [lax.axis_size(axis) for axis in axes]
    rows = value.shape[0]
    groups = math.prod(sizes)
    if not all(is_power_of_two(n) for n in sizes) or rows % groups:
        return (
            lax.psum_scatter(value, axes, scatter_dimension=0, tiled=True),
            None if tally is None else lax.psum(tally, axes),
        )
    stages = [
        (axis, 1 << (n.bit_length() - 2 - i))
        for axis, n in zip(axes, sizes)
        for i in range(n.bit_length() - 1)
    ]
    if not stages:
        return value, tally
    rest = value.shape[1:]
    value = value.reshape((2,) * len(stages) + (rows // groups,) + rest)
    names = list(stages)

    def step(part, part_names, stage, send_type):
        dim = part_names.index(stage)
        return halve(part, dim, *stage, send_type), part_names[:dim] + part_names[dim + 1 :]

    first = (first_axis, 1) if (first_axis, 1) in stages else stages[-1]
    def count_along(tally, anchor, stage):
        if tally is None:
            return tally, anchor
        return swap_add(tally, anchor, *stage)

    def run_tail(value, names, tally):
        for stage in tail:
            value, names = step(value, names, stage, wire_type)
            tally, value = count_along(tally, value, stage)
        return value, names, tally

    value, names = step(value, names, first, wire_type)
    tally, value = count_along(tally, value, first)
    middle = [s for s in stages if s[0] == first[0] and s != first]
    tail = [s for s in stages if s[0] != first[0]][::-1]
    if tail_first:
        value, names, tally = run_tail(value, names, tally)
    if balance and len(middle) > 1 and rest[-1] % 2 == 0:
        cut = rest[-1] // 2
        left, right = value[..., :cut], value[..., cut:]
        left_names, right_names = list(names), list(names)
        for a, b in zip(middle, middle[::-1]):
            left, left_names = step(left, left_names, a, wire_type)
            tally, left = count_along(tally, left, a)
            right, right_names = step(right, right_names, b, wire_type)
        value = jnp.concatenate([left, right], axis=-1)
        names = left_names
    else:
        for stage in middle:
            value, names = step(value, names, stage, wire_type)
            tally, value = count_along(tally, value, stage)
    if not tail_first:
        value, names, tally = run_tail(value, names, tally)
    return value, tally


def band_block(queries, keys_blk, values_blk, grad_attn, valid, inv_scale):
    scores = (
        jnp.einsum("qgc,kgc->gqk", queries, keys_blk, preferred_element_type=jnp.float32)
        * inv_scale
    )
    exp_terms = jnp.exp(scores) * valid[None]
    probs = exp_terms / jnp.sum(exp_terms, axis=-1, keepdims=True)
    probs_low = probs.astype(jnp.bfloat16)
    attended = jnp.einsum(
        "gqk,kgc->qgc", probs_low, values_blk, preferred_element_type=jnp.float32
    ).astype(jnp.bfloat16)
    delta = jnp.sum(grad_attn.astype(jnp.float32) * attended.astype(jnp.float32), axis=-1)
    grad_probs = jnp.einsum(
        "qgc,kgc->gqk", grad_attn, values_blk, preferred_element_type=jnp.float32
    )
    grad_scores = (probs * (grad_probs - jnp.transpose(delta)[:, :, None]) * inv_scale).astype(
        jnp.bfloat16
    )
    grad_query = jnp.einsum(
        "gqk,kgc->gcq", grad_scores, keys_blk, preferred_element_type=jnp.float32
    )
    grad_key = jnp.einsum("gqk,qgc->gck", grad_scores, queries, preferred_element_type=jnp.float32)
    grad_value = jnp.einsum(
        "gqk,qgc->gck", probs_low, grad_attn, preferred_element_type=jnp.float32
    )
    return (attended, grad_query, grad_key, grad_value)


def shards(patches, weights, cotangent, loss_mask):
    rows = patches.shape[1]
    width = patches.shape[2]
    inner = weights.shape[2]
    span = (WIN + rows - 2) // rows
    block_rows = min(512, rows)
    key_len = block_rows + span * rows
    group = HEADS
    group_cols = group * HSIZE
    inv_scale = 1.0 / math.sqrt(HSIZE)
    local_in = patches[0].astype(jnp.float32)
    inv_rms = lax.rsqrt(jnp.mean(local_in * local_in, axis=-1) + 1e-06)
    normed_full = local_in * inv_rms[:, None]
    normed = normed_full.astype(jnp.bfloat16)
    projected = jnp.einsum(
        "rd,dwh->wrh", normed, weights, preferred_element_type=jnp.float32
    ).astype(jnp.bfloat16)
    queries = projected[0]
    key_vals = projected[1:3]
    arrived = {offset: shifted(key_vals, "tm", offset) for offset in range(1, span + 1)}
    earlier = [arrived[offset] for offset in range(span, 0, -1)]
    extended = jnp.concatenate(earlier + [key_vals], axis=1)
    local_count = jnp.sum(loss_mask.astype(jnp.int32))
    tokens_all = rows * lax.axis_size("tm") * lax.axis_size("night")
    local_cot = cotangent[0]
    grad_out = jnp.where(loss_mask[0][:, None] > 0, local_cot, jnp.zeros_like(local_cot))
    grad_attn = jnp.einsum(
        "rd,dwh->wrh", grad_out, weights, preferred_element_type=jnp.float32
    )[3].astype(jnp.bfloat16)
    base = lax.axis_index("tm") * rows
    query_idx = jnp.arange(block_rows, dtype=jnp.int32)[:, None]
    key_idx = jnp.arange(key_len, dtype=jnp.int32)[None, :]
    offsets = query_idx - key_idx + span * rows
    band = (offsets >= 0) & (offsets < WIN)
    valid = (band & (key_idx >= span * rows - base)).astype(jnp.float32)
    attended, grad_query, grad_key, grad_value = band_block(
        queries.reshape(rows, HEADS, HSIZE),
        extended[0].reshape(key_len, HEADS, HSIZE),
        extended[1].reshape(key_len, HEADS, HSIZE),
        grad_attn.reshape(rows, HEADS, HSIZE),
        valid,
        inv_scale,
    )
    attended_all = attended.reshape(rows, inner)
    grad_q = grad_query.astype(jnp.bfloat16)
    query_part = jnp.einsum(
        "rd,gcr->dgc", normed, grad_q, preferred_element_type=jnp.float32
    ).reshape(width, inner)
    out_part = jnp.einsum("rd,rh->dh", grad_out, attended_all, preferred_element_type=jnp.float32)
    early_terms = jnp.stack([query_part, out_part], axis=1)
    blocks = lax.axis_size("tm") * lax.axis_size("night")
    block_rows_out = width // blocks
    bits = rows.bit_length()
    if width % blocks == 0 and block_rows_out % 8 == 0 and blocks <= 256 and bits <= inner:
        digits = (local_count // (2 ** jnp.arange(bits, dtype=jnp.int32))) % 2
        count_rows = jnp.zeros((blocks, 8) + early_terms.shape[1:], jnp.float32)
        count_rows = count_rows.at[:, 0, 0, :bits].set(digits.astype(jnp.float32))
        payload = jnp.concatenate(
            [early_terms.reshape((blocks, block_rows_out) + early_terms.shape[1:]), count_rows],
            axis=1,
        ).reshape((-1,) + early_terms.shape[1:])
        early, _ = scatter_rows(
            payload, None, ("tm", "night"), "tm", jnp.bfloat16, tail_first=True
        )
        digit_sums = early[block_rows_out, 0, :bits].astype(jnp.int32)
        count = jnp.sum(digit_sums * (2 ** jnp.arange(bits, dtype=jnp.int32)))
        early = early[:block_rows_out]
    else:
        early, count = scatter_rows(
            early_terms, local_count, ("tm", "night"), "tm", jnp.bfloat16, tail_first=True
        )
    owned = jnp.stack([grad_key[..., span * rows :], grad_value[..., span * rows :]])
    for offset in range(1, span + 1):
        lower = (span - offset) * rows
        piece = jnp.stack(
            [grad_key[..., lower : lower + rows], grad_value[..., lower : lower + rows]]
        )
        owned = owned + shifted(piece.astype(jnp.bfloat16), "tm", -offset).astype(jnp.float32)
    grad_kv = owned.astype(jnp.bfloat16)
    grad_proj = jnp.concatenate([grad_q[None], grad_kv, jnp.zeros_like(grad_q)[None]], axis=0)
    grad_rows = grad_proj.transpose(0, 3, 1, 2).reshape(grad_proj.shape[0], rows, inner)
    grad_normed = jnp.einsum(
        "wrh,dwh->rd", grad_rows, weights, preferred_element_type=jnp.float32
    )
    along = jnp.sum(grad_normed * normed_full, axis=-1) / width
    unscaled_input = inv_rms[:, None] * (grad_normed - normed_full * along[:, None])
    key_value_part = jnp.einsum(
        "rd,wgcr->dwgc", normed, grad_proj[1:3], preferred_element_type=jnp.float32
    ).reshape(width, 2, inner)
    late, _ = scatter_rows(
        key_value_part, None, ("tm", "night"), "tm", jnp.bfloat16, balance=False
    )
    summed = jnp.concatenate([early[:, :1], late, early[:, 1:]], axis=1)
    total_count = count.astype(jnp.float32)
    loss_scale = jnp.float32(tokens_all) / total_count
    grad_input = (loss_scale * unscaled_input).astype(jnp.bfloat16)
    grad_weights = summed * (jnp.sqrt(jnp.float32(tokens_all)) / total_count)
    return (grad_input[None], grad_weights)


def solution(mesh):
    return jax.shard_map(
        shards,
        mesh=mesh,
        in_specs=(P("night", "tm", None), P(), P("night", "tm", None), P("night", "tm")),
        out_specs=(P("night", "tm", None), P(("tm", "night"), None, None)),
        check_vma=False,
    )
```

```python
import math

import jax
import jax.numpy as jnp
from jax import lax
from jax.sharding import PartitionSpec as P

HEADS = 8
HSIZE = 64
WIN = 1024


def shifted(value, axis, by):
    peers = lax.axis_size(axis)
    pairs = [(i, i + by) for i in range(peers) if 0 <= i + by < peers]
    return lax.ppermute(value, axis, pairs)


def is_power_of_two(n):
    return n > 0 and n & (n - 1) == 0


def halve(value, dim, axis, flip, send_type):
    peers = lax.axis_size(axis)
    bit = (lax.axis_index(axis) // flip) % 2
    keep = lax.dynamic_index_in_dim(value, bit, dim, keepdims=False)
    send = lax.dynamic_index_in_dim(value, 1 - bit, dim, keepdims=False)
    pairs = [(i, i ^ flip) for i in range(peers)]
    return keep + lax.ppermute(send.astype(send_type), axis, pairs).astype(keep.dtype)


def swap_add(value, anchor, axis, flip):
    value, anchor = lax.optimization_barrier((value, anchor))
    peers = lax.axis_size(axis)
    pairs = [(i, i ^ flip) for i in range(peers)]
    return value + lax.ppermute(value, axis, pairs), anchor


def scatter_rows(value, tally, axes, first_axis, wire_type, tail_first=False, balance=True):
    sizes = [lax.axis_size(axis) for axis in axes]
    rows = value.shape[0]
    groups = math.prod(sizes)
    if not all(is_power_of_two(n) for n in sizes) or rows % groups:
        return (
            lax.psum_scatter(value, axes, scatter_dimension=0, tiled=True),
            None if tally is None else lax.psum(tally, axes),
        )
    stages = [
        (axis, 1 << (n.bit_length() - 2 - i))
        for axis, n in zip(axes, sizes)
        for i in range(n.bit_length() - 1)
    ]
    if not stages:
        return value, tally
    rest = value.shape[1:]
    value = value.reshape((2,) * len(stages) + (rows // groups,) + rest)
    names = list(stages)

    def step(part, part_names, stage, send_type):
        dim = part_names.index(stage)
        return halve(part, dim, *stage, send_type), part_names[:dim] + part_names[dim + 1 :]

    first = (first_axis, 1) if (first_axis, 1) in stages else stages[-1]
    def count_along(tally, anchor, stage):
        if tally is None:
            return tally, anchor
        return swap_add(tally, anchor, *stage)

    def run_tail(value, names, tally):
        for stage in tail:
            value, names = step(value, names, stage, wire_type)
            tally, value = count_along(tally, value, stage)
        return value, names, tally

    value, names = step(value, names, first, wire_type)
    tally, value = count_along(tally, value, first)
    middle = [s for s in stages if s[0] == first[0] and s != first]
    tail = [s for s in stages if s[0] != first[0]][::-1]
    if tail_first:
        value, names, tally = run_tail(value, names, tally)
    if balance and len(middle) > 1 and rest[-1] % 2 == 0:
        cut = rest[-1] // 2
        left, right = value[..., :cut], value[..., cut:]
        left_names, right_names = list(names), list(names)
        for a, b in zip(middle, middle[::-1]):
            left, left_names = step(left, left_names, a, wire_type)
            tally, left = count_along(tally, left, a)
            right, right_names = step(right, right_names, b, wire_type)
        value = jnp.concatenate([left, right], axis=-1)
        names = left_names
    else:
        for stage in middle:
            value, names = step(value, names, stage, wire_type)
            tally, value = count_along(tally, value, stage)
    if not tail_first:
        value, names, tally = run_tail(value, names, tally)
    return value, tally


def band_block(queries, keys_blk, values_blk, grad_attn, valid, inv_scale):
    scores = (
        jnp.einsum("qgc,kgc->gqk", queries, keys_blk, preferred_element_type=jnp.float32)
        * inv_scale
    )
    exp_terms = jnp.exp(scores) * valid[None]
    probs = exp_terms / jnp.sum(exp_terms, axis=-1, keepdims=True)
    probs_low = probs.astype(jnp.bfloat16)
    attended = jnp.einsum(
        "gqk,kgc->qgc", probs_low, values_blk, preferred_element_type=jnp.float32
    ).astype(jnp.bfloat16)
    delta = jnp.sum(grad_attn.astype(jnp.float32) * attended.astype(jnp.float32), axis=-1)
    grad_probs = jnp.einsum(
        "qgc,kgc->gqk", grad_attn, values_blk, preferred_element_type=jnp.float32
    )
    grad_scores = (probs * (grad_probs - jnp.transpose(delta)[:, :, None]) * inv_scale).astype(
        jnp.bfloat16
    )
    grad_query = jnp.einsum(
        "gqk,kgc->gcq", grad_scores, keys_blk, preferred_element_type=jnp.float32
    )
    grad_key = jnp.einsum("gqk,qgc->gck", grad_scores, queries, preferred_element_type=jnp.float32)
    grad_value = jnp.einsum(
        "gqk,qgc->gck", probs_low, grad_attn, preferred_element_type=jnp.float32
    )
    return (attended, grad_query, grad_key, grad_value)


def shards(patches, weights, cotangent, loss_mask):
    rows = patches.shape[1]
    width = patches.shape[2]
    inner = weights.shape[2]
    span = (WIN + rows - 2) // rows
    block_rows = min(512, rows)
    key_len = block_rows + span * rows
    group = HEADS
    group_cols = group * HSIZE
    inv_scale = 1.0 / math.sqrt(HSIZE)
    local_in = patches[0].astype(jnp.float32)
    inv_rms = lax.rsqrt(jnp.mean(local_in * local_in, axis=-1) + 1e-06)
    normed_full = local_in * inv_rms[:, None]
    normed = normed_full.astype(jnp.bfloat16)
    projected = jnp.einsum(
        "rd,dwh->wrh", normed, weights, preferred_element_type=jnp.float32
    ).astype(jnp.bfloat16)
    queries = projected[0]
    key_vals = projected[1:3]
    arrived = {offset: shifted(key_vals, "tm", offset) for offset in range(1, span + 1)}
    earlier = [arrived[offset] for offset in range(span, 0, -1)]
    extended = jnp.concatenate(earlier + [key_vals], axis=1)
    local_count = jnp.sum(loss_mask.astype(jnp.int32))
    tokens_all = rows * lax.axis_size("tm") * lax.axis_size("night")
    local_cot = cotangent[0]
    grad_out = jnp.where(loss_mask[0][:, None] > 0, local_cot, jnp.zeros_like(local_cot))
    grad_attn = jnp.einsum(
        "rd,dwh->wrh", grad_out, weights, preferred_element_type=jnp.float32
    )[3].astype(jnp.bfloat16)
    base = lax.axis_index("tm") * rows
    query_idx = jnp.arange(block_rows, dtype=jnp.int32)[:, None]
    key_idx = jnp.arange(key_len, dtype=jnp.int32)[None, :]
    offsets = query_idx - key_idx + span * rows
    band = (offsets >= 0) & (offsets < WIN)
    valid = (band & (key_idx >= span * rows - base)).astype(jnp.float32)
    attended, grad_query, grad_key, grad_value = band_block(
        queries.reshape(rows, HEADS, HSIZE),
        extended[0].reshape(key_len, HEADS, HSIZE),
        extended[1].reshape(key_len, HEADS, HSIZE),
        grad_attn.reshape(rows, HEADS, HSIZE),
        valid,
        inv_scale,
    )
    attended_all = attended.reshape(rows, inner)
    grad_q = grad_query.astype(jnp.bfloat16)
    query_part = jnp.einsum(
        "rd,gcr->dgc", normed, grad_q, preferred_element_type=jnp.float32
    ).reshape(width, inner)
    out_part = jnp.einsum("rd,rh->dh", grad_out, attended_all, preferred_element_type=jnp.float32)
    early_terms = jnp.stack([query_part, out_part], axis=1)
    blocks = lax.axis_size("tm") * lax.axis_size("night")
    block_rows_out = width // blocks
    bits = rows.bit_length()
    if width % blocks == 0 and block_rows_out % 8 == 0 and blocks <= 256 and bits <= inner:
        digits = (local_count // (2 ** jnp.arange(bits, dtype=jnp.int32))) % 2
        count_rows = jnp.zeros((blocks, 8) + early_terms.shape[1:], jnp.float32)
        count_rows = count_rows.at[:, 0, 0, :bits].set(digits.astype(jnp.float32))
        payload = jnp.concatenate(
            [early_terms.reshape((blocks, block_rows_out) + early_terms.shape[1:]), count_rows],
            axis=1,
        ).reshape((-1,) + early_terms.shape[1:])
        early, _ = scatter_rows(
            payload, None, ("tm", "night"), "tm", jnp.bfloat16, tail_first=True, balance=False
        )
        digit_sums = early[block_rows_out, 0, :bits].astype(jnp.int32)
        count = jnp.sum(digit_sums * (2 ** jnp.arange(bits, dtype=jnp.int32)))
        early = early[:block_rows_out]
    else:
        early, count = scatter_rows(
            early_terms, local_count, ("tm", "night"), "tm", jnp.bfloat16, tail_first=True
        )
    owned = jnp.stack([grad_key[..., span * rows :], grad_value[..., span * rows :]])
    for offset in range(1, span + 1):
        lower = (span - offset) * rows
        piece = jnp.stack(
            [grad_key[..., lower : lower + rows], grad_value[..., lower : lower + rows]]
        )
        owned = owned + shifted(piece.astype(jnp.bfloat16), "tm", -offset).astype(jnp.float32)
    grad_kv = owned.astype(jnp.bfloat16)
    grad_proj = jnp.concatenate([grad_q[None], grad_kv, jnp.zeros_like(grad_q)[None]], axis=0)
    grad_rows = grad_proj.transpose(0, 3, 1, 2).reshape(grad_proj.shape[0], rows, inner)
    grad_normed = jnp.einsum(
        "wrh,dwh->rd", grad_rows, weights, preferred_element_type=jnp.float32
    )
    along = jnp.sum(grad_normed * normed_full, axis=-1) / width
    unscaled_input = inv_rms[:, None] * (grad_normed - normed_full * along[:, None])
    key_value_part = jnp.einsum(
        "rd,wgcr->dwgc", normed, grad_proj[1:3], preferred_element_type=jnp.float32
    ).reshape(width, 2, inner)
    late, _ = scatter_rows(key_value_part, None, ("tm", "night"), "tm", jnp.bfloat16)
    summed = jnp.concatenate([early[:, :1], late, early[:, 1:]], axis=1)
    total_count = count.astype(jnp.float32)
    loss_scale = jnp.float32(tokens_all) / total_count
    grad_input = (loss_scale * unscaled_input).astype(jnp.bfloat16)
    grad_weights = summed * (jnp.sqrt(jnp.float32(tokens_all)) / total_count)
    return (grad_input[None], grad_weights)


def solution(mesh):
    return jax.shard_map(
        shards,
        mesh=mesh,
        in_specs=(P("night", "tm", None), P(), P("night", "tm", None), P("night", "tm")),
        out_specs=(P("night", "tm", None), P(("tm", "night"), None, None)),
        check_vma=False,
    )
```

```python
import math

import jax
import jax.numpy as jnp
from jax import lax
from jax.sharding import PartitionSpec as P

HEADS = 8
HSIZE = 64
WIN = 1024


def shifted(value, axis, by):
    peers = lax.axis_size(axis)
    pairs = [(i, i + by) for i in range(peers) if 0 <= i + by < peers]
    return lax.ppermute(value, axis, pairs)


def is_power_of_two(n):
    return n > 0 and n & (n - 1) == 0


def halve(value, dim, axis, flip, send_type):
    peers = lax.axis_size(axis)
    bit = (lax.axis_index(axis) // flip) % 2
    keep = lax.dynamic_index_in_dim(value, bit, dim, keepdims=False)
    send = lax.dynamic_index_in_dim(value, 1 - bit, dim, keepdims=False)
    pairs = [(i, i ^ flip) for i in range(peers)]
    return keep + lax.ppermute(send.astype(send_type), axis, pairs).astype(keep.dtype)


def swap_add(value, anchor, axis, flip):
    value, anchor = lax.optimization_barrier((value, anchor))
    peers = lax.axis_size(axis)
    pairs = [(i, i ^ flip) for i in range(peers)]
    return value + lax.ppermute(value, axis, pairs), anchor


def scatter_rows(value, tally, axes, first_axis, wire_type, tail_first=False, balance=True):
    sizes = [lax.axis_size(axis) for axis in axes]
    rows = value.shape[0]
    groups = math.prod(sizes)
    if not all(is_power_of_two(n) for n in sizes) or rows % groups:
        return (
            lax.psum_scatter(value, axes, scatter_dimension=0, tiled=True),
            None if tally is None else lax.psum(tally, axes),
        )
    stages = [
        (axis, 1 << (n.bit_length() - 2 - i))
        for axis, n in zip(axes, sizes)
        for i in range(n.bit_length() - 1)
    ]
    if not stages:
        return value, tally
    rest = value.shape[1:]
    value = value.reshape((2,) * len(stages) + (rows // groups,) + rest)
    names = list(stages)

    def step(part, part_names, stage, send_type):
        dim = part_names.index(stage)
        return halve(part, dim, *stage, send_type), part_names[:dim] + part_names[dim + 1 :]

    first = (first_axis, 1) if (first_axis, 1) in stages else stages[-1]
    def count_along(tally, anchor, stage):
        if tally is None:
            return tally, anchor
        return swap_add(tally, anchor, *stage)

    def run_tail(value, names, tally):
        for stage in tail:
            value, names = step(value, names, stage, wire_type)
            tally, value = count_along(tally, value, stage)
        return value, names, tally

    value, names = step(value, names, first, wire_type)
    tally, value = count_along(tally, value, first)
    middle = [s for s in stages if s[0] == first[0] and s != first]
    tail = [s for s in stages if s[0] != first[0]][::-1]
    if tail_first:
        value, names, tally = run_tail(value, names, tally)
    if balance and len(middle) > 1 and rest[-1] % 2 == 0:
        cut = rest[-1] // 2
        left, right = value[..., :cut], value[..., cut:]
        left_names, right_names = list(names), list(names)
        for a, b in zip(middle, middle[::-1]):
            left, left_names = step(left, left_names, a, wire_type)
            tally, left = count_along(tally, left, a)
            right, right_names = step(right, right_names, b, wire_type)
        value = jnp.concatenate([left, right], axis=-1)
        names = left_names
    else:
        for stage in middle:
            value, names = step(value, names, stage, wire_type)
            tally, value = count_along(tally, value, stage)
    if not tail_first:
        value, names, tally = run_tail(value, names, tally)
    return value, tally


def band_block(queries, keys_blk, values_blk, grad_attn, valid, inv_scale):
    scores = (
        jnp.einsum("qgc,kgc->gqk", queries, keys_blk, preferred_element_type=jnp.float32)
        * inv_scale
    )
    exp_terms = jnp.exp(scores) * valid[None]
    probs = exp_terms / jnp.sum(exp_terms, axis=-1, keepdims=True)
    probs_low = probs.astype(jnp.bfloat16)
    attended = jnp.einsum(
        "gqk,kgc->qgc", probs_low, values_blk, preferred_element_type=jnp.float32
    ).astype(jnp.bfloat16)
    delta = jnp.sum(grad_attn.astype(jnp.float32) * attended.astype(jnp.float32), axis=-1)
    grad_probs = jnp.einsum(
        "qgc,kgc->gqk", grad_attn, values_blk, preferred_element_type=jnp.float32
    )
    grad_scores = (probs * (grad_probs - jnp.transpose(delta)[:, :, None]) * inv_scale).astype(
        jnp.bfloat16
    )
    grad_query = jnp.einsum(
        "gqk,kgc->gcq", grad_scores, keys_blk, preferred_element_type=jnp.float32
    )
    grad_key = jnp.einsum("gqk,qgc->gck", grad_scores, queries, preferred_element_type=jnp.float32)
    grad_value = jnp.einsum(
        "gqk,qgc->gck", probs_low, grad_attn, preferred_element_type=jnp.float32
    )
    return (attended, grad_query, grad_key, grad_value)


def shards(patches, weights, cotangent, loss_mask):
    rows = patches.shape[1]
    width = patches.shape[2]
    inner = weights.shape[2]
    span = (WIN + rows - 2) // rows
    block_rows = min(512, rows)
    key_len = block_rows + span * rows
    group = HEADS
    group_cols = group * HSIZE
    inv_scale = 1.0 / math.sqrt(HSIZE)
    local_in = patches[0].astype(jnp.float32)
    inv_rms = lax.rsqrt(jnp.mean(local_in * local_in, axis=-1) + 1e-06)
    normed_full = local_in * inv_rms[:, None]
    normed = normed_full.astype(jnp.bfloat16)
    local_cot = cotangent[0]
    grad_out = jnp.where(loss_mask[0][:, None] > 0, local_cot, jnp.zeros_like(local_cot))
    both = jnp.einsum(
        "rd,dwh->wrh",
        jnp.concatenate([normed, grad_out], axis=0),
        weights,
        preferred_element_type=jnp.float32,
    ).astype(jnp.bfloat16)
    projected = both[:, :rows]
    grad_attn = both[3, rows:]
    queries = projected[0]
    key_vals = projected[1:3]
    arrived = {offset: shifted(key_vals, "tm", offset) for offset in range(1, span + 1)}
    earlier = [arrived[offset] for offset in range(span, 0, -1)]
    extended = jnp.concatenate(earlier + [key_vals], axis=1)
    local_count = jnp.sum(loss_mask.astype(jnp.int32))
    tokens_all = rows * lax.axis_size("tm") * lax.axis_size("night")
    base = lax.axis_index("tm") * rows
    query_idx = jnp.arange(block_rows, dtype=jnp.int32)[:, None]
    key_idx = jnp.arange(key_len, dtype=jnp.int32)[None, :]
    offsets = query_idx - key_idx + span * rows
    band = (offsets >= 0) & (offsets < WIN)
    valid = (band & (key_idx >= span * rows - base)).astype(jnp.float32)
    attended, grad_query, grad_key, grad_value = band_block(
        queries.reshape(rows, HEADS, HSIZE),
        extended[0].reshape(key_len, HEADS, HSIZE),
        extended[1].reshape(key_len, HEADS, HSIZE),
        grad_attn.reshape(rows, HEADS, HSIZE),
        valid,
        inv_scale,
    )
    attended_all = attended.reshape(rows, inner)
    grad_q = grad_query.astype(jnp.bfloat16)
    query_part = jnp.einsum(
        "rd,gcr->dgc", normed, grad_q, preferred_element_type=jnp.float32
    ).reshape(width, inner)
    out_part = jnp.einsum("rd,rh->dh", grad_out, attended_all, preferred_element_type=jnp.float32)
    early_terms = jnp.stack([query_part, out_part], axis=1)
    blocks = lax.axis_size("tm") * lax.axis_size("night")
    block_rows_out = width // blocks
    bits = rows.bit_length()
    if width % blocks == 0 and block_rows_out % 8 == 0 and blocks <= 256 and bits <= inner:
        digits = (local_count // (2 ** jnp.arange(bits, dtype=jnp.int32))) % 2
        count_rows = jnp.zeros((blocks, 8) + early_terms.shape[1:], jnp.float32)
        count_rows = count_rows.at[:, 0, 0, :bits].set(digits.astype(jnp.float32))
        payload = jnp.concatenate(
            [early_terms.reshape((blocks, block_rows_out) + early_terms.shape[1:]), count_rows],
            axis=1,
        ).reshape((-1,) + early_terms.shape[1:])
        early, _ = scatter_rows(
            payload, None, ("tm", "night"), "tm", jnp.bfloat16, tail_first=True, balance=False
        )
        digit_sums = early[block_rows_out, 0, :bits].astype(jnp.int32)
        count = jnp.sum(digit_sums * (2 ** jnp.arange(bits, dtype=jnp.int32)))
        early = early[:block_rows_out]
    else:
        early, count = scatter_rows(
            early_terms, local_count, ("tm", "night"), "tm", jnp.bfloat16, tail_first=True
        )
    owned = jnp.stack([grad_key[..., span * rows :], grad_value[..., span * rows :]])
    for offset in range(1, span + 1):
        lower = (span - offset) * rows
        piece = jnp.stack(
            [grad_key[..., lower : lower + rows], grad_value[..., lower : lower + rows]]
        )
        owned = owned + shifted(piece.astype(jnp.bfloat16), "tm", -offset).astype(jnp.float32)
    grad_kv = owned.astype(jnp.bfloat16)
    grad_proj = jnp.concatenate([grad_q[None], grad_kv, jnp.zeros_like(grad_q)[None]], axis=0)
    grad_rows = grad_proj.transpose(0, 3, 1, 2).reshape(grad_proj.shape[0], rows, inner)
    grad_normed = jnp.einsum(
        "wrh,dwh->rd", grad_rows, weights, preferred_element_type=jnp.float32
    )
    along = jnp.sum(grad_normed * normed_full, axis=-1) / width
    unscaled_input = inv_rms[:, None] * (grad_normed - normed_full * along[:, None])
    key_value_part = jnp.einsum(
        "rd,wgcr->dwgc", normed, grad_proj[1:3], preferred_element_type=jnp.float32
    ).reshape(width, 2, inner)
    late, _ = scatter_rows(key_value_part, None, ("tm", "night"), "tm", jnp.bfloat16)
    summed = jnp.concatenate([early[:, :1], late, early[:, 1:]], axis=1)
    total_count = count.astype(jnp.float32)
    loss_scale = jnp.float32(tokens_all) / total_count
    grad_input = (loss_scale * unscaled_input).astype(jnp.bfloat16)
    grad_weights = summed * (jnp.sqrt(jnp.float32(tokens_all)) / total_count)
    return (grad_input[None], grad_weights)


def solution(mesh):
    return jax.shard_map(
        shards,
        mesh=mesh,
        in_specs=(P("night", "tm", None), P(), P("night", "tm", None), P("night", "tm")),
        out_specs=(P("night", "tm", None), P(("tm", "night"), None, None)),
        check_vma=False,
    )
```

```python
import math

import jax
import jax.numpy as jnp
from jax import lax
from jax.sharding import PartitionSpec as P

HEADS = 8
HSIZE = 64
WIN = 1024


def shifted(value, axis, by):
    peers = lax.axis_size(axis)
    pairs = [(i, i + by) for i in range(peers) if 0 <= i + by < peers]
    return lax.ppermute(value, axis, pairs)


def is_power_of_two(n):
    return n > 0 and n & (n - 1) == 0


def halve(value, dim, axis, flip, send_type):
    peers = lax.axis_size(axis)
    bit = (lax.axis_index(axis) // flip) % 2
    keep = lax.dynamic_index_in_dim(value, bit, dim, keepdims=False)
    send = lax.dynamic_index_in_dim(value, 1 - bit, dim, keepdims=False)
    pairs = [(i, i ^ flip) for i in range(peers)]
    return keep + lax.ppermute(send.astype(send_type), axis, pairs).astype(keep.dtype)


def swap_add(value, anchor, axis, flip):
    value, anchor = lax.optimization_barrier((value, anchor))
    peers = lax.axis_size(axis)
    pairs = [(i, i ^ flip) for i in range(peers)]
    return value + lax.ppermute(value, axis, pairs), anchor


def scatter_rows(value, tally, axes, first_axis, wire_type, tail_first=False, balance=True):
    sizes = [lax.axis_size(axis) for axis in axes]
    rows = value.shape[0]
    groups = math.prod(sizes)
    if not all(is_power_of_two(n) for n in sizes) or rows % groups:
        return (
            lax.psum_scatter(value, axes, scatter_dimension=0, tiled=True),
            None if tally is None else lax.psum(tally, axes),
        )
    stages = [
        (axis, 1 << (n.bit_length() - 2 - i))
        for axis, n in zip(axes, sizes)
        for i in range(n.bit_length() - 1)
    ]
    if not stages:
        return value, tally
    rest = value.shape[1:]
    value = value.reshape((2,) * len(stages) + (rows // groups,) + rest)
    names = list(stages)

    def step(part, part_names, stage, send_type):
        dim = part_names.index(stage)
        return halve(part, dim, *stage, send_type), part_names[:dim] + part_names[dim + 1 :]

    first = (first_axis, 1) if (first_axis, 1) in stages else stages[-1]
    def count_along(tally, anchor, stage):
        if tally is None:
            return tally, anchor
        return swap_add(tally, anchor, *stage)

    def run_tail(value, names, tally):
        for stage in tail:
            value, names = step(value, names, stage, wire_type)
            tally, value = count_along(tally, value, stage)
        return value, names, tally

    value, names = step(value, names, first, wire_type)
    tally, value = count_along(tally, value, first)
    middle = [s for s in stages if s[0] == first[0] and s != first]
    tail = [s for s in stages if s[0] != first[0]][::-1]
    if tail_first:
        value, names, tally = run_tail(value, names, tally)
    if balance and len(middle) > 1 and rest[-1] % 2 == 0:
        cut = rest[-1] // 2
        left, right = value[..., :cut], value[..., cut:]
        left_names, right_names = list(names), list(names)
        for a, b in zip(middle, middle[::-1]):
            left, left_names = step(left, left_names, a, wire_type)
            tally, left = count_along(tally, left, a)
            right, right_names = step(right, right_names, b, wire_type)
        value = jnp.concatenate([left, right], axis=-1)
        names = left_names
    else:
        for stage in middle:
            value, names = step(value, names, stage, wire_type)
            tally, value = count_along(tally, value, stage)
    if not tail_first:
        value, names, tally = run_tail(value, names, tally)
    return value, tally


def band_block(queries, keys_blk, values_blk, grad_attn, valid, inv_scale):
    scores = (
        jnp.einsum("qgc,kgc->gqk", queries, keys_blk, preferred_element_type=jnp.float32)
        * inv_scale
    )
    exp_terms = jnp.exp(scores) * valid[None]
    probs = exp_terms / jnp.sum(exp_terms, axis=-1, keepdims=True)
    probs_low = probs.astype(jnp.bfloat16)
    attended = jnp.einsum(
        "gqk,kgc->qgc", probs_low, values_blk, preferred_element_type=jnp.float32
    ).astype(jnp.bfloat16)
    delta = jnp.sum(grad_attn.astype(jnp.float32) * attended.astype(jnp.float32), axis=-1)
    grad_probs = jnp.einsum(
        "qgc,kgc->gqk", grad_attn, values_blk, preferred_element_type=jnp.float32
    )
    grad_scores = (probs * (grad_probs - jnp.transpose(delta)[:, :, None]) * inv_scale).astype(
        jnp.bfloat16
    )
    grad_query = jnp.einsum(
        "gqk,kgc->gcq", grad_scores, keys_blk, preferred_element_type=jnp.float32
    )
    grad_key = jnp.einsum("gqk,qgc->gck", grad_scores, queries, preferred_element_type=jnp.float32)
    grad_value = jnp.einsum(
        "gqk,qgc->gck", probs_low, grad_attn, preferred_element_type=jnp.float32
    )
    return (attended, grad_query, grad_key, grad_value)


def shards(patches, weights, cotangent, loss_mask):
    rows = patches.shape[1]
    width = patches.shape[2]
    inner = weights.shape[2]
    span = (WIN + rows - 2) // rows
    block_rows = min(512, rows)
    key_len = block_rows + span * rows
    group = HEADS
    group_cols = group * HSIZE
    inv_scale = 1.0 / math.sqrt(HSIZE)
    local_in = patches[0].astype(jnp.float32)
    inv_rms = lax.rsqrt(jnp.mean(local_in * local_in, axis=-1) + 1e-06)
    normed_full = local_in * inv_rms[:, None]
    normed = normed_full.astype(jnp.bfloat16)
    projected = jnp.einsum(
        "rd,dwh->wrh", normed, weights, preferred_element_type=jnp.float32
    ).astype(jnp.bfloat16)
    queries = projected[0]
    key_vals = projected[1:3]
    arrived = {offset: shifted(key_vals, "tm", offset) for offset in range(1, span + 1)}
    earlier = [arrived[offset] for offset in range(span, 0, -1)]
    extended = jnp.concatenate(earlier + [key_vals], axis=1)
    local_count = jnp.sum(loss_mask.astype(jnp.int32))
    tokens_all = rows * lax.axis_size("tm") * lax.axis_size("night")
    local_cot = cotangent[0]
    grad_out = jnp.where(loss_mask[0][:, None] > 0, local_cot, jnp.zeros_like(local_cot))
    grad_attn = jnp.einsum(
        "rd,dwh->wrh", grad_out, weights, preferred_element_type=jnp.float32
    )[3].astype(jnp.bfloat16)
    base = lax.axis_index("tm") * rows
    query_idx = jnp.arange(block_rows, dtype=jnp.int32)[:, None]
    key_idx = jnp.arange(key_len, dtype=jnp.int32)[None, :]
    offsets = query_idx - key_idx + span * rows
    band = (offsets >= 0) & (offsets < WIN)
    valid = (band & (key_idx >= span * rows - base)).astype(jnp.float32)
    attended, grad_query, grad_key, grad_value = band_block(
        queries.reshape(rows, HEADS, HSIZE),
        extended[0].reshape(key_len, HEADS, HSIZE),
        extended[1].reshape(key_len, HEADS, HSIZE),
        grad_attn.reshape(rows, HEADS, HSIZE),
        valid,
        inv_scale,
    )
    attended_all = attended.reshape(rows, inner)
    grad_q = grad_query.astype(jnp.bfloat16)
    query_part = jnp.einsum(
        "rd,gcr->dgc", normed, grad_q, preferred_element_type=jnp.float32
    ).reshape(width, inner)
    out_part = jnp.einsum("rd,rh->dh", grad_out, attended_all, preferred_element_type=jnp.float32)
    early_terms = jnp.stack([query_part, out_part], axis=1)
    blocks = lax.axis_size("tm") * lax.axis_size("night")
    block_rows_out = width // blocks
    bits = rows.bit_length()
    if width % blocks == 0 and block_rows_out % 8 == 0 and blocks <= 256 and bits <= inner:
        digits = (local_count // (2 ** jnp.arange(bits, dtype=jnp.int32))) % 2
        count_rows = jnp.zeros((blocks, 8) + early_terms.shape[1:], jnp.float32)
        count_rows = count_rows.at[:, 0, 0, :bits].set(digits.astype(jnp.float32))
        payload = jnp.concatenate(
            [early_terms.reshape((blocks, block_rows_out) + early_terms.shape[1:]), count_rows],
            axis=1,
        ).reshape((-1,) + early_terms.shape[1:])
        early, _ = scatter_rows(
            payload, None, ("tm", "night"), "tm", jnp.bfloat16, tail_first=True, balance=False
        )
        digit_sums = early[block_rows_out, 0, :bits].astype(jnp.int32)
        count = jnp.sum(digit_sums * (2 ** jnp.arange(bits, dtype=jnp.int32)))
        early = early[:block_rows_out]
    else:
        early, count = scatter_rows(
            early_terms, local_count, ("tm", "night"), "tm", jnp.bfloat16, tail_first=True
        )
    owned = jnp.stack([grad_key[..., span * rows :], grad_value[..., span * rows :]])
    for offset in range(1, span + 1):
        lower = (span - offset) * rows
        piece = jnp.stack(
            [grad_key[..., lower : lower + rows], grad_value[..., lower : lower + rows]]
        )
        owned = owned + shifted(piece.astype(jnp.bfloat16), "tm", -offset).astype(jnp.float32)
    grad_kv = owned.astype(jnp.bfloat16)
    grad_proj = jnp.concatenate([grad_q[None], grad_kv, jnp.zeros_like(grad_q)[None]], axis=0)
    grad_rows = grad_proj.transpose(0, 3, 1, 2).reshape(grad_proj.shape[0], rows, inner)
    grad_normed = jnp.einsum(
        "wrh,dwh->rd", grad_rows, weights, preferred_element_type=jnp.float32
    )
    along = jnp.sum(grad_normed * normed_full, axis=-1) / width
    unscaled_input = inv_rms[:, None] * (grad_normed - normed_full * along[:, None])
    key_value_part = jnp.einsum(
        "rd,wgcr->dwgc", normed, grad_proj[1:3], preferred_element_type=jnp.float32
    ).reshape(width, 2, inner)
    late, _ = scatter_rows(
        key_value_part, None, ("tm", "night"), "tm", jnp.bfloat16, tail_first=True
    )
    summed = jnp.concatenate([early[:, :1], late, early[:, 1:]], axis=1)
    total_count = count.astype(jnp.float32)
    loss_scale = jnp.float32(tokens_all) / total_count
    grad_input = (loss_scale * unscaled_input).astype(jnp.bfloat16)
    grad_weights = summed * (jnp.sqrt(jnp.float32(tokens_all)) / total_count)
    return (grad_input[None], grad_weights)


def solution(mesh):
    return jax.shard_map(
        shards,
        mesh=mesh,
        in_specs=(P("night", "tm", None), P(), P("night", "tm", None), P("night", "tm")),
        out_specs=(P("night", "tm", None), P(("tm", "night"), None, None)),
        check_vma=False,
    )
```

```python
import math

import jax
import jax.numpy as jnp
from jax import lax
from jax.sharding import PartitionSpec as P

HEADS = 8
HSIZE = 64
WIN = 1024


def shifted(value, axis, by):
    peers = lax.axis_size(axis)
    pairs = [(i, i + by) for i in range(peers) if 0 <= i + by < peers]
    return lax.ppermute(value, axis, pairs)


def is_power_of_two(n):
    return n > 0 and n & (n - 1) == 0


def halve(value, dim, axis, flip, send_type):
    peers = lax.axis_size(axis)
    bit = (lax.axis_index(axis) // flip) % 2
    keep = lax.dynamic_index_in_dim(value, bit, dim, keepdims=False)
    send = lax.dynamic_index_in_dim(value, 1 - bit, dim, keepdims=False)
    pairs = [(i, i ^ flip) for i in range(peers)]
    return keep + lax.ppermute(send.astype(send_type), axis, pairs).astype(keep.dtype)


def swap_add(value, anchor, axis, flip):
    value, anchor = lax.optimization_barrier((value, anchor))
    peers = lax.axis_size(axis)
    pairs = [(i, i ^ flip) for i in range(peers)]
    return value + lax.ppermute(value, axis, pairs), anchor


def scatter_rows(value, tally, axes, first_axis, wire_type, tail_first=False, balance=True):
    sizes = [lax.axis_size(axis) for axis in axes]
    rows = value.shape[0]
    groups = math.prod(sizes)
    if not all(is_power_of_two(n) for n in sizes) or rows % groups:
        return (
            lax.psum_scatter(value, axes, scatter_dimension=0, tiled=True),
            None if tally is None else lax.psum(tally, axes),
        )
    stages = [
        (axis, 1 << (n.bit_length() - 2 - i))
        for axis, n in zip(axes, sizes)
        for i in range(n.bit_length() - 1)
    ]
    if not stages:
        return value, tally
    rest = value.shape[1:]
    value = value.reshape((2,) * len(stages) + (rows // groups,) + rest)
    names = list(stages)

    def step(part, part_names, stage, send_type):
        dim = part_names.index(stage)
        return halve(part, dim, *stage, send_type), part_names[:dim] + part_names[dim + 1 :]

    first = (first_axis, 1) if (first_axis, 1) in stages else stages[-1]
    def count_along(tally, anchor, stage):
        if tally is None:
            return tally, anchor
        return swap_add(tally, anchor, *stage)

    def run_tail(value, names, tally):
        for stage in tail:
            value, names = step(value, names, stage, wire_type)
            tally, value = count_along(tally, value, stage)
        return value, names, tally

    value, names = step(value, names, first, wire_type)
    tally, value = count_along(tally, value, first)
    middle = [s for s in stages if s[0] == first[0] and s != first]
    tail = [s for s in stages if s[0] != first[0]][::-1]
    if tail_first:
        value, names, tally = run_tail(value, names, tally)
    if balance and len(middle) > 1 and rest[-1] % 2 == 0:
        cut = rest[-1] // 2
        left, right = value[..., :cut], value[..., cut:]
        left_names, right_names = list(names), list(names)
        for a, b in zip(middle, middle[::-1]):
            left, left_names = step(left, left_names, a, wire_type)
            tally, left = count_along(tally, left, a)
            right, right_names = step(right, right_names, b, wire_type)
        value = jnp.concatenate([left, right], axis=-1)
        names = left_names
    else:
        for stage in middle:
            value, names = step(value, names, stage, wire_type)
            tally, value = count_along(tally, value, stage)
    if not tail_first:
        value, names, tally = run_tail(value, names, tally)
    return value, tally


def band_block(queries, keys_blk, values_blk, grad_attn, valid, inv_scale):
    scores = (
        jnp.einsum("qgc,kgc->gqk", queries, keys_blk, preferred_element_type=jnp.float32)
        * inv_scale
    )
    exp_terms = jnp.exp(scores) * valid[None]
    probs = exp_terms / jnp.sum(exp_terms, axis=-1, keepdims=True)
    probs_low = probs.astype(jnp.bfloat16)
    attended = jnp.einsum(
        "gqk,kgc->qgc", probs_low, values_blk, preferred_element_type=jnp.float32
    ).astype(jnp.bfloat16)
    delta = jnp.sum(grad_attn.astype(jnp.float32) * attended.astype(jnp.float32), axis=-1)
    grad_probs = jnp.einsum(
        "qgc,kgc->gqk", grad_attn, values_blk, preferred_element_type=jnp.float32
    )
    grad_scores = (probs * (grad_probs - jnp.transpose(delta)[:, :, None]) * inv_scale).astype(
        jnp.bfloat16
    )
    grad_query = jnp.einsum(
        "gqk,kgc->gcq", grad_scores, keys_blk, preferred_element_type=jnp.float32
    )
    grad_key = jnp.einsum("gqk,qgc->gck", grad_scores, queries, preferred_element_type=jnp.float32)
    grad_value = jnp.einsum(
        "gqk,qgc->gck", probs_low, grad_attn, preferred_element_type=jnp.float32
    )
    return (attended, grad_query, grad_key, grad_value)


def shards(patches, weights, cotangent, loss_mask):
    rows = patches.shape[1]
    width = patches.shape[2]
    inner = weights.shape[2]
    span = (WIN + rows - 2) // rows
    block_rows = min(512, rows)
    key_len = block_rows + span * rows
    group = HEADS
    group_cols = group * HSIZE
    inv_scale = 1.0 / math.sqrt(HSIZE)
    local_in = patches[0].astype(jnp.float32)
    inv_rms = lax.rsqrt(jnp.mean(local_in * local_in, axis=-1) + 1e-06)
    normed_full = local_in * inv_rms[:, None]
    normed = normed_full.astype(jnp.bfloat16)
    projected = jnp.einsum(
        "rd,dwh->wrh", normed, weights, preferred_element_type=jnp.float32
    ).astype(jnp.bfloat16)
    queries = projected[0]
    key_vals = projected[1:3]
    arrived = {offset: shifted(key_vals, "tm", offset) for offset in range(1, span + 1)}
    earlier = [arrived[offset] for offset in range(span, 0, -1)]
    extended = jnp.concatenate(earlier + [key_vals], axis=1)
    local_count = jnp.sum(loss_mask.astype(jnp.int32))
    tokens_all = rows * lax.axis_size("tm") * lax.axis_size("night")
    local_cot = cotangent[0]
    grad_out = jnp.where(loss_mask[0][:, None] > 0, local_cot, jnp.zeros_like(local_cot))
    grad_attn = jnp.einsum(
        "rd,dwh->wrh", grad_out, weights, preferred_element_type=jnp.float32
    )[3].astype(jnp.bfloat16)
    base = lax.axis_index("tm") * rows
    query_idx = jnp.arange(block_rows, dtype=jnp.int32)[:, None]
    key_idx = jnp.arange(key_len, dtype=jnp.int32)[None, :]
    offsets = query_idx - key_idx + span * rows
    band = (offsets >= 0) & (offsets < WIN)
    valid = (band & (key_idx >= span * rows - base)).astype(jnp.float32)
    attended, grad_query, grad_key, grad_value = band_block(
        queries.reshape(rows, HEADS, HSIZE),
        extended[0].reshape(key_len, HEADS, HSIZE),
        extended[1].reshape(key_len, HEADS, HSIZE),
        grad_attn.reshape(rows, HEADS, HSIZE),
        valid,
        inv_scale,
    )
    attended_all = attended.reshape(rows, inner)
    grad_q = grad_query.astype(jnp.bfloat16)
    query_part = jnp.einsum(
        "rd,gcr->dgc", normed, grad_q, preferred_element_type=jnp.float32
    ).reshape(width, inner)
    out_part = jnp.einsum("rd,rh->dh", grad_out, attended_all, preferred_element_type=jnp.float32)
    early_terms = jnp.stack([query_part, out_part], axis=1)
    blocks = lax.axis_size("tm") * lax.axis_size("night")
    block_rows_out = width // blocks
    bits = rows.bit_length()
    if width % blocks == 0 and block_rows_out % 8 == 0 and blocks <= 256 and bits <= inner:
        digits = (local_count // (2 ** jnp.arange(bits, dtype=jnp.int32))) % 2
        count_rows = jnp.zeros((blocks, 8) + early_terms.shape[1:], jnp.float32)
        count_rows = count_rows.at[:, 0, 0, :bits].set(digits.astype(jnp.float32))
        payload = jnp.concatenate(
            [early_terms.reshape((blocks, block_rows_out) + early_terms.shape[1:]), count_rows],
            axis=1,
        ).reshape((-1,) + early_terms.shape[1:])
        early, _ = scatter_rows(
            payload, None, ("tm", "night"), "tm", jnp.bfloat16, tail_first=True, balance=False
        )
        digit_sums = early[block_rows_out, 0, :bits].astype(jnp.int32)
        count = jnp.sum(digit_sums * (2 ** jnp.arange(bits, dtype=jnp.int32)))
        early = early[:block_rows_out]
    else:
        early, count = scatter_rows(
            early_terms, local_count, ("tm", "night"), "tm", jnp.bfloat16, tail_first=True
        )
    owned = jnp.stack([grad_key[..., span * rows :], grad_value[..., span * rows :]])
    for offset in range(1, span + 1):
        lower = (span - offset) * rows
        piece = jnp.stack(
            [grad_key[..., lower : lower + rows], grad_value[..., lower : lower + rows]]
        )
        owned = owned + shifted(piece.astype(jnp.bfloat16), "tm", -offset).astype(jnp.float32)
    grad_kv = owned.astype(jnp.bfloat16)
    grad_proj = jnp.concatenate([grad_q[None], grad_kv, jnp.zeros_like(grad_q)[None]], axis=0)
    grad_rows = grad_proj.transpose(0, 3, 1, 2).reshape(grad_proj.shape[0], rows, inner)
    grad_normed = jnp.einsum(
        "wrh,dwh->rd", grad_rows, weights, preferred_element_type=jnp.float32
    )
    along = jnp.sum(grad_normed * normed_full, axis=-1) / width
    centred_grad = grad_normed - normed_full * along[:, None]
    key_value_part = jnp.einsum(
        "rd,wgcr->dwgc", normed, grad_proj[1:3], preferred_element_type=jnp.float32
    ).reshape(width, 2, inner)
    late, _ = scatter_rows(key_value_part, None, ("tm", "night"), "tm", jnp.bfloat16)
    summed = jnp.concatenate([early[:, :1], late, early[:, 1:]], axis=1)
    total_count = count.astype(jnp.float32)
    loss_scale = jnp.float32(tokens_all) / total_count
    grad_input = (loss_scale * inv_rms[:, None] * centred_grad).astype(jnp.bfloat16)
    grad_weights = summed * (jnp.sqrt(jnp.float32(tokens_all)) / total_count)
    return (grad_input[None], grad_weights)


def solution(mesh):
    return jax.shard_map(
        shards,
        mesh=mesh,
        in_specs=(P("night", "tm", None), P(), P("night", "tm", None), P("night", "tm")),
        out_specs=(P("night", "tm", None), P(("tm", "night"), None, None)),
        check_vma=False,
    )
```

```python
import math

import jax
import jax.numpy as jnp
from jax import lax
from jax.sharding import PartitionSpec as P

HEADS = 8
HSIZE = 64
WIN = 1024


def shifted(value, axis, by):
    peers = lax.axis_size(axis)
    pairs = [(i, i + by) for i in range(peers) if 0 <= i + by < peers]
    return lax.ppermute(value, axis, pairs)


def is_power_of_two(n):
    return n > 0 and n & (n - 1) == 0


def halve(value, dim, axis, flip, send_type):
    peers = lax.axis_size(axis)
    bit = (lax.axis_index(axis) // flip) % 2
    keep = lax.dynamic_index_in_dim(value, bit, dim, keepdims=False)
    send = lax.dynamic_index_in_dim(value, 1 - bit, dim, keepdims=False)
    pairs = [(i, i ^ flip) for i in range(peers)]
    return keep + lax.ppermute(send.astype(send_type), axis, pairs).astype(keep.dtype)


def swap_add(value, anchor, axis, flip):
    value, anchor = lax.optimization_barrier((value, anchor))
    peers = lax.axis_size(axis)
    pairs = [(i, i ^ flip) for i in range(peers)]
    return value + lax.ppermute(value, axis, pairs), anchor


def scatter_rows(value, tally, axes, first_axis, wire_type, tail_first=False, balance=True):
    sizes = [lax.axis_size(axis) for axis in axes]
    rows = value.shape[0]
    groups = math.prod(sizes)
    if not all(is_power_of_two(n) for n in sizes) or rows % groups:
        return (
            lax.psum_scatter(value, axes, scatter_dimension=0, tiled=True),
            None if tally is None else lax.psum(tally, axes),
        )
    stages = [
        (axis, 1 << (n.bit_length() - 2 - i))
        for axis, n in zip(axes, sizes)
        for i in range(n.bit_length() - 1)
    ]
    if not stages:
        return value, tally
    rest = value.shape[1:]
    value = value.reshape((2,) * len(stages) + (rows // groups,) + rest)
    names = list(stages)

    def step(part, part_names, stage, send_type):
        dim = part_names.index(stage)
        return halve(part, dim, *stage, send_type), part_names[:dim] + part_names[dim + 1 :]

    first = (first_axis, 1) if (first_axis, 1) in stages else stages[-1]
    def count_along(tally, anchor, stage):
        if tally is None:
            return tally, anchor
        return swap_add(tally, anchor, *stage)

    def run_tail(value, names, tally):
        for stage in tail:
            value, names = step(value, names, stage, wire_type)
            tally, value = count_along(tally, value, stage)
        return value, names, tally

    value, names = step(value, names, first, wire_type)
    tally, value = count_along(tally, value, first)
    middle = [s for s in stages if s[0] == first[0] and s != first]
    tail = [s for s in stages if s[0] != first[0]][::-1]
    if tail_first:
        value, names, tally = run_tail(value, names, tally)
    if balance and len(middle) > 1 and rest[-1] % 2 == 0:
        cut = rest[-1] // 2
        left, right = value[..., :cut], value[..., cut:]
        left_names, right_names = list(names), list(names)
        for a, b in zip(middle, middle[::-1]):
            left, left_names = step(left, left_names, a, wire_type)
            tally, left = count_along(tally, left, a)
            right, right_names = step(right, right_names, b, wire_type)
        value = jnp.concatenate([left, right], axis=-1)
        names = left_names
    else:
        for stage in middle:
            value, names = step(value, names, stage, wire_type)
            tally, value = count_along(tally, value, stage)
    if not tail_first:
        value, names, tally = run_tail(value, names, tally)
    return value, tally


def band_block(queries, keys_blk, values_blk, grad_attn, valid, inv_scale):
    scores = (
        jnp.einsum("qgc,kgc->gqk", queries, keys_blk, preferred_element_type=jnp.float32)
        * inv_scale
    )
    exp_terms = jnp.where(valid[None], jnp.exp(scores), 0.0)
    probs = exp_terms / jnp.sum(exp_terms, axis=-1, keepdims=True)
    probs_low = probs.astype(jnp.bfloat16)
    attended = jnp.einsum(
        "gqk,kgc->qgc", probs_low, values_blk, preferred_element_type=jnp.float32
    ).astype(jnp.bfloat16)
    delta = jnp.sum(grad_attn.astype(jnp.float32) * attended.astype(jnp.float32), axis=-1)
    grad_probs = jnp.einsum(
        "qgc,kgc->gqk", grad_attn, values_blk, preferred_element_type=jnp.float32
    )
    grad_scores = (probs * (grad_probs - jnp.transpose(delta)[:, :, None]) * inv_scale).astype(
        jnp.bfloat16
    )
    grad_query = jnp.einsum(
        "gqk,kgc->gcq", grad_scores, keys_blk, preferred_element_type=jnp.float32
    )
    grad_key = jnp.einsum("gqk,qgc->gck", grad_scores, queries, preferred_element_type=jnp.float32)
    grad_value = jnp.einsum(
        "gqk,qgc->gck", probs_low, grad_attn, preferred_element_type=jnp.float32
    )
    return (attended, grad_query, grad_key, grad_value)


def shards(patches, weights, cotangent, loss_mask):
    rows = patches.shape[1]
    width = patches.shape[2]
    inner = weights.shape[2]
    span = (WIN + rows - 2) // rows
    block_rows = min(512, rows)
    key_len = block_rows + span * rows
    group = HEADS
    group_cols = group * HSIZE
    inv_scale = 1.0 / math.sqrt(HSIZE)
    local_in = patches[0].astype(jnp.float32)
    inv_rms = lax.rsqrt(jnp.mean(local_in * local_in, axis=-1) + 1e-06)
    normed_full = local_in * inv_rms[:, None]
    normed = normed_full.astype(jnp.bfloat16)
    projected = jnp.einsum(
        "rd,dwh->wrh", normed, weights, preferred_element_type=jnp.float32
    ).astype(jnp.bfloat16)
    queries = projected[0]
    key_vals = projected[1:3]
    arrived = {offset: shifted(key_vals, "tm", offset) for offset in range(1, span + 1)}
    earlier = [arrived[offset] for offset in range(span, 0, -1)]
    extended = jnp.concatenate(earlier + [key_vals], axis=1)
    local_count = jnp.sum(loss_mask.astype(jnp.int32))
    tokens_all = rows * lax.axis_size("tm") * lax.axis_size("night")
    local_cot = cotangent[0]
    grad_out = jnp.where(loss_mask[0][:, None] > 0, local_cot, jnp.zeros_like(local_cot))
    grad_attn = jnp.einsum(
        "rd,dwh->wrh", grad_out, weights, preferred_element_type=jnp.float32
    )[3].astype(jnp.bfloat16)
    base = lax.axis_index("tm") * rows
    query_idx = jnp.arange(block_rows, dtype=jnp.int32)[:, None]
    key_idx = jnp.arange(key_len, dtype=jnp.int32)[None, :]
    offsets = query_idx - key_idx + span * rows
    band = (offsets >= 0) & (offsets < WIN)
    valid = band & (key_idx >= span * rows - base)
    attended, grad_query, grad_key, grad_value = band_block(
        queries.reshape(rows, HEADS, HSIZE),
        extended[0].reshape(key_len, HEADS, HSIZE),
        extended[1].reshape(key_len, HEADS, HSIZE),
        grad_attn.reshape(rows, HEADS, HSIZE),
        valid,
        inv_scale,
    )
    attended_all = attended.reshape(rows, inner)
    grad_q = grad_query.astype(jnp.bfloat16)
    query_part = jnp.einsum(
        "rd,gcr->dgc", normed, grad_q, preferred_element_type=jnp.float32
    ).reshape(width, inner)
    out_part = jnp.einsum("rd,rh->dh", grad_out, attended_all, preferred_element_type=jnp.float32)
    early_terms = jnp.stack([query_part, out_part], axis=1)
    blocks = lax.axis_size("tm") * lax.axis_size("night")
    block_rows_out = width // blocks
    bits = rows.bit_length()
    if width % blocks == 0 and block_rows_out % 8 == 0 and blocks <= 256 and bits <= inner:
        digits = (local_count // (2 ** jnp.arange(bits, dtype=jnp.int32))) % 2
        count_rows = jnp.zeros((blocks, 8) + early_terms.shape[1:], jnp.float32)
        count_rows = count_rows.at[:, 0, 0, :bits].set(digits.astype(jnp.float32))
        payload = jnp.concatenate(
            [early_terms.reshape((blocks, block_rows_out) + early_terms.shape[1:]), count_rows],
            axis=1,
        ).reshape((-1,) + early_terms.shape[1:])
        early, _ = scatter_rows(
            payload, None, ("tm", "night"), "tm", jnp.bfloat16, tail_first=True, balance=False
        )
        digit_sums = early[block_rows_out, 0, :bits].astype(jnp.int32)
        count = jnp.sum(digit_sums * (2 ** jnp.arange(bits, dtype=jnp.int32)))
        early = early[:block_rows_out]
    else:
        early, count = scatter_rows(
            early_terms, local_count, ("tm", "night"), "tm", jnp.bfloat16, tail_first=True
        )
    owned = jnp.stack([grad_key[..., span * rows :], grad_value[..., span * rows :]])
    for offset in range(1, span + 1):
        lower = (span - offset) * rows
        piece = jnp.stack(
            [grad_key[..., lower : lower + rows], grad_value[..., lower : lower + rows]]
        )
        owned = owned + shifted(piece.astype(jnp.bfloat16), "tm", -offset).astype(jnp.float32)
    grad_kv = owned.astype(jnp.bfloat16)
    grad_proj = jnp.concatenate([grad_q[None], grad_kv, jnp.zeros_like(grad_q)[None]], axis=0)
    grad_rows = grad_proj.transpose(0, 3, 1, 2).reshape(grad_proj.shape[0], rows, inner)
    grad_normed = jnp.einsum(
        "wrh,dwh->rd", grad_rows, weights, preferred_element_type=jnp.float32
    )
    along = jnp.sum(grad_normed * normed_full, axis=-1) / width
    centred_grad = grad_normed - normed_full * along[:, None]
    key_value_part = jnp.einsum(
        "rd,wgcr->dwgc", normed, grad_proj[1:3], preferred_element_type=jnp.float32
    ).reshape(width, 2, inner)
    late, _ = scatter_rows(key_value_part, None, ("tm", "night"), "tm", jnp.bfloat16)
    summed = jnp.concatenate([early[:, :1], late, early[:, 1:]], axis=1)
    total_count = count.astype(jnp.float32)
    loss_scale = jnp.float32(tokens_all) / total_count
    grad_input = (loss_scale * inv_rms[:, None] * centred_grad).astype(jnp.bfloat16)
    grad_weights = summed * (jnp.sqrt(jnp.float32(tokens_all)) / total_count)
    return (grad_input[None], grad_weights)


def solution(mesh):
    return jax.shard_map(
        shards,
        mesh=mesh,
        in_specs=(P("night", "tm", None), P(), P("night", "tm", None), P("night", "tm")),
        out_specs=(P("night", "tm", None), P(("tm", "night"), None, None)),
        check_vma=False,
    )
```

```python
import math

import jax
import jax.numpy as jnp
from jax import lax
from jax.sharding import PartitionSpec as P

HEADS = 8
HSIZE = 64
WIN = 1024


def shifted(value, axis, by):
    peers = lax.axis_size(axis)
    pairs = [(i, i + by) for i in range(peers) if 0 <= i + by < peers]
    return lax.ppermute(value, axis, pairs)


def is_power_of_two(n):
    return n > 0 and n & (n - 1) == 0


def halve(value, dim, axis, flip, send_type):
    peers = lax.axis_size(axis)
    bit = (lax.axis_index(axis) // flip) % 2
    keep = lax.dynamic_index_in_dim(value, bit, dim, keepdims=False)
    send = lax.dynamic_index_in_dim(value, 1 - bit, dim, keepdims=False)
    pairs = [(i, i ^ flip) for i in range(peers)]
    return keep + lax.ppermute(send.astype(send_type), axis, pairs).astype(keep.dtype)


def swap_add(value, anchor, axis, flip):
    value, anchor = lax.optimization_barrier((value, anchor))
    peers = lax.axis_size(axis)
    pairs = [(i, i ^ flip) for i in range(peers)]
    return value + lax.ppermute(value, axis, pairs), anchor


def scatter_rows(value, tally, axes, first_axis, wire_type, tail_first=False, balance=True):
    sizes = [lax.axis_size(axis) for axis in axes]
    rows = value.shape[0]
    groups = math.prod(sizes)
    if not all(is_power_of_two(n) for n in sizes) or rows % groups:
        return (
            lax.psum_scatter(value, axes, scatter_dimension=0, tiled=True),
            None if tally is None else lax.psum(tally, axes),
        )
    stages = [
        (axis, 1 << (n.bit_length() - 2 - i))
        for axis, n in zip(axes, sizes)
        for i in range(n.bit_length() - 1)
    ]
    if not stages:
        return value, tally
    rest = value.shape[1:]
    value = value.reshape((2,) * len(stages) + (rows // groups,) + rest)
    names = list(stages)

    def step(part, part_names, stage, send_type):
        dim = part_names.index(stage)
        return halve(part, dim, *stage, send_type), part_names[:dim] + part_names[dim + 1 :]

    first = (first_axis, 1) if (first_axis, 1) in stages else stages[-1]
    def count_along(tally, anchor, stage):
        if tally is None:
            return tally, anchor
        return swap_add(tally, anchor, *stage)

    def run_tail(value, names, tally):
        for stage in tail:
            value, names = step(value, names, stage, wire_type)
            tally, value = count_along(tally, value, stage)
        return value, names, tally

    value, names = step(value, names, first, wire_type)
    tally, value = count_along(tally, value, first)
    middle = [s for s in stages if s[0] == first[0] and s != first]
    tail = [s for s in stages if s[0] != first[0]][::-1]
    if tail_first:
        value, names, tally = run_tail(value, names, tally)
    if balance and len(middle) > 1 and rest[-1] % 2 == 0:
        axis = -2 if len(rest) > 1 and rest[-2] % 2 == 0 else -1
        cut = rest[axis] // 2
        left, right = jnp.split(value, [cut], axis=axis)
        left_names, right_names = list(names), list(names)
        for a, b in zip(middle, middle[::-1]):
            left, left_names = step(left, left_names, a, wire_type)
            tally, left = count_along(tally, left, a)
            right, right_names = step(right, right_names, b, wire_type)
        value = jnp.concatenate([left, right], axis=axis)
        names = left_names
    else:
        for stage in middle:
            value, names = step(value, names, stage, wire_type)
            tally, value = count_along(tally, value, stage)
    if not tail_first:
        value, names, tally = run_tail(value, names, tally)
    return value, tally


def band_block(queries, keys_blk, values_blk, grad_attn, valid, inv_scale):
    scores = (
        jnp.einsum("qgc,kgc->gqk", queries, keys_blk, preferred_element_type=jnp.float32)
        * inv_scale
    )
    exp_terms = jnp.exp(scores) * valid[None]
    probs = exp_terms / jnp.sum(exp_terms, axis=-1, keepdims=True)
    probs_low = probs.astype(jnp.bfloat16)
    attended = jnp.einsum(
        "gqk,kgc->qgc", probs_low, values_blk, preferred_element_type=jnp.float32
    ).astype(jnp.bfloat16)
    delta = jnp.sum(grad_attn.astype(jnp.float32) * attended.astype(jnp.float32), axis=-1)
    grad_probs = jnp.einsum(
        "qgc,kgc->gqk", grad_attn, values_blk, preferred_element_type=jnp.float32
    )
    grad_scores = (probs * (grad_probs - jnp.transpose(delta)[:, :, None]) * inv_scale).astype(
        jnp.bfloat16
    )
    grad_query = jnp.einsum(
        "gqk,kgc->gcq", grad_scores, keys_blk, preferred_element_type=jnp.float32
    )
    grad_key = jnp.einsum("gqk,qgc->gck", grad_scores, queries, preferred_element_type=jnp.float32)
    grad_value = jnp.einsum(
        "gqk,qgc->gck", probs_low, grad_attn, preferred_element_type=jnp.float32
    )
    return (attended, grad_query, grad_key, grad_value)


def shards(patches, weights, cotangent, loss_mask):
    rows = patches.shape[1]
    width = patches.shape[2]
    inner = weights.shape[2]
    span = (WIN + rows - 2) // rows
    block_rows = min(512, rows)
    key_len = block_rows + span * rows
    group = HEADS
    group_cols = group * HSIZE
    inv_scale = 1.0 / math.sqrt(HSIZE)
    local_in = patches[0].astype(jnp.float32)
    inv_rms = lax.rsqrt(jnp.mean(local_in * local_in, axis=-1) + 1e-06)
    normed_full = local_in * inv_rms[:, None]
    normed = normed_full.astype(jnp.bfloat16)
    projected = jnp.einsum(
        "rd,dwh->wrh", normed, weights, preferred_element_type=jnp.float32
    ).astype(jnp.bfloat16)
    queries = projected[0]
    key_vals = projected[1:3]
    arrived = {offset: shifted(key_vals, "tm", offset) for offset in range(1, span + 1)}
    earlier = [arrived[offset] for offset in range(span, 0, -1)]
    extended = jnp.concatenate(earlier + [key_vals], axis=1)
    local_count = jnp.sum(loss_mask.astype(jnp.int32))
    tokens_all = rows * lax.axis_size("tm") * lax.axis_size("night")
    local_cot = cotangent[0]
    grad_out = jnp.where(loss_mask[0][:, None] > 0, local_cot, jnp.zeros_like(local_cot))
    grad_attn = jnp.einsum(
        "rd,dwh->wrh", grad_out, weights, preferred_element_type=jnp.float32
    )[3].astype(jnp.bfloat16)
    base = lax.axis_index("tm") * rows
    query_idx = jnp.arange(block_rows, dtype=jnp.int32)[:, None]
    key_idx = jnp.arange(key_len, dtype=jnp.int32)[None, :]
    offsets = query_idx - key_idx + span * rows
    band = (offsets >= 0) & (offsets < WIN)
    valid = (band & (key_idx >= span * rows - base)).astype(jnp.float32)
    attended, grad_query, grad_key, grad_value = band_block(
        queries.reshape(rows, HEADS, HSIZE),
        extended[0].reshape(key_len, HEADS, HSIZE),
        extended[1].reshape(key_len, HEADS, HSIZE),
        grad_attn.reshape(rows, HEADS, HSIZE),
        valid,
        inv_scale,
    )
    attended_all = attended.reshape(rows, inner)
    grad_q = grad_query.astype(jnp.bfloat16)
    query_part = jnp.einsum(
        "rd,gcr->dgc", normed, grad_q, preferred_element_type=jnp.float32
    ).reshape(width, inner)
    out_part = jnp.einsum("rd,rh->dh", grad_out, attended_all, preferred_element_type=jnp.float32)
    early_terms = jnp.stack([query_part, out_part], axis=1)
    blocks = lax.axis_size("tm") * lax.axis_size("night")
    block_rows_out = width // blocks
    bits = rows.bit_length()
    if width % blocks == 0 and block_rows_out % 8 == 0 and blocks <= 256 and bits <= inner:
        digits = (local_count // (2 ** jnp.arange(bits, dtype=jnp.int32))) % 2
        count_rows = jnp.zeros((blocks, 8) + early_terms.shape[1:], jnp.float32)
        count_rows = count_rows.at[:, 0, 0, :bits].set(digits.astype(jnp.float32))
        payload = jnp.concatenate(
            [early_terms.reshape((blocks, block_rows_out) + early_terms.shape[1:]), count_rows],
            axis=1,
        ).reshape((-1,) + early_terms.shape[1:])
        early, _ = scatter_rows(
            payload, None, ("tm", "night"), "tm", jnp.bfloat16, tail_first=True, balance=False
        )
        digit_sums = early[block_rows_out, 0, :bits].astype(jnp.int32)
        count = jnp.sum(digit_sums * (2 ** jnp.arange(bits, dtype=jnp.int32)))
        early = early[:block_rows_out]
    else:
        early, count = scatter_rows(
            early_terms, local_count, ("tm", "night"), "tm", jnp.bfloat16, tail_first=True
        )
    owned = jnp.stack([grad_key[..., span * rows :], grad_value[..., span * rows :]])
    for offset in range(1, span + 1):
        lower = (span - offset) * rows
        piece = jnp.stack(
            [grad_key[..., lower : lower + rows], grad_value[..., lower : lower + rows]]
        )
        owned = owned + shifted(piece.astype(jnp.bfloat16), "tm", -offset).astype(jnp.float32)
    grad_kv = owned.astype(jnp.bfloat16)
    grad_proj = jnp.concatenate([grad_q[None], grad_kv, jnp.zeros_like(grad_q)[None]], axis=0)
    grad_rows = grad_proj.transpose(0, 3, 1, 2).reshape(grad_proj.shape[0], rows, inner)
    grad_normed = jnp.einsum(
        "wrh,dwh->rd", grad_rows, weights, preferred_element_type=jnp.float32
    )
    along = jnp.sum(grad_normed * normed_full, axis=-1) / width
    centred_grad = grad_normed - normed_full * along[:, None]
    key_value_part = jnp.einsum(
        "rd,wgcr->dwgc", normed, grad_proj[1:3], preferred_element_type=jnp.float32
    ).reshape(width, 2, inner)
    late, _ = scatter_rows(key_value_part, None, ("tm", "night"), "tm", jnp.bfloat16)
    summed = jnp.concatenate([early[:, :1], late, early[:, 1:]], axis=1)
    total_count = count.astype(jnp.float32)
    loss_scale = jnp.float32(tokens_all) / total_count
    grad_input = (loss_scale * inv_rms[:, None] * centred_grad).astype(jnp.bfloat16)
    grad_weights = summed * (jnp.sqrt(jnp.float32(tokens_all)) / total_count)
    return (grad_input[None], grad_weights)


def solution(mesh):
    return jax.shard_map(
        shards,
        mesh=mesh,
        in_specs=(P("night", "tm", None), P(), P("night", "tm", None), P("night", "tm")),
        out_specs=(P("night", "tm", None), P(("tm", "night"), None, None)),
        check_vma=False,
    )
```
